32 devices in a mesh: groups: 2 (over y), seq: 4 (over z), head: 2 (over x), sub: 2 (over core).
Axes of the slice: x: 2, y: 2, z: 4, core: 2. Of those that a mesh axis runs over, the one named last changes fastest.
Arguments:
- queries: bfloat16 [64, 1024, 128], P(('head', 'sub'), ('groups', 'seq')), parts along dimension 1, may hold values from -6 to 6
- keys_values: bfloat16 [8, 1024, 256], P(('head', 'sub'), ('groups', 'seq')), parts along dimension 1, may hold values from -6 to 6
- student_x: bfloat16 [64, 1024, 128], P(('head', 'sub'), ('groups', 'seq')), parts along dimension 1, may hold values from -32 to 32
- state_maps: bfloat16 [8, 1024, 128], P(('head', 'sub'), ('groups', 'seq')), parts along dimension 1, may hold values from -0.75 to 0.75
- decay_logit: float32 [64, 1024], P(('head', 'sub'), ('groups', 'seq')), parts along dimension 1, may hold values from 0 to 16
- skip_gain: float32 [64], P(('head', 'sub')), may hold values from 0.5 to 2
- init_state: float32 [128, 64, 128], P(('groups', 'head', 'sub')), parts along dimension 0, may hold values from -6 to 6
Outputs:
- grad_x: bfloat16 [64, 1024, 128], P(('head', 'sub'), ('groups', 'seq')), parts along dimension 1
- grad_maps: bfloat16 [8, 1024, 128], P(('head', 'sub'), ('groups', 'seq')), parts along dimension 1
- grad_log_decay: float32 [64, 1024], P(('head', 'sub'), ('groups', 'seq')), parts along dimension 1
The draws below stay inside these ranges and needn't reach their ends.
There are 2 independent parts, one for each index of `groups`. The reference program is written for one: setup_inputs(seed, part) draws one part's arguments, and reference() takes and returns one part's arrays. A program takes and returns all parts, laid end to end along the dimension named above; an argument that names none is the same for every part. Nothing has to cross between parts.
All inputs are finite; a program needn't handle non-finite values.
Results may differ from the reference program's by a relative error of at most 0.013.
Values may be sent and summed in bfloat16 or wider, within the bound.
No kernel may reach another device: no remote copies, remote signals or barrier semaphores. Data moves between devices by JAX's collectives and lax.ppermute only.
A program may use at most 64 MiB of HBM per device.

```python
import math
import jax
import jax.numpy as jnp
from jax import lax

HEAD_COUNT = 64
KV_HEADS = 8
HEAD_DIM = 128
STATE = 64
TOK_DEV = 128
PER_GROUP = 8
SPAN_TOKENS = 512


def draw_queries(key, part):
    values = jnp.clip(jax.random.normal(jax.random.fold_in(key, 11), (HEAD_COUNT, SPAN_TOKENS, HEAD_DIM), jnp.float32), -6.0, 6.0)
    return values.astype(jnp.bfloat16)


def draw_keys_values(key, part):
    values = jnp.clip(jax.random.normal(jax.random.fold_in(key, 13), (KV_HEADS, SPAN_TOKENS, 2 * HEAD_DIM), jnp.float32), -6.0, 6.0)
    return values.astype(jnp.bfloat16)


def draw_student_x(key, part):
    divided_keys = jax.random.split(key, 3)
    row_scale = jnp.exp(jax.random.uniform(divided_keys[1], (HEAD_COUNT, SPAN_TOKENS, 1), jnp.float32, math.log(0.5), math.log(2.0)))
    column_scale = jnp.exp(jax.random.uniform(divided_keys[0], (HEAD_COUNT, 1, HEAD_DIM), jnp.float32, math.log(0.4), math.log(4.0)))
    noise = jnp.clip(jax.random.normal(divided_keys[2], (HEAD_COUNT, SPAN_TOKENS, HEAD_DIM), jnp.float32), -4.0, 4.0)
    return (noise * column_scale * row_scale).astype(jnp.bfloat16)


def draw_decay_logit(key, part):
    divided_keys = jax.random.split(key, 7)
    ordering = jax.random.permutation(divided_keys[0], HEAD_COUNT)
    quick = ordering < HEAD_COUNT // 2
    quick_rate = jnp.exp(jax.random.uniform(divided_keys[1], (HEAD_COUNT,), jnp.float32, math.log(1.0 / 64.0), math.log(1.0 / 8.0)))
    steady_rate = jnp.exp(jax.random.uniform(divided_keys[2], (HEAD_COUNT,), jnp.float32, math.log(0.03 / SPAN_TOKENS), math.log(0.5 / SPAN_TOKENS)))
    level = -jnp.log(jnp.where(quick, quick_rate, steady_rate))[:, None]
    rough = jax.random.uniform(divided_keys[3], (HEAD_COUNT, SPAN_TOKENS), jnp.float32, -0.7, 0.7)
    block_offsets = jax.random.uniform(divided_keys[4], (HEAD_COUNT, SPAN_TOKENS // TOK_DEV), jnp.float32, -0.7, 0.7)
    score_logits = level + rough + jnp.repeat(block_offsets, TOK_DEV, axis=1)
    spike_events = jax.random.randint(divided_keys[5], (3,), 0, SPAN_TOKENS)
    row_numbers = jnp.arange(SPAN_TOKENS)
    is_spike_event = jnp.any(row_numbers[None, :] == spike_events[:, None], axis=0)
    spike_value_rows = jax.random.uniform(divided_keys[6], (HEAD_COUNT, SPAN_TOKENS), jnp.float32, 0.0, 1.4)
    return jnp.where(is_spike_event[None, :], spike_value_rows, score_logits)


def block_scale(own_key, extent, cuts, smallest, largest):
    def one(dim, shards_of):
        heights = jax.random.uniform(jax.random.fold_in(jax.random.fold_in(own_key, 6), dim), (shards_of,), jnp.float32, smallest / len(cuts), largest / len(cuts))
        return jnp.repeat(jnp.exp(heights), extent[dim] // shards_of).reshape((-1,) + (1,) * (len(extent) - dim - 1))

    level = one(*cuts[0])
    for cut in cuts[1:]:
        level = level * one(*cut)
    return level


def normal_values(own_key, extent, scale, reach, shards=(), kind=jnp.bfloat16):
    level = block_scale(own_key, extent, shards, -0.22, 0.18) if shards else 1.0
    entries = jax.random.normal(own_key, extent, jnp.float32) * scale * level
    return jnp.minimum(jnp.maximum(entries, -reach), reach).astype(kind)


def setup_inputs(seed: int = 0, part: int = 0) -> dict:
    key_list = jax.random.split(jax.random.key(seed), 8)
    part_keys = jax.random.split(jax.random.fold_in(key_list[7], part), 8)
    return {
        "queries": draw_queries(jax.random.fold_in(jax.random.fold_in(key_list[7], part), 71), part),
        "keys_values": draw_keys_values(jax.random.fold_in(jax.random.fold_in(key_list[7], part), 71), part),
        "student_x": draw_student_x(jax.random.fold_in(jax.random.fold_in(key_list[7], part), 71), part),
        "state_maps": normal_values(part_keys[3], (KV_HEADS, SPAN_TOKENS, 2 * STATE), 0.125, 0.75, ((0, 4), (1, 4))),
        "decay_logit": draw_decay_logit(jax.random.fold_in(jax.random.fold_in(key_list[7], part), 71), part),
        "skip_gain": jnp.clip(0.5 + 1.5 * jax.random.uniform(key_list[5], (HEAD_COUNT,), jnp.float32) ** block_scale(key_list[5], (HEAD_COUNT,), ((0, 4),), -0.2, 0.2), 0.5, 2.0),
        "init_state": normal_values(part_keys[6], (HEAD_COUNT, STATE, HEAD_DIM), 1.0, 6.0, ((0, 4),), jnp.float32),
    }


epsilon = 1e-05
highest = lax.Precision.HIGHEST

def reference(queries, keys_values, student_x, state_maps, decay_logit, skip_gain, init_state):
    positions = jnp.arange(SPAN_TOKENS)
    causal = positions[:, None] >= positions[None, :]

    def teacher_one(number):
        paired = keys_values[number // PER_GROUP]
        scores = jnp.dot(queries[number], paired[:, :HEAD_DIM].T, preferred_element_type=jnp.float32) * HEAD_DIM ** (-0.5)
        scores = jnp.where(causal, scores, -jnp.inf)
        highest_score = lax.optimization_barrier(jnp.max(scores, axis=1, keepdims=True))
        exponentials = jnp.exp(scores - highest_score)
        row_sums = lax.optimization_barrier(jnp.sum(exponentials, axis=1, keepdims=True))
        mixed = jnp.dot(exponentials.astype(jnp.bfloat16), paired[:, HEAD_DIM:], preferred_element_type=jnp.float32) / row_sums
        return mixed.astype(jnp.bfloat16)
    teacher = lax.map(teacher_one, jnp.arange(HEAD_COUNT))
    log_decay = jax.nn.log_sigmoid(decay_logit)

    def student_one(number):
        maps_head = state_maps[number // PER_GROUP].astype(jnp.float32)
        x_head = student_x[number].astype(jnp.float32)
        teacher_head = teacher[number].astype(jnp.float32)
        target = teacher_head * lax.rsqrt(lax.optimization_barrier(jnp.mean(teacher_head * teacher_head, axis=1, keepdims=True)) + epsilon)
        skip_head = skip_gain[number]
        start_state = init_state[number]

        def loss_of(x_in, in_map, out_map, log_head):
            cumulative = jnp.cumsum(log_head)
            gaps = cumulative[:, None] - cumulative[None, :]
            decayed = jnp.where(causal, jnp.exp(jnp.where(causal, gaps, 0.0)), 0.0)
            intersection = jnp.dot(out_map, in_map.T, precision=highest)
            state_out = jnp.dot(intersection * decayed, x_in, precision=highest)
            state_out = state_out + jnp.exp(cumulative)[:, None] * jnp.dot(out_map, start_state, precision=highest)
            outputs = state_out + skip_head * x_in
            normed = outputs * lax.rsqrt(lax.optimization_barrier(jnp.mean(outputs * outputs, axis=1, keepdims=True)) + epsilon)
            return 0.5 * jnp.sum((normed - target) ** 2)
        return jax.grad(loss_of, argnums=(0, 1, 2, 3))(x_head, maps_head[:, :STATE], maps_head[:, STATE:], log_decay[number])
    grad_x, grad_in, grad_out, grad_log = lax.map(student_one, jnp.arange(HEAD_COUNT))
    grad_maps = jnp.concatenate([grad_in, grad_out], axis=2).reshape(KV_HEADS, PER_GROUP, SPAN_TOKENS, 2 * STATE).sum(axis=1)
    return (grad_x.astype(jnp.bfloat16), grad_maps.astype(jnp.bfloat16), grad_log)
```

```python
import jax
import jax.numpy as jnp
from jax import lax
from jax.sharding import PartitionSpec as P

epsilon = 1e-05
highest = lax.Precision.HIGHEST


def split_three(values):
    top = lax.reduce_precision(values, exponent_bits=8, mantissa_bits=7)
    rest = values - top
    middle = lax.reduce_precision(rest, exponent_bits=8, mantissa_bits=7)
    low = rest - middle
    return jnp.stack([top, middle, low]).astype(jnp.bfloat16)


def join_three(parts):
    wide = parts.astype(jnp.float32)
    return wide[..., 0, :] + wide[..., 1, :] + wide[..., 2, :]


def pack(big, small):
    flat = big.astype(jnp.bfloat16).reshape(-1)
    extra = split_three(small).reshape(-1)
    pad = (-extra.shape[0]) % 128
    return jnp.concatenate([flat, extra, jnp.zeros((pad,), jnp.bfloat16)])


def unpack(gathered, big_shape, small_count):
    seq_count = gathered.shape[0]
    size = 1
    for d in big_shape:
        size *= d
    big = gathered[:, :size].reshape((seq_count,) + tuple(big_shape))
    small = join_three(gathered[:, size : size + 3 * small_count].reshape(seq_count, 3, small_count))
    return big, small


def teacher_rows(queries, kv_all, seq_rank):
    local_heads, tok_dev, head_width = queries.shape
    seq_count, local_groups = kv_all.shape[0], kv_all.shape[1]
    per_group = local_heads // local_groups
    grouped = queries.reshape(local_groups, per_group, tok_dev, head_width)
    keys = kv_all[..., :head_width]
    values = kv_all[..., head_width:]
    scores = jnp.einsum("gptd,sgkd->gptsk", grouped, keys, preferred_element_type=jnp.float32)
    scores = scores.reshape(local_groups, per_group, tok_dev, seq_count * tok_dev) * head_width ** (-0.5)
    query_pos = seq_rank * tok_dev + jnp.arange(tok_dev)
    key_pos = jnp.arange(seq_count * tok_dev)
    causal = query_pos[:, None] >= key_pos[None, :]
    scores = jnp.where(causal, scores, -jnp.inf)
    highest_score = jnp.max(scores, axis=3, keepdims=True)
    exponentials = jnp.exp(scores - highest_score)
    row_sums = jnp.sum(exponentials, axis=3, keepdims=True)
    probabilities = exponentials.astype(jnp.bfloat16).reshape(
        local_groups, per_group, tok_dev, seq_count, tok_dev
    )
    mixed = jnp.einsum("gptsk,sgkd->gptd", probabilities, values, preferred_element_type=jnp.float32)
    mixed = mixed / row_sums
    return mixed.astype(jnp.bfloat16).reshape(local_heads, tok_dev, head_width)


def body(queries, keys_values, student_x, state_maps, decay_logit, skip_gain, init_state):
    local_heads, tok_dev, head_width = student_x.shape
    local_groups = state_maps.shape[0]
    per_group = local_heads // local_groups
    state_size = state_maps.shape[2] // 2
    seq_count = lax.axis_size("seq")
    seq_rank = lax.axis_index("seq")

    kv_all = lax.all_gather(keys_values.reshape(-1), "seq", axis=0).reshape(
        (seq_count,) + keys_values.shape
    )

    log_decay = jax.nn.log_sigmoid(decay_logit)
    cumulative = jnp.cumsum(log_decay, axis=1)
    totals = cumulative[:, -1]
    to_end = jnp.exp(totals[:, None] - cumulative)
    from_start = jnp.exp(cumulative)
    in_maps = state_maps[:, :, :state_size]
    out_maps = state_maps[:, :, state_size:]
    inputs_wide = student_x.astype(jnp.float32)
    in_heads = jnp.repeat(in_maps.astype(jnp.float32), per_group, axis=0)
    out_heads = jnp.repeat(out_maps.astype(jnp.float32), per_group, axis=0)
    weighted_in = in_heads * to_end[..., None]
    end_state = jnp.einsum("hsn,hsp->hnp", weighted_in, inputs_wide, precision=highest)

    state_all = lax.all_gather(pack(end_state, totals), "seq", axis=0)
    ends_all, totals_all = unpack(state_all, end_state.shape, local_heads)

    chunk_ids = jnp.arange(seq_count)
    inclusive = jnp.cumsum(totals_all, axis=0)
    exclusive = inclusive - totals_all
    before_me = exclusive[seq_rank]
    through_me = inclusive[seq_rank]
    earlier = (chunk_ids < seq_rank)[:, None]
    forward_weights = jnp.where(earlier, jnp.exp(jnp.where(earlier, before_me[None] - inclusive, 0.0)), 0.0)
    prefix_state = jnp.sum(forward_weights[:, :, None, None] * ends_all.astype(jnp.float32), axis=0)
    entering = prefix_state + jnp.exp(before_me)[:, None, None] * init_state

    intersection = jnp.einsum("gtn,gsn->gts", out_maps, in_maps, preferred_element_type=jnp.float32)
    order_ids = jnp.arange(tok_dev)
    causal = (order_ids[:, None] >= order_ids[None, :])[None]
    gaps = cumulative[:, :, None] - cumulative[:, None, :]
    decayed = jnp.where(causal, jnp.exp(jnp.where(causal, gaps, 0.0)), 0.0)
    mixing = (
        decayed.reshape(local_groups, per_group, tok_dev, tok_dev) * intersection[:, None]
    ).reshape(local_heads, tok_dev, tok_dev)
    local_out = jnp.einsum("hts,hsp->htp", mixing, inputs_wide, precision=highest)

    teacher = teacher_rows(queries, kv_all, seq_rank)
    teacher_wide = teacher.astype(jnp.float32)
    target = teacher_wide * lax.rsqrt(
        jnp.mean(teacher_wide * teacher_wide, axis=2, keepdims=True) + epsilon
    )

    state_out = local_out + from_start[..., None] * jnp.einsum(
        "htn,hnp->htp", out_heads, entering, precision=highest
    )
    outputs = state_out + skip_gain[:, None, None] * inputs_wide
    inverse = lax.rsqrt(jnp.mean(outputs * outputs, axis=2, keepdims=True) + epsilon)
    normed = outputs * inverse
    residual = normed - target
    grad_out = (residual - normed * jnp.mean(residual * normed, axis=2, keepdims=True)) * inverse
    local_dx = jnp.einsum("hts,htp->hsp", mixing, grad_out, precision=highest)
    cross = jnp.einsum("htp,hsp->hts", grad_out, inputs_wide, precision=highest)
    paired = decayed * cross
    local_din = jnp.einsum("hts,htn->hsn", paired, out_heads, precision=highest)
    grad_output_maps = jnp.einsum("hts,hsn->htn", paired, in_heads, precision=highest)
    grad_output_maps = grad_output_maps + from_start[..., None] * jnp.einsum(
        "hnp,htp->htn", entering, grad_out, precision=highest
    )
    forward_term = jnp.sum(grad_out * state_out, axis=2)
    flow = jnp.einsum(
        "htn,htp->hnp", out_heads * from_start[..., None], grad_out, precision=highest
    )
    closing = jnp.sum(forward_term - jnp.sum(inputs_wide * local_dx, axis=2), axis=1)

    flow_all_packed = lax.all_gather(pack(flow, closing), "seq", axis=0)
    flows_all, closing_all = unpack(flow_all_packed, flow.shape, local_heads)

    later = (chunk_ids > seq_rank)[:, None]
    back_weights = jnp.where(later, jnp.exp(jnp.where(later, exclusive - through_me[None], 0.0)), 0.0)
    incoming = jnp.sum(back_weights[:, :, None, None] * flows_all.astype(jnp.float32), axis=0)
    pair_dots = jnp.einsum("jhnp,ihnp->jih", ends_all, flows_all, preferred_element_type=jnp.float32)
    after_pair = chunk_ids[None, :] > chunk_ids[:, None]
    pair_gap = exclusive[None, :, :] - inclusive[:, None, :]
    pair_weights = jnp.where(
        after_pair[:, :, None], jnp.exp(jnp.where(after_pair[:, :, None], pair_gap, 0.0)), 0.0
    )
    through_later = jnp.sum(pair_weights * pair_dots, axis=1)
    later_sum = jnp.sum(jnp.where(later, closing_all - through_later, 0.0), axis=0)

    state_dx = local_dx + jnp.einsum("hsn,hnp->hsp", weighted_in, incoming, precision=highest)
    terms = forward_term - jnp.sum(inputs_wide * state_dx, axis=2)
    grad_log_decay = later_sum[:, None] + lax.cumsum(terms, axis=1, reverse=True)
    grad_input_maps = (
        local_din
        + jnp.einsum("hnp,hsp->hsn", incoming, inputs_wide, precision=highest) * to_end[..., None]
    )
    grad_maps = jnp.concatenate([grad_input_maps, grad_output_maps], axis=2)
    grad_maps = grad_maps.reshape(local_groups, per_group, tok_dev, 2 * state_size).sum(axis=1)
    grad_x = state_dx + skip_gain[:, None, None] * grad_out
    return (grad_x.astype(jnp.bfloat16), grad_maps.astype(jnp.bfloat16), grad_log_decay)


def solution(mesh):
    in_specs = (
        P(("head", "sub"), ("groups", "seq"), None),
        P(("head", "sub"), ("groups", "seq"), None),
        P(("head", "sub"), ("groups", "seq"), None),
        P(("head", "sub"), ("groups", "seq"), None),
        P(("head", "sub"), ("groups", "seq")),
        P(("head", "sub")),
        P(("groups", "head", "sub"), None, None),
    )
    out_specs = (
        P(("head", "sub"), ("groups", "seq"), None),
        P(("head", "sub"), ("groups", "seq"), None),
        P(("head", "sub"), ("groups", "seq")),
    )
    return jax.shard_map(body, mesh=mesh, in_specs=in_specs, out_specs=out_specs, check_vma=False)
```

```python
import numpy as np
import jax
import jax.numpy as jnp
from jax import lax
from jax.sharding import PartitionSpec as P

epsilon = 1e-05
highest = lax.Precision.HIGHEST


def split_three(values):
    top = lax.reduce_precision(values, exponent_bits=8, mantissa_bits=7)
    rest = values - top
    middle = lax.reduce_precision(rest, exponent_bits=8, mantissa_bits=7)
    low = rest - middle
    return jnp.stack([top, middle, low]).astype(jnp.bfloat16)


def join_three(parts):
    wide = parts.astype(jnp.float32)
    return wide[..., 0, :] + wide[..., 1, :] + wide[..., 2, :]


def pack_rows(big, smalls):
    rows = big.astype(jnp.bfloat16).reshape(-1, 128)
    vector = jnp.concatenate([v.reshape(-1) for v in smalls])
    padded = -(-vector.shape[0] // 128) * 128
    vector = jnp.pad(vector, (0, padded - vector.shape[0]))
    extra = split_three(vector).reshape(3 * padded // 128, 128)
    extra = jnp.pad(extra, ((0, (-extra.shape[0]) % 16), (0, 0)))
    return jnp.concatenate([rows, extra], axis=0)


def unpack_rows(received, big_shape, small_shapes):
    count = received.shape[0]
    big_rows = 1
    for d in big_shape:
        big_rows *= d
    big_rows //= 128
    big = received[:, :big_rows].reshape((count,) + tuple(big_shape))
    sizes = []
    for shape in small_shapes:
        size = 1
        for d in shape:
            size *= d
        sizes.append(size)
    padded = -(-sum(sizes) // 128) * 128
    extra = received[:, big_rows : big_rows + 3 * padded // 128].reshape(count, 3, padded)
    vector = join_three(extra)
    smalls = []
    offset = 0
    for shape, size in zip(small_shapes, sizes):
        smalls.append(vector[:, offset : offset + size].reshape((count,) + tuple(shape)))
        offset += size
    return big, smalls


def shifted(x, step):
    seq_count = lax.axis_size("seq")
    seq_rank = lax.axis_index("seq")
    if seq_count <= 8:
        moved = []
        for distance in range(1, seq_count):
            if step > 0:
                pairs = [(j, j + distance) for j in range(seq_count - distance)]
            else:
                pairs = [(j + distance, j) for j in range(seq_count - distance)]
            moved.append(lax.ppermute(x, "seq", pairs))
        return jnp.stack(moved)
    gathered = lax.all_gather(x, "seq", axis=0)
    source = seq_rank + step * jnp.arange(1, seq_count)
    valid = (source >= 0) & (source < seq_count)
    picked = jnp.take(gathered, jnp.clip(source, 0, seq_count - 1), axis=0)
    return jnp.where(valid.reshape((-1,) + (1,) * x.ndim), picked, jnp.zeros_like(picked))


def teacher_rows(queries, kv_blocks, seq_rank):
    local_heads, tok_dev, head_width = queries.shape
    block_count, local_groups = kv_blocks.shape[0], kv_blocks.shape[1]
    per_group = local_heads // local_groups
    grouped = queries.reshape(local_groups, per_group, tok_dev, head_width)
    keys = kv_blocks[..., :head_width]
    values = kv_blocks[..., head_width:]
    scores = jnp.einsum("gptd,sgkd->gptsk", grouped, keys, preferred_element_type=jnp.float32)
    scores = scores * head_width ** (-0.5)
    distance = jnp.arange(block_count)[:, None, None]
    rows = jnp.arange(tok_dev)
    within = (rows[:, None] >= rows[None, :])[None]
    allowed = ((distance == 0) & within) | ((distance >= 1) & (distance <= seq_rank))
    allowed = jnp.transpose(allowed, (1, 0, 2))
    scores = jnp.where(allowed, scores, -jnp.inf)
    highest_score = jnp.max(scores, axis=(3, 4), keepdims=True)
    exponentials = jnp.exp(scores - highest_score)
    row_sums = jnp.sum(exponentials, axis=(3, 4))
    probabilities = exponentials.astype(jnp.bfloat16)
    mixed = jnp.einsum("gptsk,sgkd->gptd", probabilities, values, preferred_element_type=jnp.float32)
    mixed = mixed / row_sums[..., None]
    return mixed.astype(jnp.bfloat16).reshape(local_heads, tok_dev, head_width)


def body(queries, keys_values, student_x, state_maps, decay_logit, skip_gain, init_state):
    local_heads, tok_dev, head_width = student_x.shape
    local_groups = state_maps.shape[0]
    per_group = local_heads // local_groups
    state_size = state_maps.shape[2] // 2
    seq_count = lax.axis_size("seq")
    seq_rank = lax.axis_index("seq")
    distances = jnp.arange(1, seq_count)

    kv_earlier = shifted(keys_values, 1)

    log_decay = jax.nn.log_sigmoid(decay_logit)
    cumulative = jnp.cumsum(log_decay, axis=1)
    totals = cumulative[:, -1]
    to_end = jnp.exp(totals[:, None] - cumulative)
    from_start = jnp.exp(cumulative)
    in_maps = state_maps[:, :, :state_size]
    out_maps = state_maps[:, :, state_size:]
    inputs_wide = student_x.astype(jnp.float32)
    in_heads = jnp.repeat(in_maps.astype(jnp.float32), per_group, axis=0)
    out_heads = jnp.repeat(out_maps.astype(jnp.float32), per_group, axis=0)
    weighted_in = in_heads * to_end[..., None]
    end_state = jnp.einsum("hsn,hsp->hnp", weighted_in, inputs_wide, precision=highest)

    state_earlier = shifted(pack_rows(end_state, [totals]), 1)
    ends_earlier, (totals_earlier,) = unpack_rows(state_earlier, end_state.shape, [totals.shape])

    valid_earlier = (distances <= seq_rank)[:, None]
    totals_earlier = jnp.where(valid_earlier, totals_earlier, 0.0)
    gap_earlier = jnp.cumsum(totals_earlier, axis=0) - totals_earlier
    forward_weights = jnp.where(valid_earlier, jnp.exp(gap_earlier), 0.0)
    prefix_state = jnp.sum(forward_weights[:, :, None, None] * ends_earlier.astype(jnp.float32), axis=0)
    entering = prefix_state + jnp.exp(jnp.sum(totals_earlier, axis=0))[:, None, None] * init_state

    intersection = jnp.einsum("gtn,gsn->gts", out_maps, in_maps, preferred_element_type=jnp.float32)
    order_ids = jnp.arange(tok_dev)
    causal = (order_ids[:, None] >= order_ids[None, :])[None]
    gaps = cumulative[:, :, None] - cumulative[:, None, :]
    decayed = jnp.where(causal, jnp.exp(jnp.where(causal, gaps, 0.0)), 0.0)
    mixing = (
        decayed.reshape(local_groups, per_group, tok_dev, tok_dev) * intersection[:, None]
    ).reshape(local_heads, tok_dev, tok_dev)
    local_out = jnp.einsum("hts,hsp->htp", mixing, inputs_wide, precision=highest)

    kv_blocks = jnp.concatenate([keys_values[None], kv_earlier], axis=0)
    teacher = teacher_rows(queries, kv_blocks, seq_rank)
    teacher_wide = teacher.astype(jnp.float32)
    target = teacher_wide * lax.rsqrt(
        jnp.mean(teacher_wide * teacher_wide, axis=2, keepdims=True) + epsilon
    )

    state_out = local_out + from_start[..., None] * jnp.einsum(
        "htn,hnp->htp", out_heads, entering, precision=highest
    )
    outputs = state_out + skip_gain[:, None, None] * inputs_wide
    inverse = lax.rsqrt(jnp.mean(outputs * outputs, axis=2, keepdims=True) + epsilon)
    normed = outputs * inverse
    residual = normed - target
    grad_out = (residual - normed * jnp.mean(residual * normed, axis=2, keepdims=True)) * inverse
    forward_term = jnp.sum(grad_out * state_out, axis=2)
    flow = jnp.einsum(
        "htn,htp->hnp", out_heads * from_start[..., None], grad_out, precision=highest
    )
    local_dx = jnp.einsum("hts,htp->hsp", mixing, grad_out, precision=highest)
    closing = jnp.sum(forward_term - jnp.sum(inputs_wide * local_dx, axis=2), axis=1)
    ends_dot_flow = jnp.sum(ends_earlier.astype(jnp.float32) * flow[None], axis=(2, 3))

    flow_later = shifted(pack_rows(flow, [totals, closing, ends_dot_flow]), -1)

    cross = jnp.einsum("htp,hsp->hts", grad_out, inputs_wide, precision=highest)
    paired = decayed * cross
    local_din = jnp.einsum("hts,htn->hsn", paired, out_heads, precision=highest)
    grad_output_maps = jnp.einsum("hts,hsn->htn", paired, in_heads, precision=highest)
    grad_output_maps = grad_output_maps + from_start[..., None] * jnp.einsum(
        "hnp,htp->htn", entering, grad_out, precision=highest
    )

    flows_later, (totals_later, closing_later, dots_later) = unpack_rows(
        flow_later, flow.shape, [totals.shape, closing.shape, ends_dot_flow.shape]
    )
    valid_later = (seq_rank + distances < seq_count)[:, None]
    totals_later = jnp.where(valid_later, totals_later, 0.0)
    closing_later = jnp.where(valid_later, closing_later, 0.0)
    through_later = jnp.cumsum(totals_later, axis=0)
    gap_later = through_later - totals_later
    back_weights = jnp.where(valid_later, jnp.exp(gap_later), 0.0)
    incoming = jnp.sum(back_weights[:, :, None, None] * flows_later.astype(jnp.float32), axis=0)
    first, second = [], []
    for early in range(1, seq_count):
        for late in range(early + 1, seq_count):
            first.append(early)
            second.append(late)
    if first:
        first = np.array(first)
        second = np.array(second)
        pair_valid = (seq_rank + second < seq_count)[:, None]
        pair_gap = gap_later[second - 1] - through_later[first - 1]
        pair_terms = dots_later[second - 1, second - first - 1]
        pair_sum = jnp.sum(jnp.where(pair_valid, jnp.exp(jnp.where(pair_valid, pair_gap, 0.0)) * pair_terms, 0.0), axis=0)
    else:
        pair_sum = jnp.zeros_like(totals)
    later_sum = jnp.sum(closing_later, axis=0) - pair_sum

    state_dx = local_dx + jnp.einsum("hsn,hnp->hsp", weighted_in, incoming, precision=highest)
    terms = forward_term - jnp.sum(inputs_wide * state_dx, axis=2)
    grad_log_decay = later_sum[:, None] + lax.cumsum(terms, axis=1, reverse=True)
    grad_input_maps = (
        local_din
        + jnp.einsum("hnp,hsp->hsn", incoming, inputs_wide, precision=highest) * to_end[..., None]
    )
    grad_maps = jnp.concatenate([grad_input_maps, grad_output_maps], axis=2)
    grad_maps = grad_maps.reshape(local_groups, per_group, tok_dev, 2 * state_size).sum(axis=1)
    grad_x = state_dx + skip_gain[:, None, None] * grad_out
    return (grad_x.astype(jnp.bfloat16), grad_maps.astype(jnp.bfloat16), grad_log_decay)


def solution(mesh):
    in_specs = (
        P(("head", "sub"), ("groups", "seq"), None),
        P(("head", "sub"), ("groups", "seq"), None),
        P(("head", "sub"), ("groups", "seq"), None),
        P(("head", "sub"), ("groups", "seq"), None),
        P(("head", "sub"), ("groups", "seq")),
        P(("head", "sub")),
        P(("groups", "head", "sub"), None, None),
    )
    out_specs = (
        P(("head", "sub"), ("groups", "seq"), None),
        P(("head", "sub"), ("groups", "seq"), None),
        P(("head", "sub"), ("groups", "seq")),
    )
    return jax.shard_map(body, mesh=mesh, in_specs=in_specs, out_specs=out_specs, check_vma=False)
```

```python
import jax
import jax.numpy as jnp
from jax import lax
from jax.sharding import PartitionSpec as P

epsilon = 1e-05
highest = lax.Precision.HIGHEST


def split_three(values):
    top = lax.reduce_precision(values, exponent_bits=8, mantissa_bits=7)
    rest = values - top
    middle = lax.reduce_precision(rest, exponent_bits=8, mantissa_bits=7)
    low = rest - middle
    return jnp.stack([top, middle, low]).astype(jnp.bfloat16)


def join_three(parts):
    wide = parts.astype(jnp.float32)
    return wide[..., 0, :] + wide[..., 1, :] + wide[..., 2, :]


def pack_rows(big, smalls):
    rows = big.astype(jnp.bfloat16).reshape(-1, 128)
    vector = jnp.concatenate([v.reshape(-1) for v in smalls])
    padded = -(-vector.shape[0] // 128) * 128
    vector = jnp.pad(vector, (0, padded - vector.shape[0]))
    extra = split_three(vector).reshape(3 * padded // 128, 128)
    extra = jnp.pad(extra, ((0, (-extra.shape[0]) % 16), (0, 0)))
    return jnp.concatenate([rows, extra], axis=0)


def unpack_rows(received, big_shape, small_shapes):
    big_rows = 1
    for d in big_shape:
        big_rows *= d
    big_rows //= 128
    big = received[:big_rows].reshape(big_shape)
    sizes = []
    for shape in small_shapes:
        size = 1
        for d in shape:
            size *= d
        sizes.append(size)
    padded = -(-sum(sizes) // 128) * 128
    extra = received[big_rows : big_rows + 3 * padded // 128].reshape(3, padded)
    vector = join_three(extra)
    smalls = []
    offset = 0
    for shape, size in zip(small_shapes, sizes):
        smalls.append(vector[offset : offset + size].reshape(shape))
        offset += size
    return big, smalls


def shifted(x, step):
    seq_count = lax.axis_size("seq")
    seq_rank = lax.axis_index("seq")
    if seq_count <= 8:
        moved = []
        for distance in range(1, seq_count):
            if step > 0:
                pairs = [(j, j + distance) for j in range(seq_count - distance)]
            else:
                pairs = [(j + distance, j) for j in range(seq_count - distance)]
            moved.append(lax.ppermute(x, "seq", pairs))
        return moved
    gathered = lax.all_gather(x, "seq", axis=0)
    moved = []
    for distance in range(1, seq_count):
        source = seq_rank + step * distance
        valid = (source >= 0) & (source < seq_count)
        picked = lax.dynamic_index_in_dim(gathered, jnp.clip(source, 0, seq_count - 1), 0, False)
        moved.append(jnp.where(valid, picked, jnp.zeros_like(picked)))
    return moved


def teacher_rows(queries, kv_list, seq_rank):
    local_heads, tok_dev, head_width = queries.shape
    local_groups = kv_list[0].shape[0]
    per_group = local_heads // local_groups
    grouped = queries.reshape(local_groups, per_group, tok_dev, head_width)
    rows = jnp.arange(tok_dev)
    within = rows[:, None] >= rows[None, :]
    block_scores = []
    for distance, block in enumerate(kv_list):
        scores = jnp.einsum(
            "gptd,gkd->gptk", grouped, block[..., :head_width], preferred_element_type=jnp.float32
        )
        scores = scores * head_width ** (-0.5)
        if distance == 0:
            allowed = within
        else:
            allowed = distance <= seq_rank
        block_scores.append(jnp.where(allowed, scores, -jnp.inf))
    highest_score = block_scores[0].max(axis=3, keepdims=True)
    for scores in block_scores[1:]:
        highest_score = jnp.maximum(highest_score, scores.max(axis=3, keepdims=True))
    row_sums = None
    mixed = None
    for scores, block in zip(block_scores, kv_list):
        exponentials = jnp.exp(scores - highest_score)
        part_sum = jnp.sum(exponentials, axis=3, keepdims=True)
        part = jnp.einsum(
            "gptk,gkd->gptd",
            exponentials.astype(jnp.bfloat16),
            block[..., head_width:],
            preferred_element_type=jnp.float32,
        )
        row_sums = part_sum if row_sums is None else row_sums + part_sum
        mixed = part if mixed is None else mixed + part
    mixed = mixed / row_sums
    return mixed.astype(jnp.bfloat16).reshape(local_heads, tok_dev, head_width)


def body(queries, keys_values, student_x, state_maps, decay_logit, skip_gain, init_state):
    local_heads, tok_dev, head_width = student_x.shape
    local_groups = state_maps.shape[0]
    per_group = local_heads // local_groups
    state_size = state_maps.shape[2] // 2
    seq_count = lax.axis_size("seq")
    seq_rank = lax.axis_index("seq")

    kv_earlier = shifted(keys_values, 1)

    log_decay = jax.nn.log_sigmoid(decay_logit)
    cumulative = jnp.cumsum(log_decay, axis=1)
    totals = cumulative[:, -1]
    to_end = jnp.exp(totals[:, None] - cumulative)
    from_start = jnp.exp(cumulative)
    in_maps = state_maps[:, :, :state_size]
    out_maps = state_maps[:, :, state_size:]
    inputs_wide = student_x.astype(jnp.float32)
    in_heads = jnp.repeat(in_maps.astype(jnp.float32), per_group, axis=0)
    out_heads = jnp.repeat(out_maps.astype(jnp.float32), per_group, axis=0)
    weighted_in = in_heads * to_end[..., None]
    end_state = jnp.einsum("hsn,hsp->hnp", weighted_in, inputs_wide, precision=highest)

    state_earlier = shifted(pack_rows(end_state, [totals]), 1)
    ends_earlier = []
    prefix_state = jnp.zeros_like(end_state)
    gap = jnp.zeros_like(totals)
    for distance, received in enumerate(state_earlier, start=1):
        ends, (totals_there,) = unpack_rows(received, end_state.shape, [totals.shape])
        valid = distance <= seq_rank
        totals_there = jnp.where(valid, totals_there, 0.0)
        weight = jnp.where(valid, jnp.exp(gap), 0.0)
        ends_earlier.append(ends)
        prefix_state = prefix_state + weight[:, None, None] * ends.astype(jnp.float32)
        gap = gap + totals_there
    entering = prefix_state + jnp.exp(gap)[:, None, None] * init_state

    intersection = jnp.einsum("gtn,gsn->gts", out_maps, in_maps, preferred_element_type=jnp.float32)
    order_ids = jnp.arange(tok_dev)
    causal = (order_ids[:, None] >= order_ids[None, :])[None]
    gaps = cumulative[:, :, None] - cumulative[:, None, :]
    decayed = jnp.where(causal, jnp.exp(jnp.where(causal, gaps, 0.0)), 0.0)
    mixing = (
        decayed.reshape(local_groups, per_group, tok_dev, tok_dev) * intersection[:, None]
    ).reshape(local_heads, tok_dev, tok_dev)
    local_out = jnp.einsum("hts,hsp->htp", mixing, inputs_wide, precision=highest)

    teacher = teacher_rows(queries, [keys_values] + kv_earlier, seq_rank)
    teacher_wide = teacher.astype(jnp.float32)
    target = teacher_wide * lax.rsqrt(
        jnp.mean(teacher_wide * teacher_wide, axis=2, keepdims=True) + epsilon
    )

    state_out = local_out + from_start[..., None] * jnp.einsum(
        "htn,hnp->htp", out_heads, entering, precision=highest
    )
    outputs = state_out + skip_gain[:, None, None] * inputs_wide
    inverse = lax.rsqrt(jnp.mean(outputs * outputs, axis=2, keepdims=True) + epsilon)
    normed = outputs * inverse
    residual = normed - target
    grad_out = (residual - normed * jnp.mean(residual * normed, axis=2, keepdims=True)) * inverse
    forward_term = jnp.sum(grad_out * state_out, axis=2)
    flow = jnp.einsum(
        "htn,htp->hnp", out_heads * from_start[..., None], grad_out, precision=highest
    )
    local_dx = jnp.einsum("hts,htp->hsp", mixing, grad_out, precision=highest)
    closing = jnp.sum(forward_term - jnp.sum(inputs_wide * local_dx, axis=2), axis=1)
    if ends_earlier:
        ends_dot_flow = jnp.stack(
            [jnp.sum(ends.astype(jnp.float32) * flow, axis=(1, 2)) for ends in ends_earlier]
        )
    else:
        ends_dot_flow = jnp.zeros((1,) + totals.shape, jnp.float32)

    flow_later = shifted(pack_rows(flow, [totals, closing, ends_dot_flow]), -1)

    cross = jnp.einsum("htp,hsp->hts", grad_out, inputs_wide, precision=highest)
    paired = decayed * cross
    local_din = jnp.einsum("hts,htn->hsn", paired, out_heads, precision=highest)
    grad_output_maps = jnp.einsum("hts,hsn->htn", paired, in_heads, precision=highest)
    grad_output_maps = grad_output_maps + from_start[..., None] * jnp.einsum(
        "hnp,htp->htn", entering, grad_out, precision=highest
    )

    incoming = jnp.zeros_like(flow)
    later_sum = jnp.zeros_like(totals)
    gap = jnp.zeros_like(totals)
    through = []
    dots_there = []
    for distance, received in enumerate(flow_later, start=1):
        flows, (totals_there, closing_there, dots) = unpack_rows(
            received, flow.shape, [totals.shape, closing.shape, ends_dot_flow.shape]
        )
        valid = seq_rank + distance < seq_count
        totals_there = jnp.where(valid, totals_there, 0.0)
        weight = jnp.where(valid, jnp.exp(gap), 0.0)
        incoming = incoming + weight[:, None, None] * flows.astype(jnp.float32)
        later_sum = later_sum + jnp.where(valid, closing_there, 0.0)
        for early in range(1, distance):
            pair_gap = gap - through[early - 1]
            later_sum = later_sum - jnp.where(
                valid, jnp.exp(jnp.where(valid, pair_gap, 0.0)) * dots[distance - early - 1], 0.0
            )
        gap = gap + totals_there
        through.append(gap)

    state_dx = local_dx + jnp.einsum("hsn,hnp->hsp", weighted_in, incoming, precision=highest)
    terms = forward_term - jnp.sum(inputs_wide * state_dx, axis=2)
    grad_log_decay = later_sum[:, None] + lax.cumsum(terms, axis=1, reverse=True)
    grad_input_maps = (
        local_din
        + jnp.einsum("hnp,hsp->hsn", incoming, inputs_wide, precision=highest) * to_end[..., None]
    )
    grad_maps = jnp.concatenate([grad_input_maps, grad_output_maps], axis=2)
    grad_maps = grad_maps.reshape(local_groups, per_group, tok_dev, 2 * state_size).sum(axis=1)
    grad_x = state_dx + skip_gain[:, None, None] * grad_out
    return (grad_x.astype(jnp.bfloat16), grad_maps.astype(jnp.bfloat16), grad_log_decay)


def solution(mesh):
    in_specs = (
        P(("head", "sub"), ("groups", "seq"), None),
        P(("head", "sub"), ("groups", "seq"), None),
        P(("head", "sub"), ("groups", "seq"), None),
        P(("head", "sub"), ("groups", "seq"), None),
        P(("head", "sub"), ("groups", "seq")),
        P(("head", "sub")),
        P(("groups", "head", "sub"), None, None),
    )
    out_specs = (
        P(("head", "sub"), ("groups", "seq"), None),
        P(("head", "sub"), ("groups", "seq"), None),
        P(("head", "sub"), ("groups", "seq")),
    )
    return jax.shard_map(body, mesh=mesh, in_specs=in_specs, out_specs=out_specs, check_vma=False)
```

```python
import jax
import jax.numpy as jnp
from jax import lax
from jax.sharding import PartitionSpec as P

epsilon = 1e-05
highest = lax.Precision.HIGHEST


def split_three(values):
    top = lax.reduce_precision(values, exponent_bits=8, mantissa_bits=7)
    rest = values - top
    middle = lax.reduce_precision(rest, exponent_bits=8, mantissa_bits=7)
    low = rest - middle
    return jnp.stack([top, middle, low]).astype(jnp.bfloat16)


def join_three(parts):
    wide = parts.astype(jnp.float32)
    return wide[..., 0, :] + wide[..., 1, :] + wide[..., 2, :]


def pack_rows(bigs, smalls):
    rows = jnp.concatenate([b.astype(jnp.bfloat16).reshape(-1, 128) for b in bigs], axis=0)
    vector = jnp.concatenate([v.reshape(-1) for v in smalls])
    padded = -(-vector.shape[0] // 128) * 128
    vector = jnp.pad(vector, (0, padded - vector.shape[0]))
    extra = split_three(vector).reshape(3 * padded // 128, 128)
    extra = jnp.pad(extra, ((0, (-extra.shape[0]) % 16), (0, 0)))
    return jnp.concatenate([rows, extra], axis=0)


def unpack_rows(received, big_shapes, small_shapes):
    bigs = []
    big_rows = 0
    for shape in big_shapes:
        count = 1
        for d in shape:
            count *= d
        count //= 128
        bigs.append(received[big_rows : big_rows + count].reshape(shape))
        big_rows += count
    sizes = []
    for shape in small_shapes:
        size = 1
        for d in shape:
            size *= d
        sizes.append(size)
    padded = -(-sum(sizes) // 128) * 128
    extra = received[big_rows : big_rows + 3 * padded // 128].reshape(3, padded)
    vector = join_three(extra)
    smalls = []
    offset = 0
    for shape, size in zip(small_shapes, sizes):
        smalls.append(vector[offset : offset + size].reshape(shape))
        offset += size
    return bigs, smalls


def shifted(x, step):
    seq_count = lax.axis_size("seq")
    seq_rank = lax.axis_index("seq")
    if seq_count <= 8:
        moved = []
        for distance in range(1, seq_count):
            if step > 0:
                pairs = [(j, j + distance) for j in range(seq_count - distance)]
            else:
                pairs = [(j + distance, j) for j in range(seq_count - distance)]
            moved.append(lax.ppermute(x, "seq", pairs))
        return moved
    gathered = lax.all_gather(x, "seq", axis=0)
    moved = []
    for distance in range(1, seq_count):
        source = seq_rank + step * distance
        valid = (source >= 0) & (source < seq_count)
        picked = lax.dynamic_index_in_dim(gathered, jnp.clip(source, 0, seq_count - 1), 0, False)
        moved.append(jnp.where(valid, picked, jnp.zeros_like(picked)))
    return moved


def teacher_rows(queries, kv_list, seq_rank):
    local_heads, tok_dev, head_width = queries.shape
    local_groups = kv_list[0][0].shape[0]
    per_group = local_heads // local_groups
    grouped = queries.reshape(local_groups, per_group, tok_dev, head_width)
    rows = jnp.arange(tok_dev)
    within = rows[:, None] >= rows[None, :]
    block_scores = []
    for distance, (keys, _) in enumerate(kv_list):
        scores = jnp.einsum("gptd,gkd->gptk", grouped, keys, preferred_element_type=jnp.float32)
        scores = scores * head_width ** (-0.5)
        if distance == 0:
            allowed = within
        else:
            allowed = distance <= seq_rank
        block_scores.append(jnp.where(allowed, scores, -jnp.inf))
    highest_score = block_scores[0].max(axis=3, keepdims=True)
    for scores in block_scores[1:]:
        highest_score = jnp.maximum(highest_score, scores.max(axis=3, keepdims=True))
    row_sums = None
    mixed = None
    for scores, (_, values) in zip(block_scores, kv_list):
        exponentials = jnp.exp(scores - highest_score)
        part_sum = jnp.sum(exponentials, axis=3, keepdims=True)
        part = jnp.einsum(
            "gptk,gkd->gptd",
            exponentials.astype(jnp.bfloat16),
            values,
            preferred_element_type=jnp.float32,
        )
        row_sums = part_sum if row_sums is None else row_sums + part_sum
        mixed = part if mixed is None else mixed + part
    mixed = mixed / row_sums
    return mixed.astype(jnp.bfloat16).reshape(local_heads, tok_dev, head_width)


def body(queries, keys_values, student_x, state_maps, decay_logit, skip_gain, init_state):
    local_heads, tok_dev, head_width = student_x.shape
    local_groups = state_maps.shape[0]
    per_group = local_heads // local_groups
    state_size = state_maps.shape[2] // 2
    seq_count = lax.axis_size("seq")
    seq_rank = lax.axis_index("seq")

    log_decay = jax.nn.log_sigmoid(decay_logit)
    cumulative = jnp.cumsum(log_decay, axis=1)
    totals = cumulative[:, -1]
    to_end = jnp.exp(totals[:, None] - cumulative)
    from_start = jnp.exp(cumulative)
    in_maps = state_maps[:, :, :state_size]
    out_maps = state_maps[:, :, state_size:]
    inputs_wide = student_x.astype(jnp.float32)
    in_heads = jnp.repeat(in_maps.astype(jnp.float32), per_group, axis=0)
    out_heads = jnp.repeat(out_maps.astype(jnp.float32), per_group, axis=0)
    weighted_in = in_heads * to_end[..., None]
    end_state = jnp.einsum("hsn,hsp->hnp", weighted_in, inputs_wide, precision=highest)

    own_keys = keys_values[..., :head_width]
    own_values = keys_values[..., head_width:]
    state_earlier = shifted(pack_rows([own_keys, own_values, end_state], [totals]), 1)
    kv_earlier = []
    ends_earlier = []
    prefix_state = jnp.zeros_like(end_state)
    gap = jnp.zeros_like(totals)
    for distance, received in enumerate(state_earlier, start=1):
        (keys_there, values_there, ends), (totals_there,) = unpack_rows(
            received, [own_keys.shape, own_values.shape, end_state.shape], [totals.shape]
        )
        kv_earlier.append((keys_there, values_there))
        valid = distance <= seq_rank
        totals_there = jnp.where(valid, totals_there, 0.0)
        weight = jnp.where(valid, jnp.exp(gap), 0.0)
        ends_earlier.append(ends)
        prefix_state = prefix_state + weight[:, None, None] * ends.astype(jnp.float32)
        gap = gap + totals_there
    entering = prefix_state + jnp.exp(gap)[:, None, None] * init_state

    intersection = jnp.einsum("gtn,gsn->gts", out_maps, in_maps, preferred_element_type=jnp.float32)
    order_ids = jnp.arange(tok_dev)
    causal = (order_ids[:, None] >= order_ids[None, :])[None]
    gaps = cumulative[:, :, None] - cumulative[:, None, :]
    decayed = jnp.where(causal, jnp.exp(jnp.where(causal, gaps, 0.0)), 0.0)
    mixing = (
        decayed.reshape(local_groups, per_group, tok_dev, tok_dev) * intersection[:, None]
    ).reshape(local_heads, tok_dev, tok_dev)
    local_out = jnp.einsum("hts,hsp->htp", mixing, inputs_wide, precision=highest)

    teacher = teacher_rows(queries, [(own_keys, own_values)] + kv_earlier, seq_rank)
    teacher_wide = teacher.astype(jnp.float32)
    target = teacher_wide * lax.rsqrt(
        jnp.mean(teacher_wide * teacher_wide, axis=2, keepdims=True) + epsilon
    )

    state_out = local_out + from_start[..., None] * jnp.einsum(
        "htn,hnp->htp", out_heads, entering, precision=highest
    )
    outputs = state_out + skip_gain[:, None, None] * inputs_wide
    inverse = lax.rsqrt(jnp.mean(outputs * outputs, axis=2, keepdims=True) + epsilon)
    normed = outputs * inverse
    residual = normed - target
    grad_out = (residual - normed * jnp.mean(residual * normed, axis=2, keepdims=True)) * inverse
    forward_term = jnp.sum(grad_out * state_out, axis=2)
    flow = jnp.einsum(
        "htn,htp->hnp", out_heads * from_start[..., None], grad_out, precision=highest
    )
    local_dx = jnp.einsum("hts,htp->hsp", mixing, grad_out, precision=highest)
    closing = jnp.sum(forward_term - jnp.sum(inputs_wide * local_dx, axis=2), axis=1)
    if ends_earlier:
        ends_dot_flow = jnp.stack(
            [jnp.sum(ends.astype(jnp.float32) * flow, axis=(1, 2)) for ends in ends_earlier]
        )
    else:
        ends_dot_flow = jnp.zeros((1,) + totals.shape, jnp.float32)

    flow_later = shifted(pack_rows([flow], [totals, closing, ends_dot_flow]), -1)

    cross = jnp.einsum("htp,hsp->hts", grad_out, inputs_wide, precision=highest)
    paired = decayed * cross
    local_din = jnp.einsum("hts,htn->hsn", paired, out_heads, precision=highest)
    grad_output_maps = jnp.einsum("hts,hsn->htn", paired, in_heads, precision=highest)
    grad_output_maps = grad_output_maps + from_start[..., None] * jnp.einsum(
        "hnp,htp->htn", entering, grad_out, precision=highest
    )

    incoming = jnp.zeros_like(flow)
    later_sum = jnp.zeros_like(totals)
    gap = jnp.zeros_like(totals)
    through = []
    dots_there = []
    for distance, received in enumerate(flow_later, start=1):
        (flows,), (totals_there, closing_there, dots) = unpack_rows(
            received, [flow.shape], [totals.shape, closing.shape, ends_dot_flow.shape]
        )
        valid = seq_rank + distance < seq_count
        totals_there = jnp.where(valid, totals_there, 0.0)
        weight = jnp.where(valid, jnp.exp(gap), 0.0)
        incoming = incoming + weight[:, None, None] * flows.astype(jnp.float32)
        later_sum = later_sum + jnp.where(valid, closing_there, 0.0)
        for early in range(1, distance):
            pair_gap = gap - through[early - 1]
            later_sum = later_sum - jnp.where(
                valid, jnp.exp(jnp.where(valid, pair_gap, 0.0)) * dots[distance - early - 1], 0.0
            )
        gap = gap + totals_there
        through.append(gap)

    state_dx = local_dx + jnp.einsum("hsn,hnp->hsp", weighted_in, incoming, precision=highest)
    terms = forward_term - jnp.sum(inputs_wide * state_dx, axis=2)
    grad_log_decay = later_sum[:, None] + lax.cumsum(terms, axis=1, reverse=True)
    grad_input_maps = (
        local_din
        + jnp.einsum("hnp,hsp->hsn", incoming, inputs_wide, precision=highest) * to_end[..., None]
    )
    grad_maps = jnp.concatenate([grad_input_maps, grad_output_maps], axis=2)
    grad_maps = grad_maps.reshape(local_groups, per_group, tok_dev, 2 * state_size).sum(axis=1)
    grad_x = state_dx + skip_gain[:, None, None] * grad_out
    return (grad_x.astype(jnp.bfloat16), grad_maps.astype(jnp.bfloat16), grad_log_decay)


def solution(mesh):
    in_specs = (
        P(("head", "sub"), ("groups", "seq"), None),
        P(("head", "sub"), ("groups", "seq"), None),
        P(("head", "sub"), ("groups", "seq"), None),
        P(("head", "sub"), ("groups", "seq"), None),
        P(("head", "sub"), ("groups", "seq")),
        P(("head", "sub")),
        P(("groups", "head", "sub"), None, None),
    )
    out_specs = (
        P(("head", "sub"), ("groups", "seq"), None),
        P(("head", "sub"), ("groups", "seq"), None),
        P(("head", "sub"), ("groups", "seq")),
    )
    return jax.shard_map(body, mesh=mesh, in_specs=in_specs, out_specs=out_specs, check_vma=False)
```

```python
import jax
import jax.numpy as jnp
from jax import lax
from jax.sharding import PartitionSpec as P

epsilon = 1e-05
highest = lax.Precision.HIGHEST


def split_three(values):
    top = lax.reduce_precision(values, exponent_bits=8, mantissa_bits=7)
    rest = values - top
    middle = lax.reduce_precision(rest, exponent_bits=8, mantissa_bits=7)
    low = rest - middle
    return jnp.stack([top, middle, low]).astype(jnp.bfloat16)


def join_three(parts):
    wide = parts.astype(jnp.float32)
    return wide[..., 0, :] + wide[..., 1, :] + wide[..., 2, :]


def pack_rows(big, smalls):
    rows = big.astype(jnp.bfloat16).reshape(-1, 128)
    vector = jnp.concatenate([v.reshape(-1) for v in smalls])
    padded = -(-vector.shape[0] // 128) * 128
    vector = jnp.pad(vector, (0, padded - vector.shape[0]))
    extra = split_three(vector).reshape(3 * padded // 128, 128)
    extra = jnp.pad(extra, ((0, (-extra.shape[0]) % 16), (0, 0)))
    return jnp.concatenate([rows, extra], axis=0)


def unpack_rows(received, big_shape, small_shapes):
    big_rows = 1
    for d in big_shape:
        big_rows *= d
    big_rows //= 128
    big = received[:big_rows].reshape(big_shape)
    sizes = []
    for shape in small_shapes:
        size = 1
        for d in shape:
            size *= d
        sizes.append(size)
    padded = -(-sum(sizes) // 128) * 128
    extra = received[big_rows : big_rows + 3 * padded // 128].reshape(3, padded)
    vector = join_three(extra)
    smalls = []
    offset = 0
    for shape, size in zip(small_shapes, sizes):
        smalls.append(vector[offset : offset + size].reshape(shape))
        offset += size
    return big, smalls


def shifted(x, step):
    seq_count = lax.axis_size("seq")
    seq_rank = lax.axis_index("seq")
    if seq_count <= 8:
        moved = []
        for distance in range(1, seq_count):
            if step > 0:
                pairs = [(j, j + distance) for j in range(seq_count - distance)]
            else:
                pairs = [(j + distance, j) for j in range(seq_count - distance)]
            moved.append(lax.ppermute(x, "seq", pairs))
        return moved
    gathered = lax.all_gather(x, "seq", axis=0)
    moved = []
    for distance in range(1, seq_count):
        source = seq_rank + step * distance
        valid = (source >= 0) & (source < seq_count)
        picked = lax.dynamic_index_in_dim(gathered, jnp.clip(source, 0, seq_count - 1), 0, False)
        moved.append(jnp.where(valid, picked, jnp.zeros_like(picked)))
    return moved


def teacher_rows(queries, kv_list, seq_rank):
    local_heads, tok_dev, head_width = queries.shape
    local_groups = kv_list[0].shape[0]
    per_group = local_heads // local_groups
    grouped = queries.reshape(local_groups, per_group, tok_dev, head_width)
    rows = jnp.arange(tok_dev)
    within = rows[:, None] >= rows[None, :]
    block_scores = []
    for distance, block in enumerate(kv_list):
        scores = jnp.einsum(
            "gptd,gkd->gptk", grouped, block[..., :head_width], preferred_element_type=jnp.float32
        )
        scores = scores * head_width ** (-0.5)
        if distance == 0:
            allowed = within
        else:
            allowed = distance <= seq_rank
        block_scores.append(jnp.where(allowed, scores, -jnp.inf))
    highest_score = block_scores[0].max(axis=3, keepdims=True)
    for scores in block_scores[1:]:
        highest_score = jnp.maximum(highest_score, scores.max(axis=3, keepdims=True))
    row_sums = None
    mixed = None
    for scores, block in zip(block_scores, kv_list):
        exponentials = jnp.exp(scores - highest_score)
        part_sum = jnp.sum(exponentials, axis=3, keepdims=True)
        part = jnp.einsum(
            "gptk,gkd->gptd",
            exponentials.astype(jnp.bfloat16),
            block[..., head_width:],
            preferred_element_type=jnp.float32,
        )
        row_sums = part_sum if row_sums is None else row_sums + part_sum
        mixed = part if mixed is None else mixed + part
    mixed = mixed / row_sums
    return mixed.astype(jnp.bfloat16).reshape(local_heads, tok_dev, head_width)


def group_body(queries, keys_values, student_x, state_maps, decay_logit, skip_gain, init_state):
    local_heads, tok_dev, head_width = student_x.shape
    local_groups = state_maps.shape[0]
    per_group = local_heads // local_groups
    state_size = state_maps.shape[2] // 2
    seq_count = lax.axis_size("seq")
    seq_rank = lax.axis_index("seq")

    kv_earlier = shifted(keys_values, 1)

    log_decay = jax.nn.log_sigmoid(decay_logit)
    cumulative = jnp.cumsum(log_decay, axis=1)
    totals = cumulative[:, -1]
    to_end = jnp.exp(totals[:, None] - cumulative)
    from_start = jnp.exp(cumulative)
    in_maps = state_maps[:, :, :state_size]
    out_maps = state_maps[:, :, state_size:]
    inputs_wide = student_x.astype(jnp.float32)
    in_heads = jnp.repeat(in_maps.astype(jnp.float32), per_group, axis=0)
    out_heads = jnp.repeat(out_maps.astype(jnp.float32), per_group, axis=0)
    weighted_in = in_heads * to_end[..., None]
    end_state = jnp.einsum("hsn,hsp->hnp", weighted_in, inputs_wide, precision=highest)

    state_earlier = shifted(pack_rows(end_state, [totals]), 1)
    ends_earlier = []
    prefix_state = jnp.zeros_like(end_state)
    gap = jnp.zeros_like(totals)
    for distance, received in enumerate(state_earlier, start=1):
        ends, (totals_there,) = unpack_rows(received, end_state.shape, [totals.shape])
        valid = distance <= seq_rank
        totals_there = jnp.where(valid, totals_there, 0.0)
        weight = jnp.where(valid, jnp.exp(gap), 0.0)
        ends_earlier.append(ends)
        prefix_state = prefix_state + weight[:, None, None] * ends.astype(jnp.float32)
        gap = gap + totals_there
    entering = prefix_state + jnp.exp(gap)[:, None, None] * init_state

    intersection = jnp.einsum("gtn,gsn->gts", out_maps, in_maps, preferred_element_type=jnp.float32)
    order_ids = jnp.arange(tok_dev)
    causal = (order_ids[:, None] >= order_ids[None, :])[None]
    gaps = cumulative[:, :, None] - cumulative[:, None, :]
    decayed = jnp.where(causal, jnp.exp(jnp.where(causal, gaps, 0.0)), 0.0)
    mixing = (
        decayed.reshape(local_groups, per_group, tok_dev, tok_dev) * intersection[:, None]
    ).reshape(local_heads, tok_dev, tok_dev)
    local_out = jnp.einsum("hts,hsp->htp", mixing, inputs_wide, precision=highest)

    teacher = teacher_rows(queries, [keys_values] + kv_earlier, seq_rank)
    teacher_wide = teacher.astype(jnp.float32)
    target = teacher_wide * lax.rsqrt(
        jnp.mean(teacher_wide * teacher_wide, axis=2, keepdims=True) + epsilon
    )

    state_out = local_out + from_start[..., None] * jnp.einsum(
        "htn,hnp->htp", out_heads, entering, precision=highest
    )
    outputs = state_out + skip_gain[:, None, None] * inputs_wide
    inverse = lax.rsqrt(jnp.mean(outputs * outputs, axis=2, keepdims=True) + epsilon)
    normed = outputs * inverse
    residual = normed - target
    grad_out = (residual - normed * jnp.mean(residual * normed, axis=2, keepdims=True)) * inverse
    forward_term = jnp.sum(grad_out * state_out, axis=2)
    flow = jnp.einsum(
        "htn,htp->hnp", out_heads * from_start[..., None], grad_out, precision=highest
    )
    local_dx = jnp.einsum("hts,htp->hsp", mixing, grad_out, precision=highest)
    closing = jnp.sum(forward_term - jnp.sum(inputs_wide * local_dx, axis=2), axis=1)
    if ends_earlier:
        ends_dot_flow = jnp.stack(
            [jnp.sum(ends.astype(jnp.float32) * flow, axis=(1, 2)) for ends in ends_earlier]
        )
    else:
        ends_dot_flow = jnp.zeros((1,) + totals.shape, jnp.float32)

    flow_later = shifted(pack_rows(flow, [totals, closing, ends_dot_flow]), -1)

    cross = jnp.einsum("htp,hsp->hts", grad_out, inputs_wide, precision=highest)
    paired = decayed * cross
    local_din = jnp.einsum("hts,htn->hsn", paired, out_heads, precision=highest)
    grad_output_maps = jnp.einsum("hts,hsn->htn", paired, in_heads, precision=highest)
    grad_output_maps = grad_output_maps + from_start[..., None] * jnp.einsum(
        "hnp,htp->htn", entering, grad_out, precision=highest
    )

    incoming = jnp.zeros_like(flow)
    later_sum = jnp.zeros_like(totals)
    gap = jnp.zeros_like(totals)
    through = []
    dots_there = []
    for distance, received in enumerate(flow_later, start=1):
        flows, (totals_there, closing_there, dots) = unpack_rows(
            received, flow.shape, [totals.shape, closing.shape, ends_dot_flow.shape]
        )
        valid = seq_rank + distance < seq_count
        totals_there = jnp.where(valid, totals_there, 0.0)
        weight = jnp.where(valid, jnp.exp(gap), 0.0)
        incoming = incoming + weight[:, None, None] * flows.astype(jnp.float32)
        later_sum = later_sum + jnp.where(valid, closing_there, 0.0)
        for early in range(1, distance):
            pair_gap = gap - through[early - 1]
            later_sum = later_sum - jnp.where(
                valid, jnp.exp(jnp.where(valid, pair_gap, 0.0)) * dots[distance - early - 1], 0.0
            )
        gap = gap + totals_there
        through.append(gap)

    state_dx = local_dx + jnp.einsum("hsn,hnp->hsp", weighted_in, incoming, precision=highest)
    terms = forward_term - jnp.sum(inputs_wide * state_dx, axis=2)
    grad_log_decay = later_sum[:, None] + lax.cumsum(terms, axis=1, reverse=True)
    grad_input_maps = (
        local_din
        + jnp.einsum("hnp,hsp->hsn", incoming, inputs_wide, precision=highest) * to_end[..., None]
    )
    grad_maps = jnp.concatenate([grad_input_maps, grad_output_maps], axis=2)
    grad_maps = grad_maps.reshape(local_groups, per_group, tok_dev, 2 * state_size).sum(axis=1)
    grad_x = state_dx + skip_gain[:, None, None] * grad_out
    return (grad_x.astype(jnp.bfloat16), grad_maps.astype(jnp.bfloat16), grad_log_decay)


def body(queries, keys_values, student_x, state_maps, decay_logit, skip_gain, init_state):
    local_groups = state_maps.shape[0]
    per_group = student_x.shape[0] // local_groups
    results = []
    for group in range(local_groups):
        heads = slice(group * per_group, (group + 1) * per_group)
        results.append(
            group_body(
                queries[heads],
                keys_values[group : group + 1],
                student_x[heads],
                state_maps[group : group + 1],
                decay_logit[heads],
                skip_gain[heads],
                init_state[heads],
            )
        )
    return tuple(jnp.concatenate(parts, axis=0) for parts in zip(*results))


def solution(mesh):
    in_specs = (
        P(("head", "sub"), ("groups", "seq"), None),
        P(("head", "sub"), ("groups", "seq"), None),
        P(("head", "sub"), ("groups", "seq"), None),
        P(("head", "sub"), ("groups", "seq"), None),
        P(("head", "sub"), ("groups", "seq")),
        P(("head", "sub")),
        P(("groups", "head", "sub"), None, None),
    )
    out_specs = (
        P(("head", "sub"), ("groups", "seq"), None),
        P(("head", "sub"), ("groups", "seq"), None),
        P(("head", "sub"), ("groups", "seq")),
    )
    return jax.shard_map(body, mesh=mesh, in_specs=in_specs, out_specs=out_specs, check_vma=False)
```

```python
import jax
import jax.numpy as jnp
from jax import lax
from jax.sharding import PartitionSpec as P

epsilon = 1e-05
highest = lax.Precision.HIGHEST


def split_three(values):
    top = lax.reduce_precision(values, exponent_bits=8, mantissa_bits=7)
    rest = values - top
    middle = lax.reduce_precision(rest, exponent_bits=8, mantissa_bits=7)
    low = rest - middle
    return jnp.stack([top, middle, low]).astype(jnp.bfloat16)


def join_three(parts):
    wide = parts.astype(jnp.float32)
    return wide[..., 0, :] + wide[..., 1, :] + wide[..., 2, :]


def pack_rows(big, smalls):
    rows = big.astype(jnp.bfloat16).reshape(-1, 128)
    vector = jnp.concatenate([v.reshape(-1) for v in smalls])
    padded = -(-vector.shape[0] // 128) * 128
    vector = jnp.pad(vector, (0, padded - vector.shape[0]))
    extra = split_three(vector).reshape(3 * padded // 128, 128)
    extra = jnp.pad(extra, ((0, (-extra.shape[0]) % 16), (0, 0)))
    return jnp.concatenate([rows, extra], axis=0)


def unpack_rows(received, big_shape, small_shapes):
    big_rows = 1
    for d in big_shape:
        big_rows *= d
    big_rows //= 128
    big = received[:big_rows].reshape(big_shape)
    sizes = []
    for shape in small_shapes:
        size = 1
        for d in shape:
            size *= d
        sizes.append(size)
    padded = -(-sum(sizes) // 128) * 128
    extra = received[big_rows : big_rows + 3 * padded // 128].reshape(3, padded)
    vector = join_three(extra)
    smalls = []
    offset = 0
    for shape, size in zip(small_shapes, sizes):
        smalls.append(vector[offset : offset + size].reshape(shape))
        offset += size
    return big, smalls


def shifted(x, step):
    seq_count = lax.axis_size("seq")
    seq_rank = lax.axis_index("seq")
    if seq_count <= 8:
        moved = []
        for distance in range(1, seq_count):
            if step > 0:
                pairs = [(j, j + distance) for j in range(seq_count - distance)]
            else:
                pairs = [(j + distance, j) for j in range(seq_count - distance)]
            moved.append(lax.ppermute(x, "seq", pairs))
        return moved
    gathered = lax.all_gather(x, "seq", axis=0)
    moved = []
    for distance in range(1, seq_count):
        source = seq_rank + step * distance
        valid = (source >= 0) & (source < seq_count)
        picked = lax.dynamic_index_in_dim(gathered, jnp.clip(source, 0, seq_count - 1), 0, False)
        moved.append(jnp.where(valid, picked, jnp.zeros_like(picked)))
    return moved


def teacher_rows(queries, kv_list, seq_rank):
    local_heads, tok_dev, head_width = queries.shape
    local_groups = kv_list[0].shape[0]
    per_group = local_heads // local_groups
    grouped = queries.reshape(local_groups, per_group, tok_dev, head_width)
    rows = jnp.arange(tok_dev)
    within = rows[:, None] >= rows[None, :]
    block_scores = []
    for distance, block in enumerate(kv_list):
        scores = jnp.einsum(
            "gptd,gkd->gptk", grouped, block[..., :head_width], preferred_element_type=jnp.float32
        )
        scores = scores * head_width ** (-0.5)
        if distance == 0:
            allowed = within
        else:
            allowed = distance <= seq_rank
        block_scores.append(jnp.where(allowed, scores, -jnp.inf))
    highest_score = block_scores[0].max(axis=3, keepdims=True)
    for scores in block_scores[1:]:
        highest_score = jnp.maximum(highest_score, scores.max(axis=3, keepdims=True))
    row_sums = None
    mixed = None
    for scores, block in zip(block_scores, kv_list):
        exponentials = jnp.exp(scores - highest_score)
        part_sum = jnp.sum(exponentials, axis=3, keepdims=True)
        part = jnp.einsum(
            "gptk,gkd->gptd",
            exponentials.astype(jnp.bfloat16),
            block[..., head_width:],
            preferred_element_type=jnp.float32,
        )
        row_sums = part_sum if row_sums is None else row_sums + part_sum
        mixed = part if mixed is None else mixed + part
    mixed = mixed / row_sums
    return mixed.astype(jnp.bfloat16).reshape(local_heads, tok_dev, head_width)


def body(queries, keys_values, student_x, state_maps, decay_logit, skip_gain, init_state):
    local_heads, tok_dev, head_width = student_x.shape
    local_groups = state_maps.shape[0]
    per_group = local_heads // local_groups
    state_size = state_maps.shape[2] // 2
    seq_count = lax.axis_size("seq")
    seq_rank = lax.axis_index("seq")

    kv_earlier = shifted(keys_values, 1)

    log_decay = jax.nn.log_sigmoid(decay_logit)
    cumulative = jnp.cumsum(log_decay, axis=1)
    totals = cumulative[:, -1]
    to_end = jnp.exp(totals[:, None] - cumulative)
    from_start = jnp.exp(cumulative)
    in_maps = state_maps[:, :, :state_size]
    out_maps = state_maps[:, :, state_size:]
    inputs_wide = student_x.astype(jnp.float32)
    in_heads = jnp.repeat(in_maps.astype(jnp.float32), per_group, axis=0)
    out_heads = jnp.repeat(out_maps.astype(jnp.float32), per_group, axis=0)
    weighted_in = in_heads * to_end[..., None]
    end_state = jnp.einsum("hsn,hsp->hnp", weighted_in, inputs_wide, precision=highest)

    state_earlier = shifted(pack_rows(end_state, [totals]), 1)
    ends_earlier = []
    prefix_state = jnp.zeros_like(end_state)
    gap = jnp.zeros_like(totals)
    for distance, received in enumerate(state_earlier, start=1):
        ends, (totals_there,) = unpack_rows(received, end_state.shape, [totals.shape])
        valid = distance <= seq_rank
        totals_there = jnp.where(valid, totals_there, 0.0)
        weight = jnp.where(valid, jnp.exp(gap), 0.0)
        ends_earlier.append(ends)
        prefix_state = prefix_state + weight[:, None, None] * ends.astype(jnp.float32)
        gap = gap + totals_there
    entering = prefix_state + jnp.exp(gap)[:, None, None] * init_state

    intersection = jnp.einsum("gtn,gsn->gts", out_maps, in_maps, preferred_element_type=jnp.float32)
    order_ids = jnp.arange(tok_dev)
    causal = (order_ids[:, None] >= order_ids[None, :])[None]
    gaps = cumulative[:, :, None] - cumulative[:, None, :]
    decayed = jnp.where(causal, jnp.exp(jnp.where(causal, gaps, 0.0)), 0.0)
    mixing = (
        decayed.reshape(local_groups, per_group, tok_dev, tok_dev) * intersection[:, None]
    ).reshape(local_heads, tok_dev, tok_dev)
    local_out = jnp.einsum("hts,hsp->htp", mixing, inputs_wide, precision=highest)

    teacher = teacher_rows(queries, [keys_values] + kv_earlier, seq_rank)
    teacher_wide = teacher.astype(jnp.float32)
    target = teacher_wide * lax.rsqrt(
        jnp.mean(teacher_wide * teacher_wide, axis=2, keepdims=True) + epsilon
    )

    state_out = local_out + from_start[..., None] * jnp.einsum(
        "htn,hnp->htp", out_heads, entering, precision=highest
    )
    outputs = state_out + skip_gain[:, None, None] * inputs_wide
    inverse = lax.rsqrt(jnp.mean(outputs * outputs, axis=2, keepdims=True) + epsilon)
    normed = outputs * inverse
    residual = normed - target
    grad_out = (residual - normed * jnp.mean(residual * normed, axis=2, keepdims=True)) * inverse
    forward_term = jnp.sum(grad_out * state_out, axis=2)
    flow = jnp.einsum(
        "htn,htp->hnp", out_heads * from_start[..., None], grad_out, precision=highest
    )
    closing = jnp.sum(flow * entering, axis=(1, 2))
    if ends_earlier:
        ends_dot_flow = jnp.stack(
            [jnp.sum(ends.astype(jnp.float32) * flow, axis=(1, 2)) for ends in ends_earlier]
        )
    else:
        ends_dot_flow = jnp.zeros((1,) + totals.shape, jnp.float32)

    flow_later = shifted(pack_rows(flow, [totals, closing, ends_dot_flow]), -1)

    local_dx = jnp.einsum("hts,htp->hsp", mixing, grad_out, precision=highest)

    cross = jnp.einsum("htp,hsp->hts", grad_out, inputs_wide, precision=highest)
    paired = decayed * cross
    local_din = jnp.einsum("hts,htn->hsn", paired, out_heads, precision=highest)
    grad_output_maps = jnp.einsum("hts,hsn->htn", paired, in_heads, precision=highest)
    grad_output_maps = grad_output_maps + from_start[..., None] * jnp.einsum(
        "hnp,htp->htn", entering, grad_out, precision=highest
    )

    incoming = jnp.zeros_like(flow)
    later_sum = jnp.zeros_like(totals)
    gap = jnp.zeros_like(totals)
    through = []
    dots_there = []
    for distance, received in enumerate(flow_later, start=1):
        flows, (totals_there, closing_there, dots) = unpack_rows(
            received, flow.shape, [totals.shape, closing.shape, ends_dot_flow.shape]
        )
        valid = seq_rank + distance < seq_count
        totals_there = jnp.where(valid, totals_there, 0.0)
        weight = jnp.where(valid, jnp.exp(gap), 0.0)
        incoming = incoming + weight[:, None, None] * flows.astype(jnp.float32)
        later_sum = later_sum + jnp.where(valid, closing_there, 0.0)
        for early in range(1, distance):
            pair_gap = gap - through[early - 1]
            later_sum = later_sum - jnp.where(
                valid, jnp.exp(jnp.where(valid, pair_gap, 0.0)) * dots[distance - early - 1], 0.0
            )
        gap = gap + totals_there
        through.append(gap)

    state_dx = local_dx + jnp.einsum("hsn,hnp->hsp", weighted_in, incoming, precision=highest)
    terms = forward_term - jnp.sum(inputs_wide * state_dx, axis=2)
    grad_log_decay = later_sum[:, None] + lax.cumsum(terms, axis=1, reverse=True)
    grad_input_maps = (
        local_din
        + jnp.einsum("hnp,hsp->hsn", incoming, inputs_wide, precision=highest) * to_end[..., None]
    )
    grad_maps = jnp.concatenate([grad_input_maps, grad_output_maps], axis=2)
    grad_maps = grad_maps.reshape(local_groups, per_group, tok_dev, 2 * state_size).sum(axis=1)
    grad_x = state_dx + skip_gain[:, None, None] * grad_out
    return (grad_x.astype(jnp.bfloat16), grad_maps.astype(jnp.bfloat16), grad_log_decay)


def solution(mesh):
    in_specs = (
        P(("head", "sub"), ("groups", "seq"), None),
        P(("head", "sub"), ("groups", "seq"), None),
        P(("head", "sub"), ("groups", "seq"), None),
        P(("head", "sub"), ("groups", "seq"), None),
        P(("head", "sub"), ("groups", "seq")),
        P(("head", "sub")),
        P(("groups", "head", "sub"), None, None),
    )
    out_specs = (
        P(("head", "sub"), ("groups", "seq"), None),
        P(("head", "sub"), ("groups", "seq"), None),
        P(("head", "sub"), ("groups", "seq")),
    )
    return jax.shard_map(body, mesh=mesh, in_specs=in_specs, out_specs=out_specs, check_vma=False)
```

```python
import jax
import jax.numpy as jnp
from jax import lax
from jax.sharding import PartitionSpec as P

epsilon = 1e-05
highest = lax.Precision.HIGHEST


def split_three(values):
    top = lax.reduce_precision(values, exponent_bits=8, mantissa_bits=7)
    rest = values - top
    middle = lax.reduce_precision(rest, exponent_bits=8, mantissa_bits=7)
    low = rest - middle
    return jnp.stack([top, middle, low]).astype(jnp.bfloat16)


def join_three(parts):
    wide = parts.astype(jnp.float32)
    return wide[..., 0, :] + wide[..., 1, :] + wide[..., 2, :]


def pack_rows(big, smalls):
    rows = big.astype(jnp.bfloat16).reshape(-1, 128)
    vector = jnp.concatenate([v.reshape(-1) for v in smalls])
    padded = -(-vector.shape[0] // 128) * 128
    vector = jnp.pad(vector, (0, padded - vector.shape[0]))
    extra = split_three(vector).reshape(3 * padded // 128, 128)
    extra = jnp.pad(extra, ((0, (-extra.shape[0]) % 16), (0, 0)))
    return jnp.concatenate([rows, extra], axis=0)


def unpack_rows(received, big_shape, small_shapes):
    big_rows = 1
    for d in big_shape:
        big_rows *= d
    big_rows //= 128
    big = received[:big_rows].reshape(big_shape)
    sizes = []
    for shape in small_shapes:
        size = 1
        for d in shape:
            size *= d
        sizes.append(size)
    padded = -(-sum(sizes) // 128) * 128
    extra = received[big_rows : big_rows + 3 * padded // 128].reshape(3, padded)
    vector = join_three(extra)
    smalls = []
    offset = 0
    for shape, size in zip(small_shapes, sizes):
        smalls.append(vector[offset : offset + size].reshape(shape))
        offset += size
    return big, smalls


def shifted(x, step):
    seq_count = lax.axis_size("seq")
    seq_rank = lax.axis_index("seq")
    if seq_count <= 8:
        moved = []
        for distance in range(1, seq_count):
            if step > 0:
                pairs = [(j, j + distance) for j in range(seq_count - distance)]
            else:
                pairs = [(j + distance, j) for j in range(seq_count - distance)]
            moved.append(lax.ppermute(x, "seq", pairs))
        return moved
    gathered = lax.all_gather(x, "seq", axis=0)
    moved = []
    for distance in range(1, seq_count):
        source = seq_rank + step * distance
        valid = (source >= 0) & (source < seq_count)
        picked = lax.dynamic_index_in_dim(gathered, jnp.clip(source, 0, seq_count - 1), 0, False)
        moved.append(jnp.where(valid, picked, jnp.zeros_like(picked)))
    return moved


def teacher_rows(queries, kv_list, seq_rank):
    local_heads, tok_dev, head_width = queries.shape
    local_groups = kv_list[0].shape[0]
    per_group = local_heads // local_groups
    grouped = queries.reshape(local_groups, per_group, tok_dev, head_width)
    rows = jnp.arange(tok_dev)
    within = rows[:, None] >= rows[None, :]
    block_scores = []
    for distance, block in enumerate(kv_list):
        scores = jnp.einsum(
            "gptd,gkd->gptk", grouped, block[..., :head_width], preferred_element_type=jnp.float32
        )
        scores = scores * head_width ** (-0.5)
        if distance == 0:
            allowed = within
        else:
            allowed = distance <= seq_rank
        block_scores.append(jnp.where(allowed, scores, -jnp.inf))
    highest_score = block_scores[0].max(axis=3, keepdims=True)
    for scores in block_scores[1:]:
        highest_score = jnp.maximum(highest_score, scores.max(axis=3, keepdims=True))
    row_sums = None
    mixed = None
    for scores, block in zip(block_scores, kv_list):
        exponentials = jnp.exp(scores - highest_score)
        part_sum = jnp.sum(exponentials, axis=3, keepdims=True)
        part = jnp.einsum(
            "gptk,gkd->gptd",
            exponentials.astype(jnp.bfloat16),
            block[..., head_width:],
            preferred_element_type=jnp.float32,
        )
        row_sums = part_sum if row_sums is None else row_sums + part_sum
        mixed = part if mixed is None else mixed + part
    mixed = mixed / row_sums
    return mixed.astype(jnp.bfloat16).reshape(local_heads, tok_dev, head_width)


def body(queries, keys_values, student_x, state_maps, decay_logit, skip_gain, init_state):
    local_heads, tok_dev, head_width = student_x.shape
    local_groups = state_maps.shape[0]
    per_group = local_heads // local_groups
    state_size = state_maps.shape[2] // 2
    seq_count = lax.axis_size("seq")
    seq_rank = lax.axis_index("seq")

    kv_earlier = shifted(keys_values, 1)

    log_decay = jax.nn.log_sigmoid(decay_logit)
    cumulative = jnp.cumsum(log_decay, axis=1)
    totals = cumulative[:, -1]
    to_end = jnp.exp(totals[:, None] - cumulative)
    from_start = jnp.exp(cumulative)
    in_maps = state_maps[:, :, :state_size]
    out_maps = state_maps[:, :, state_size:]
    inputs_wide = student_x.astype(jnp.float32)
    in_heads = jnp.repeat(in_maps.astype(jnp.float32), per_group, axis=0)
    out_heads = jnp.repeat(out_maps.astype(jnp.float32), per_group, axis=0)
    weighted_in = in_heads * to_end[..., None]
    end_state = jnp.einsum("hsn,hsp->hnp", weighted_in, inputs_wide, precision=highest)

    state_earlier = shifted(pack_rows(end_state, [totals]), 1)
    ends_earlier = []
    prefix_state = jnp.zeros_like(end_state)
    gap = jnp.zeros_like(totals)
    for distance, received in enumerate(state_earlier, start=1):
        ends, (totals_there,) = unpack_rows(received, end_state.shape, [totals.shape])
        valid = distance <= seq_rank
        totals_there = jnp.where(valid, totals_there, 0.0)
        weight = jnp.where(valid, jnp.exp(gap), 0.0)
        ends_earlier.append(ends)
        prefix_state = prefix_state + weight[:, None, None] * ends.astype(jnp.float32)
        gap = gap + totals_there
    entering = prefix_state + jnp.exp(gap)[:, None, None] * init_state

    intersection = jnp.einsum("gtn,gsn->gts", out_maps, in_maps, preferred_element_type=jnp.float32)
    order_ids = jnp.arange(tok_dev)
    causal = (order_ids[:, None] >= order_ids[None, :])[None]
    gaps = cumulative[:, :, None] - cumulative[:, None, :]
    decayed = jnp.where(causal, jnp.exp(jnp.where(causal, gaps, 0.0)), 0.0)
    mixing = (
        decayed.reshape(local_groups, per_group, tok_dev, tok_dev) * intersection[:, None]
    ).reshape(local_heads, tok_dev, tok_dev)
    local_out = jnp.einsum("hts,hsp->htp", mixing, inputs_wide, precision=highest)

    teacher = teacher_rows(queries, [keys_values] + kv_earlier, seq_rank)
    teacher_wide = teacher.astype(jnp.float32)
    target = teacher_wide * lax.rsqrt(
        jnp.mean(teacher_wide * teacher_wide, axis=2, keepdims=True) + epsilon
    )

    state_out = local_out + from_start[..., None] * jnp.einsum(
        "htn,hnp->htp", out_heads, entering, precision=highest
    )
    outputs = state_out + skip_gain[:, None, None] * inputs_wide
    inverse = lax.rsqrt(jnp.mean(outputs * outputs, axis=2, keepdims=True) + epsilon)
    normed = outputs * inverse
    residual = normed - target
    grad_out = (residual - normed * jnp.mean(residual * normed, axis=2, keepdims=True)) * inverse
    forward_term = jnp.sum(grad_out * state_out, axis=2)
    flow = jnp.einsum(
        "htn,htp->hnp", out_heads * from_start[..., None], grad_out, precision=highest
    )
    closing = jnp.sum(flow * entering, axis=(1, 2))
    if ends_earlier:
        ends_dot_flow = jnp.stack(
            [jnp.sum(ends.astype(jnp.float32) * flow, axis=(1, 2)) for ends in ends_earlier]
        )
    else:
        ends_dot_flow = jnp.zeros((1,) + totals.shape, jnp.float32)

    flow_later = shifted(pack_rows(flow, [totals, closing, ends_dot_flow]), -1)

    local_dx = jnp.einsum("hts,htp->hsp", mixing, grad_out, precision=highest)

    cross = jnp.einsum("htp,hsp->hts", grad_out, inputs_wide, precision=highest)
    paired = decayed * cross
    local_din = jnp.einsum("hts,htn->hsn", paired, out_heads, precision=highest)
    grad_output_maps = jnp.einsum("hts,hsn->htn", paired, in_heads, precision=highest)
    grad_output_maps = grad_output_maps + from_start[..., None] * jnp.einsum(
        "hnp,htp->htn", entering, grad_out, precision=highest
    )

    grad_x_local = local_dx + skip_gain[:, None, None] * grad_out
    local_terms = forward_term - jnp.sum(inputs_wide * local_dx, axis=2)
    local_tail = lax.cumsum(local_terms, axis=1, reverse=True)
    maps_in_local = local_din.reshape(local_groups, per_group, tok_dev, state_size).sum(axis=1)
    maps_out = grad_output_maps.reshape(local_groups, per_group, tok_dev, state_size).sum(axis=1)

    incoming = jnp.zeros_like(flow)
    later_sum = jnp.zeros_like(totals)
    gap = jnp.zeros_like(totals)
    through = []
    for distance, received in enumerate(flow_later, start=1):
        flows, (totals_there, closing_there, dots) = unpack_rows(
            received, flow.shape, [totals.shape, closing.shape, ends_dot_flow.shape]
        )
        valid = seq_rank + distance < seq_count
        totals_there = jnp.where(valid, totals_there, 0.0)
        weight = jnp.where(valid, jnp.exp(gap), 0.0)
        incoming = incoming + weight[:, None, None] * flows.astype(jnp.float32)
        later_sum = later_sum + jnp.where(valid, closing_there, 0.0)
        for early in range(1, distance):
            pair_gap = gap - through[early - 1]
            later_sum = later_sum - jnp.where(
                valid, jnp.exp(jnp.where(valid, pair_gap, 0.0)) * dots[distance - early - 1], 0.0
            )
        gap = gap + totals_there
        through.append(gap)

    state_extra = jnp.einsum("hsn,hnp->hsp", weighted_in, incoming, precision=highest)
    maps_extra = jnp.einsum("hnp,hsp->hsn", incoming, inputs_wide, precision=highest)
    grad_x = grad_x_local + state_extra
    extra_terms = jnp.sum(weighted_in * maps_extra, axis=2)
    upper = (order_ids[:, None] <= order_ids[None, :]).astype(jnp.float32)
    extra_tail = jnp.einsum("hu,su->hs", extra_terms, upper, precision=highest)
    grad_log_decay = later_sum[:, None] + local_tail - extra_tail
    maps_in = maps_in_local + (maps_extra * to_end[..., None]).reshape(
        local_groups, per_group, tok_dev, state_size
    ).sum(axis=1)
    grad_maps = jnp.concatenate([maps_in, maps_out], axis=2)
    return (grad_x.astype(jnp.bfloat16), grad_maps.astype(jnp.bfloat16), grad_log_decay)


def solution(mesh):
    in_specs = (
        P(("head", "sub"), ("groups", "seq"), None),
        P(("head", "sub"), ("groups", "seq"), None),
        P(("head", "sub"), ("groups", "seq"), None),
        P(("head", "sub"), ("groups", "seq"), None),
        P(("head", "sub"), ("groups", "seq")),
        P(("head", "sub")),
        P(("groups", "head", "sub"), None, None),
    )
    out_specs = (
        P(("head", "sub"), ("groups", "seq"), None),
        P(("head", "sub"), ("groups", "seq"), None),
        P(("head", "sub"), ("groups", "seq")),
    )
    return jax.shard_map(body, mesh=mesh, in_specs=in_specs, out_specs=out_specs, check_vma=False)
```

```python
import jax
import jax.numpy as jnp
from jax import lax
from jax.sharding import PartitionSpec as P

epsilon = 1e-05
highest = lax.Precision.HIGHEST


def split_three(values):
    top = lax.reduce_precision(values, exponent_bits=8, mantissa_bits=7)
    rest = values - top
    middle = lax.reduce_precision(rest, exponent_bits=8, mantissa_bits=7)
    low = rest - middle
    return jnp.stack([top, middle, low]).astype(jnp.bfloat16)


def join_three(parts):
    wide = parts.astype(jnp.float32)
    return wide[..., 0, :] + wide[..., 1, :] + wide[..., 2, :]


def pack_rows(big, smalls):
    rows = big.astype(jnp.bfloat16).reshape(-1, 128)
    vector = jnp.concatenate([v.reshape(-1) for v in smalls])
    padded = -(-vector.shape[0] // 128) * 128
    vector = jnp.pad(vector, (0, padded - vector.shape[0]))
    extra = split_three(vector).reshape(3 * padded // 128, 128)
    extra = jnp.pad(extra, ((0, (-extra.shape[0]) % 16), (0, 0)))
    return jnp.concatenate([rows, extra], axis=0)


def unpack_rows(received, big_shape, small_shapes):
    big_rows = 1
    for d in big_shape:
        big_rows *= d
    big_rows //= 128
    big = received[:big_rows].reshape(big_shape)
    sizes = []
    for shape in small_shapes:
        size = 1
        for d in shape:
            size *= d
        sizes.append(size)
    padded = -(-sum(sizes) // 128) * 128
    extra = received[big_rows : big_rows + 3 * padded // 128].reshape(3, padded)
    vector = join_three(extra)
    smalls = []
    offset = 0
    for shape, size in zip(small_shapes, sizes):
        smalls.append(vector[offset : offset + size].reshape(shape))
        offset += size
    return big, smalls


def shifted(x, step):
    seq_count = lax.axis_size("seq")
    seq_rank = lax.axis_index("seq")
    if seq_count <= 8:
        moved = []
        for distance in range(1, seq_count):
            if step > 0:
                pairs = [(j, j + distance) for j in range(seq_count - distance)]
            else:
                pairs = [(j + distance, j) for j in range(seq_count - distance)]
            moved.append(lax.ppermute(x, "seq", pairs))
        return moved
    gathered = lax.all_gather(x, "seq", axis=0)
    moved = []
    for distance in range(1, seq_count):
        source = seq_rank + step * distance
        valid = (source >= 0) & (source < seq_count)
        picked = lax.dynamic_index_in_dim(gathered, jnp.clip(source, 0, seq_count - 1), 0, False)
        moved.append(jnp.where(valid, picked, jnp.zeros_like(picked)))
    return moved


def teacher_rows(queries, kv_list, seq_rank):
    local_heads, tok_dev, head_width = queries.shape
    local_groups = kv_list[0].shape[0]
    per_group = local_heads // local_groups
    grouped = queries.reshape(local_groups, per_group, tok_dev, head_width)
    rows = jnp.arange(tok_dev)
    within = rows[:, None] >= rows[None, :]
    block_scores = []
    for distance, block in enumerate(kv_list):
        scores = jnp.einsum(
            "gptd,gkd->gptk", grouped, block[..., :head_width], preferred_element_type=jnp.float32
        )
        scores = scores * head_width ** (-0.5)
        if distance == 0:
            allowed = within
        else:
            allowed = distance <= seq_rank
        block_scores.append(jnp.where(allowed, scores, -jnp.inf))
    highest_score = block_scores[0].max(axis=3, keepdims=True)
    for scores in block_scores[1:]:
        highest_score = jnp.maximum(highest_score, scores.max(axis=3, keepdims=True))
    row_sums = None
    mixed = None
    for scores, block in zip(block_scores, kv_list):
        exponentials = jnp.exp(scores - highest_score)
        part_sum = jnp.sum(exponentials, axis=3, keepdims=True)
        part = jnp.einsum(
            "gptk,gkd->gptd",
            exponentials.astype(jnp.bfloat16),
            block[..., head_width:],
            preferred_element_type=jnp.float32,
        )
        row_sums = part_sum if row_sums is None else row_sums + part_sum
        mixed = part if mixed is None else mixed + part
    mixed = mixed / row_sums
    return mixed.astype(jnp.bfloat16).reshape(local_heads, tok_dev, head_width)


def body(queries, keys_values, student_x, state_maps, decay_logit, skip_gain, init_state):
    local_heads, tok_dev, head_width = student_x.shape
    local_groups = state_maps.shape[0]
    per_group = local_heads // local_groups
    state_size = state_maps.shape[2] // 2
    seq_count = lax.axis_size("seq")
    seq_rank = lax.axis_index("seq")

    kv_earlier = shifted(keys_values, 1)

    log_decay = jax.nn.log_sigmoid(decay_logit)
    cumulative = jnp.cumsum(log_decay, axis=1)
    totals = cumulative[:, -1]
    to_end = jnp.exp(totals[:, None] - cumulative)
    from_start = jnp.exp(cumulative)
    in_maps = state_maps[:, :, :state_size]
    out_maps = state_maps[:, :, state_size:]
    inputs_wide = student_x.astype(jnp.float32)
    in_heads = jnp.repeat(in_maps.astype(jnp.float32), per_group, axis=0)
    out_heads = jnp.repeat(out_maps.astype(jnp.float32), per_group, axis=0)
    weighted_in = in_heads * to_end[..., None]
    end_state = jnp.einsum("hsn,hsp->hnp", weighted_in, inputs_wide, precision=highest)

    state_earlier = shifted(pack_rows(end_state, [totals]), 1)
    prefix_state = jnp.zeros_like(end_state)
    gap = jnp.zeros_like(totals)
    for distance, received in enumerate(state_earlier, start=1):
        ends, (totals_there,) = unpack_rows(received, end_state.shape, [totals.shape])
        valid = distance <= seq_rank
        totals_there = jnp.where(valid, totals_there, 0.0)
        weight = jnp.where(valid, jnp.exp(gap), 0.0)
        prefix_state = prefix_state + weight[:, None, None] * ends.astype(jnp.float32)
        gap = gap + totals_there
    entering = prefix_state + jnp.exp(gap)[:, None, None] * init_state

    intersection = jnp.einsum("gtn,gsn->gts", out_maps, in_maps, preferred_element_type=jnp.float32)
    order_ids = jnp.arange(tok_dev)
    causal = (order_ids[:, None] >= order_ids[None, :])[None]
    gaps = cumulative[:, :, None] - cumulative[:, None, :]
    decayed = jnp.where(causal, jnp.exp(jnp.where(causal, gaps, 0.0)), 0.0)
    mixing = (
        decayed.reshape(local_groups, per_group, tok_dev, tok_dev) * intersection[:, None]
    ).reshape(local_heads, tok_dev, tok_dev)
    local_out = jnp.einsum("hts,hsp->htp", mixing, inputs_wide, precision=highest)

    teacher = teacher_rows(queries, [keys_values] + kv_earlier, seq_rank)
    teacher_wide = teacher.astype(jnp.float32)
    target = teacher_wide * lax.rsqrt(
        jnp.mean(teacher_wide * teacher_wide, axis=2, keepdims=True) + epsilon
    )

    state_out = local_out + from_start[..., None] * jnp.einsum(
        "htn,hnp->htp", out_heads, entering, precision=highest
    )
    outputs = state_out + skip_gain[:, None, None] * inputs_wide
    inverse = lax.rsqrt(jnp.mean(outputs * outputs, axis=2, keepdims=True) + epsilon)
    normed = outputs * inverse
    residual = normed - target
    grad_out = (residual - normed * jnp.mean(residual * normed, axis=2, keepdims=True)) * inverse
    forward_term = jnp.sum(grad_out * state_out, axis=2)
    flow = jnp.einsum(
        "htn,htp->hnp", out_heads * from_start[..., None], grad_out, precision=highest
    )
    flow_later = shifted(pack_rows(flow, [totals]), -1)

    local_dx = jnp.einsum("hts,htp->hsp", mixing, grad_out, precision=highest)

    cross = jnp.einsum("htp,hsp->hts", grad_out, inputs_wide, precision=highest)
    paired = decayed * cross
    local_din = jnp.einsum("hts,htn->hsn", paired, out_heads, precision=highest)
    grad_output_maps = jnp.einsum("hts,hsn->htn", paired, in_heads, precision=highest)
    grad_output_maps = grad_output_maps + from_start[..., None] * jnp.einsum(
        "hnp,htp->htn", entering, grad_out, precision=highest
    )

    incoming = jnp.zeros_like(flow)
    gap = jnp.zeros_like(totals)
    for distance, received in enumerate(flow_later, start=1):
        flows, (totals_there,) = unpack_rows(received, flow.shape, [totals.shape])
        valid = seq_rank + distance < seq_count
        totals_there = jnp.where(valid, totals_there, 0.0)
        weight = jnp.where(valid, jnp.exp(gap), 0.0)
        incoming = incoming + weight[:, None, None] * flows.astype(jnp.float32)
        gap = gap + totals_there
    leaving = jnp.exp(totals)[:, None, None] * entering + end_state
    later_sum = jnp.sum(incoming * leaving, axis=(1, 2))

    state_dx = local_dx + jnp.einsum("hsn,hnp->hsp", weighted_in, incoming, precision=highest)
    terms = forward_term - jnp.sum(inputs_wide * state_dx, axis=2)
    grad_log_decay = later_sum[:, None] + lax.cumsum(terms, axis=1, reverse=True)
    grad_input_maps = (
        local_din
        + jnp.einsum("hnp,hsp->hsn", incoming, inputs_wide, precision=highest) * to_end[..., None]
    )
    grad_maps = jnp.concatenate([grad_input_maps, grad_output_maps], axis=2)
    grad_maps = grad_maps.reshape(local_groups, per_group, tok_dev, 2 * state_size).sum(axis=1)
    grad_x = state_dx + skip_gain[:, None, None] * grad_out
    return (grad_x.astype(jnp.bfloat16), grad_maps.astype(jnp.bfloat16), grad_log_decay)


def solution(mesh):
    in_specs = (
        P(("head", "sub"), ("groups", "seq"), None),
        P(("head", "sub"), ("groups", "seq"), None),
        P(("head", "sub"), ("groups", "seq"), None),
        P(("head", "sub"), ("groups", "seq"), None),
        P(("head", "sub"), ("groups", "seq")),
        P(("head", "sub")),
        P(("groups", "head", "sub"), None, None),
    )
    out_specs = (
        P(("head", "sub"), ("groups", "seq"), None),
        P(("head", "sub"), ("groups", "seq"), None),
        P(("head", "sub"), ("groups", "seq")),
    )
    return jax.shard_map(body, mesh=mesh, in_specs=in_specs, out_specs=out_specs, check_vma=False)
```

```python
import jax
import jax.numpy as jnp
from jax import lax
from jax.sharding import PartitionSpec as P

epsilon = 1e-05
highest = lax.Precision.HIGHEST


def split_three(values):
    top = lax.reduce_precision(values, exponent_bits=8, mantissa_bits=7)
    rest = values - top
    middle = lax.reduce_precision(rest, exponent_bits=8, mantissa_bits=7)
    low = rest - middle
    return jnp.stack([top, middle, low]).astype(jnp.bfloat16)


def join_three(parts):
    wide = parts.astype(jnp.float32)
    return wide[..., 0, :] + wide[..., 1, :] + wide[..., 2, :]


def pack_rows(big, smalls):
    rows = big.astype(jnp.bfloat16).reshape(-1, 128)
    vector = jnp.concatenate([v.reshape(-1) for v in smalls])
    padded = -(-vector.shape[0] // 128) * 128
    vector = jnp.pad(vector, (0, padded - vector.shape[0]))
    extra = split_three(vector).reshape(3 * padded // 128, 128)
    extra = jnp.pad(extra, ((0, (-extra.shape[0]) % 16), (0, 0)))
    return jnp.concatenate([rows, extra], axis=0)


def unpack_rows(received, big_shape, small_shapes):
    big_rows = 1
    for d in big_shape:
        big_rows *= d
    big_rows //= 128
    big = received[:big_rows].reshape(big_shape)
    sizes = []
    for shape in small_shapes:
        size = 1
        for d in shape:
            size *= d
        sizes.append(size)
    padded = -(-sum(sizes) // 128) * 128
    extra = received[big_rows : big_rows + 3 * padded // 128].reshape(3, padded)
    vector = join_three(extra)
    smalls = []
    offset = 0
    for shape, size in zip(small_shapes, sizes):
        smalls.append(vector[offset : offset + size].reshape(shape))
        offset += size
    return big, smalls


def shifted(x, step):
    seq_count = lax.axis_size("seq")
    seq_rank = lax.axis_index("seq")
    if seq_count <= 8:
        moved = []
        for distance in range(1, seq_count):
            if step > 0:
                pairs = [(j, j + distance) for j in range(seq_count - distance)]
            else:
                pairs = [(j + distance, j) for j in range(seq_count - distance)]
            moved.append(lax.ppermute(x, "seq", pairs))
        return moved
    gathered = lax.all_gather(x, "seq", axis=0)
    moved = []
    for distance in range(1, seq_count):
        source = seq_rank + step * distance
        valid = (source >= 0) & (source < seq_count)
        picked = lax.dynamic_index_in_dim(gathered, jnp.clip(source, 0, seq_count - 1), 0, False)
        moved.append(jnp.where(valid, picked, jnp.zeros_like(picked)))
    return moved


def teacher_rows(queries, kv_list, seq_rank):
    local_heads, tok_dev, head_width = queries.shape
    local_groups = kv_list[0].shape[0]
    per_group = local_heads // local_groups
    grouped = queries.reshape(local_groups, per_group, tok_dev, head_width)
    rows = jnp.arange(tok_dev)
    within = rows[:, None] >= rows[None, :]
    block_scores = []
    for distance, block in enumerate(kv_list):
        scores = jnp.einsum(
            "gptd,gkd->gptk", grouped, block[..., :head_width], preferred_element_type=jnp.float32
        )
        scores = scores * head_width ** (-0.5)
        if distance == 0:
            allowed = within
        else:
            allowed = distance <= seq_rank
        block_scores.append(jnp.where(allowed, scores, -jnp.inf))
    highest_score = block_scores[0].max(axis=3, keepdims=True)
    for scores in block_scores[1:]:
        highest_score = jnp.maximum(highest_score, scores.max(axis=3, keepdims=True))
    row_sums = None
    mixed = None
    for scores, block in zip(block_scores, kv_list):
        exponentials = jnp.exp(scores - highest_score)
        part_sum = jnp.sum(exponentials, axis=3, keepdims=True)
        part = jnp.einsum(
            "gptk,gkd->gptd",
            exponentials.astype(jnp.bfloat16),
            block[..., head_width:],
            preferred_element_type=jnp.float32,
        )
        row_sums = part_sum if row_sums is None else row_sums + part_sum
        mixed = part if mixed is None else mixed + part
    mixed = mixed / row_sums
    return mixed.astype(jnp.bfloat16).reshape(local_heads, tok_dev, head_width)


def body(queries, keys_values, student_x, state_maps, decay_logit, skip_gain, init_state):
    local_heads, tok_dev, head_width = student_x.shape
    local_groups = state_maps.shape[0]
    per_group = local_heads // local_groups
    state_size = state_maps.shape[2] // 2
    seq_count = lax.axis_size("seq")
    seq_rank = lax.axis_index("seq")

    kv_earlier = shifted(keys_values, 1)

    log_decay = jax.nn.log_sigmoid(decay_logit)
    cumulative = jnp.cumsum(log_decay, axis=1)
    totals = cumulative[:, -1]
    to_end = jnp.exp(totals[:, None] - cumulative)
    from_start = jnp.exp(cumulative)
    in_maps = state_maps[:, :, :state_size]
    out_maps = state_maps[:, :, state_size:]
    inputs_wide = student_x.astype(jnp.float32)
    in_heads = jnp.repeat(in_maps.astype(jnp.float32), per_group, axis=0)
    out_heads = jnp.repeat(out_maps.astype(jnp.float32), per_group, axis=0)
    weighted_in = in_heads * to_end[..., None]
    end_state = jnp.einsum("hsn,hsp->hnp", weighted_in, inputs_wide, precision=highest)

    state_earlier = shifted(pack_rows(end_state, [totals]), 1)
    prefix_state = jnp.zeros_like(end_state)
    gap = jnp.zeros_like(totals)
    for distance, received in enumerate(state_earlier, start=1):
        ends, (totals_there,) = unpack_rows(received, end_state.shape, [totals.shape])
        valid = distance <= seq_rank
        totals_there = jnp.where(valid, totals_there, 0.0)
        weight = jnp.where(valid, jnp.exp(gap), 0.0)
        prefix_state = prefix_state + weight[:, None, None] * ends.astype(jnp.float32)
        gap = gap + totals_there
    entering = prefix_state + jnp.exp(gap)[:, None, None] * init_state

    intersection = jnp.einsum("gtn,gsn->gts", out_maps, in_maps, preferred_element_type=jnp.float32)
    order_ids = jnp.arange(tok_dev)
    causal = (order_ids[:, None] >= order_ids[None, :])[None]
    gaps = cumulative[:, :, None] - cumulative[:, None, :]
    decayed = jnp.where(causal, jnp.exp(jnp.where(causal, gaps, 0.0)), 0.0)
    mixing = (
        decayed.reshape(local_groups, per_group, tok_dev, tok_dev) * intersection[:, None]
    ).reshape(local_heads, tok_dev, tok_dev)
    local_out = jnp.einsum("hts,hsp->htp", mixing, inputs_wide, precision=highest)

    teacher = teacher_rows(queries, [keys_values] + kv_earlier, seq_rank)
    teacher_wide = teacher.astype(jnp.float32)
    target = teacher_wide * lax.rsqrt(
        jnp.mean(teacher_wide * teacher_wide, axis=2, keepdims=True) + epsilon
    )

    state_out = local_out + from_start[..., None] * jnp.einsum(
        "htn,hnp->htp", out_heads, entering, precision=highest
    )
    outputs = state_out + skip_gain[:, None, None] * inputs_wide
    inverse = lax.rsqrt(jnp.mean(outputs * outputs, axis=2, keepdims=True) + epsilon)
    normed = outputs * inverse
    residual = normed - target
    grad_out = (residual - normed * jnp.mean(residual * normed, axis=2, keepdims=True)) * inverse
    forward_term = jnp.sum(grad_out * state_out, axis=2)
    flow = jnp.einsum(
        "htn,htp->hnp", out_heads * from_start[..., None], grad_out, precision=highest
    )
    if seq_count == 4:
        payload = pack_rows(flow, [totals])
        next_one = lax.ppermute(payload, "seq", [(3, 2), (2, 1)])
        next_two = lax.ppermute(payload, "seq", [(3, 1)])
    else:
        flow_later = shifted(pack_rows(flow, [totals]), -1)

    local_dx = jnp.einsum("hts,htp->hsp", mixing, grad_out, precision=highest)

    cross = jnp.einsum("htp,hsp->hts", grad_out, inputs_wide, precision=highest)
    paired = decayed * cross
    local_din = jnp.einsum("hts,htn->hsn", paired, out_heads, precision=highest)
    grad_output_maps = jnp.einsum("hts,hsn->htn", paired, in_heads, precision=highest)
    grad_output_maps = grad_output_maps + from_start[..., None] * jnp.einsum(
        "hnp,htp->htn", entering, grad_out, precision=highest
    )

    if seq_count == 4:
        flow_one, (totals_one,) = unpack_rows(next_one, flow.shape, [totals.shape])
        flow_two, _ = unpack_rows(next_two, flow.shape, [totals.shape])
        has_one = (seq_rank == 1) | (seq_rank == 2)
        has_two = seq_rank == 1
        incoming = jnp.where(has_one, flow_one.astype(jnp.float32), 0.0) + jnp.where(
            has_two, jnp.exp(totals_one)[:, None, None] * flow_two.astype(jnp.float32), 0.0
        )
        handoff = flow + jnp.exp(totals)[:, None, None] * incoming
        first_incoming = lax.ppermute(handoff.astype(jnp.bfloat16), "seq", [(1, 0)])
        incoming = jnp.where(seq_rank == 0, first_incoming.astype(jnp.float32), incoming)
    else:
        incoming = jnp.zeros_like(flow)
        gap = jnp.zeros_like(totals)
        for distance, received in enumerate(flow_later, start=1):
            flows, (totals_there,) = unpack_rows(received, flow.shape, [totals.shape])
            valid = seq_rank + distance < seq_count
            totals_there = jnp.where(valid, totals_there, 0.0)
            weight = jnp.where(valid, jnp.exp(gap), 0.0)
            incoming = incoming + weight[:, None, None] * flows.astype(jnp.float32)
            gap = gap + totals_there
    leaving = jnp.exp(totals)[:, None, None] * entering + end_state
    later_sum = jnp.sum(incoming * leaving, axis=(1, 2))

    state_dx = local_dx + jnp.einsum("hsn,hnp->hsp", weighted_in, incoming, precision=highest)
    terms = forward_term - jnp.sum(inputs_wide * state_dx, axis=2)
    grad_log_decay = later_sum[:, None] + lax.cumsum(terms, axis=1, reverse=True)
    grad_input_maps = (
        local_din
        + jnp.einsum("hnp,hsp->hsn", incoming, inputs_wide, precision=highest) * to_end[..., None]
    )
    grad_maps = jnp.concatenate([grad_input_maps, grad_output_maps], axis=2)
    grad_maps = grad_maps.reshape(local_groups, per_group, tok_dev, 2 * state_size).sum(axis=1)
    grad_x = state_dx + skip_gain[:, None, None] * grad_out
    return (grad_x.astype(jnp.bfloat16), grad_maps.astype(jnp.bfloat16), grad_log_decay)


def solution(mesh):
    in_specs = (
        P(("head", "sub"), ("groups", "seq"), None),
        P(("head", "sub"), ("groups", "seq"), None),
        P(("head", "sub"), ("groups", "seq"), None),
        P(("head", "sub"), ("groups", "seq"), None),
        P(("head", "sub"), ("groups", "seq")),
        P(("head", "sub")),
        P(("groups", "head", "sub"), None, None),
    )
    out_specs = (
        P(("head", "sub"), ("groups", "seq"), None),
        P(("head", "sub"), ("groups", "seq"), None),
        P(("head", "sub"), ("groups", "seq")),
    )
    return jax.shard_map(body, mesh=mesh, in_specs=in_specs, out_specs=out_specs, check_vma=False)
```

```python
import jax
import jax.numpy as jnp
from jax import lax
from jax.sharding import PartitionSpec as P

epsilon = 1e-05
highest = lax.Precision.HIGHEST


def split_three(values):
    top = lax.reduce_precision(values, exponent_bits=8, mantissa_bits=7)
    rest = values - top
    middle = lax.reduce_precision(rest, exponent_bits=8, mantissa_bits=7)
    low = rest - middle
    return jnp.stack([top, middle, low]).astype(jnp.bfloat16)


def join_three(parts):
    wide = parts.astype(jnp.float32)
    return wide[..., 0, :] + wide[..., 1, :] + wide[..., 2, :]


def pack_rows(big, smalls):
    rows = big.astype(jnp.bfloat16).reshape(-1, 128)
    vector = jnp.concatenate([v.reshape(-1) for v in smalls])
    padded = -(-vector.shape[0] // 128) * 128
    vector = jnp.pad(vector, (0, padded - vector.shape[0]))
    extra = split_three(vector).reshape(3 * padded // 128, 128)
    extra = jnp.pad(extra, ((0, (-extra.shape[0]) % 16), (0, 0)))
    return jnp.concatenate([rows, extra], axis=0)


def unpack_rows(received, big_shape, small_shapes):
    big_rows = 1
    for d in big_shape:
        big_rows *= d
    big_rows //= 128
    big = received[:big_rows].reshape(big_shape)
    sizes = []
    for shape in small_shapes:
        size = 1
        for d in shape:
            size *= d
        sizes.append(size)
    padded = -(-sum(sizes) // 128) * 128
    extra = received[big_rows : big_rows + 3 * padded // 128].reshape(3, padded)
    vector = join_three(extra)
    smalls = []
    offset = 0
    for shape, size in zip(small_shapes, sizes):
        smalls.append(vector[offset : offset + size].reshape(shape))
        offset += size
    return big, smalls


def shifted(x, step):
    seq_count = lax.axis_size("seq")
    seq_rank = lax.axis_index("seq")
    if seq_count <= 8:
        moved = []
        for distance in range(1, seq_count):
            if step > 0:
                pairs = [(j, j + distance) for j in range(seq_count - distance)]
            else:
                pairs = [(j + distance, j) for j in range(seq_count - distance)]
            moved.append(lax.ppermute(x, "seq", pairs))
        return moved
    gathered = lax.all_gather(x, "seq", axis=0)
    moved = []
    for distance in range(1, seq_count):
        source = seq_rank + step * distance
        valid = (source >= 0) & (source < seq_count)
        picked = lax.dynamic_index_in_dim(gathered, jnp.clip(source, 0, seq_count - 1), 0, False)
        moved.append(jnp.where(valid, picked, jnp.zeros_like(picked)))
    return moved


def teacher_rows(queries, kv_list, seq_rank):
    local_heads, tok_dev, head_width = queries.shape
    local_groups = kv_list[0].shape[0]
    per_group = local_heads // local_groups
    grouped = queries.reshape(local_groups, per_group, tok_dev, head_width)
    rows = jnp.arange(tok_dev)
    within = rows[:, None] >= rows[None, :]
    block_scores = []
    for distance, block in enumerate(kv_list):
        scores = jnp.einsum(
            "gptd,gkd->gptk", grouped, block[..., :head_width], preferred_element_type=jnp.float32
        )
        scores = scores * head_width ** (-0.5)
        if distance == 0:
            allowed = within
        else:
            allowed = distance <= seq_rank
        block_scores.append(jnp.where(allowed, scores, -jnp.inf))
    highest_score = block_scores[0].max(axis=3, keepdims=True)
    for scores in block_scores[1:]:
        highest_score = jnp.maximum(highest_score, scores.max(axis=3, keepdims=True))
    row_sums = None
    mixed = None
    for scores, block in zip(block_scores, kv_list):
        exponentials = jnp.exp(scores - highest_score)
        part_sum = jnp.sum(exponentials, axis=3, keepdims=True)
        part = jnp.einsum(
            "gptk,gkd->gptd",
            exponentials.astype(jnp.bfloat16),
            block[..., head_width:],
            preferred_element_type=jnp.float32,
        )
        row_sums = part_sum if row_sums is None else row_sums + part_sum
        mixed = part if mixed is None else mixed + part
    mixed = mixed / row_sums
    return mixed.astype(jnp.bfloat16).reshape(local_heads, tok_dev, head_width)


def body(queries, keys_values, student_x, state_maps, decay_logit, skip_gain, init_state):
    local_heads, tok_dev, head_width = student_x.shape
    local_groups = state_maps.shape[0]
    per_group = local_heads // local_groups
    state_size = state_maps.shape[2] // 2
    seq_count = lax.axis_size("seq")
    seq_rank = lax.axis_index("seq")

    log_decay = jax.nn.log_sigmoid(decay_logit)
    cumulative = jnp.cumsum(log_decay, axis=1)
    totals = cumulative[:, -1]
    to_end = jnp.exp(totals[:, None] - cumulative)
    from_start = jnp.exp(cumulative)
    in_maps = state_maps[:, :, :state_size]
    out_maps = state_maps[:, :, state_size:]
    inputs_wide = student_x.astype(jnp.float32)
    in_heads = jnp.repeat(in_maps.astype(jnp.float32), per_group, axis=0)
    out_heads = jnp.repeat(out_maps.astype(jnp.float32), per_group, axis=0)
    weighted_in = in_heads * to_end[..., None]
    end_state = jnp.einsum("hsn,hsp->hnp", weighted_in, inputs_wide, precision=highest)

    kv_ready, state_ready = lax.optimization_barrier((keys_values, pack_rows(end_state, [totals])))
    kv_earlier = shifted(kv_ready, 1)
    state_earlier = shifted(state_ready, 1)
    ends_earlier = []
    prefix_state = jnp.zeros_like(end_state)
    gap = jnp.zeros_like(totals)
    for distance, received in enumerate(state_earlier, start=1):
        ends, (totals_there,) = unpack_rows(received, end_state.shape, [totals.shape])
        valid = distance <= seq_rank
        totals_there = jnp.where(valid, totals_there, 0.0)
        weight = jnp.where(valid, jnp.exp(gap), 0.0)
        ends_earlier.append(ends)
        prefix_state = prefix_state + weight[:, None, None] * ends.astype(jnp.float32)
        gap = gap + totals_there
    entering = prefix_state + jnp.exp(gap)[:, None, None] * init_state

    intersection = jnp.einsum("gtn,gsn->gts", out_maps, in_maps, preferred_element_type=jnp.float32)
    order_ids = jnp.arange(tok_dev)
    causal = (order_ids[:, None] >= order_ids[None, :])[None]
    gaps = cumulative[:, :, None] - cumulative[:, None, :]
    decayed = jnp.where(causal, jnp.exp(jnp.where(causal, gaps, 0.0)), 0.0)
    mixing = (
        decayed.reshape(local_groups, per_group, tok_dev, tok_dev) * intersection[:, None]
    ).reshape(local_heads, tok_dev, tok_dev)
    local_out = jnp.einsum("hts,hsp->htp", mixing, inputs_wide, precision=highest)

    teacher = teacher_rows(queries, [keys_values] + kv_earlier, seq_rank)
    teacher_wide = teacher.astype(jnp.float32)
    target = teacher_wide * lax.rsqrt(
        jnp.mean(teacher_wide * teacher_wide, axis=2, keepdims=True) + epsilon
    )

    state_out = local_out + from_start[..., None] * jnp.einsum(
        "htn,hnp->htp", out_heads, entering, precision=highest
    )
    outputs = state_out + skip_gain[:, None, None] * inputs_wide
    inverse = lax.rsqrt(jnp.mean(outputs * outputs, axis=2, keepdims=True) + epsilon)
    normed = outputs * inverse
    residual = normed - target
    grad_out = (residual - normed * jnp.mean(residual * normed, axis=2, keepdims=True)) * inverse
    forward_term = jnp.sum(grad_out * state_out, axis=2)
    flow = jnp.einsum(
        "htn,htp->hnp", out_heads * from_start[..., None], grad_out, precision=highest
    )
    closing = jnp.sum(flow * entering, axis=(1, 2))
    if ends_earlier:
        ends_dot_flow = jnp.stack(
            [jnp.sum(ends.astype(jnp.float32) * flow, axis=(1, 2)) for ends in ends_earlier]
        )
    else:
        ends_dot_flow = jnp.zeros((1,) + totals.shape, jnp.float32)

    flow_later = shifted(pack_rows(flow, [totals, closing, ends_dot_flow]), -1)

    local_dx = jnp.einsum("hts,htp->hsp", mixing, grad_out, precision=highest)

    cross = jnp.einsum("htp,hsp->hts", grad_out, inputs_wide, precision=highest)
    paired = decayed * cross
    local_din = jnp.einsum("hts,htn->hsn", paired, out_heads, precision=highest)
    grad_output_maps = jnp.einsum("hts,hsn->htn", paired, in_heads, precision=highest)
    grad_output_maps = grad_output_maps + from_start[..., None] * jnp.einsum(
        "hnp,htp->htn", entering, grad_out, precision=highest
    )

    incoming = jnp.zeros_like(flow)
    later_sum = jnp.zeros_like(totals)
    gap = jnp.zeros_like(totals)
    through = []
    dots_there = []
    for distance, received in enumerate(flow_later, start=1):
        flows, (totals_there, closing_there, dots) = unpack_rows(
            received, flow.shape, [totals.shape, closing.shape, ends_dot_flow.shape]
        )
        valid = seq_rank + distance < seq_count
        totals_there = jnp.where(valid, totals_there, 0.0)
        weight = jnp.where(valid, jnp.exp(gap), 0.0)
        incoming = incoming + weight[:, None, None] * flows.astype(jnp.float32)
        later_sum = later_sum + jnp.where(valid, closing_there, 0.0)
        for early in range(1, distance):
            pair_gap = gap - through[early - 1]
            later_sum = later_sum - jnp.where(
                valid, jnp.exp(jnp.where(valid, pair_gap, 0.0)) * dots[distance - early - 1], 0.0
            )
        gap = gap + totals_there
        through.append(gap)

    state_dx = local_dx + jnp.einsum("hsn,hnp->hsp", weighted_in, incoming, precision=highest)
    terms = forward_term - jnp.sum(inputs_wide * state_dx, axis=2)
    grad_log_decay = later_sum[:, None] + lax.cumsum(terms, axis=1, reverse=True)
    grad_input_maps = (
        local_din
        + jnp.einsum("hnp,hsp->hsn", incoming, inputs_wide, precision=highest) * to_end[..., None]
    )
    grad_maps = jnp.concatenate([grad_input_maps, grad_output_maps], axis=2)
    grad_maps = grad_maps.reshape(local_groups, per_group, tok_dev, 2 * state_size).sum(axis=1)
    grad_x = state_dx + skip_gain[:, None, None] * grad_out
    return (grad_x.astype(jnp.bfloat16), grad_maps.astype(jnp.bfloat16), grad_log_decay)


def solution(mesh):
    in_specs = (
        P(("head", "sub"), ("groups", "seq"), None),
        P(("head", "sub"), ("groups", "seq"), None),
        P(("head", "sub"), ("groups", "seq"), None),
        P(("head", "sub"), ("groups", "seq"), None),
        P(("head", "sub"), ("groups", "seq")),
        P(("head", "sub")),
        P(("groups", "head", "sub"), None, None),
    )
    out_specs = (
        P(("head", "sub"), ("groups", "seq"), None),
        P(("head", "sub"), ("groups", "seq"), None),
        P(("head", "sub"), ("groups", "seq")),
    )
    return jax.shard_map(body, mesh=mesh, in_specs=in_specs, out_specs=out_specs, check_vma=False)
```

```python
import jax
import jax.numpy as jnp
from jax import lax
from jax.sharding import PartitionSpec as P

epsilon = 1e-05
highest = lax.Precision.HIGHEST


def split_three(values):
    top = lax.reduce_precision(values, exponent_bits=8, mantissa_bits=7)
    rest = values - top
    middle = lax.reduce_precision(rest, exponent_bits=8, mantissa_bits=7)
    low = rest - middle
    return jnp.stack([top, middle, low]).astype(jnp.bfloat16)


def join_three(parts):
    wide = parts.astype(jnp.float32)
    return wide[..., 0, :] + wide[..., 1, :] + wide[..., 2, :]


def pack_rows(big, smalls):
    rows = big.astype(jnp.bfloat16).reshape(-1, 128)
    vector = jnp.concatenate([v.reshape(-1) for v in smalls])
    padded = -(-vector.shape[0] // 128) * 128
    vector = jnp.pad(vector, (0, padded - vector.shape[0]))
    extra = split_three(vector).reshape(3 * padded // 128, 128)
    extra = jnp.pad(extra, ((0, (-extra.shape[0]) % 16), (0, 0)))
    return jnp.concatenate([rows, extra], axis=0)


def unpack_rows(received, big_shape, small_shapes):
    big_rows = 1
    for d in big_shape:
        big_rows *= d
    big_rows //= 128
    big = received[:big_rows].reshape(big_shape)
    sizes = []
    for shape in small_shapes:
        size = 1
        for d in shape:
            size *= d
        sizes.append(size)
    padded = -(-sum(sizes) // 128) * 128
    extra = received[big_rows : big_rows + 3 * padded // 128].reshape(3, padded)
    vector = join_three(extra)
    smalls = []
    offset = 0
    for shape, size in zip(small_shapes, sizes):
        smalls.append(vector[offset : offset + size].reshape(shape))
        offset += size
    return big, smalls


def shifted(x, step):
    seq_count = lax.axis_size("seq")
    seq_rank = lax.axis_index("seq")
    if seq_count <= 8:
        moved = []
        for distance in range(1, seq_count):
            if step > 0:
                pairs = [(j, j + distance) for j in range(seq_count - distance)]
            else:
                pairs = [(j + distance, j) for j in range(seq_count - distance)]
            moved.append(lax.ppermute(x, "seq", pairs))
        return moved
    gathered = lax.all_gather(x, "seq", axis=0)
    moved = []
    for distance in range(1, seq_count):
        source = seq_rank + step * distance
        valid = (source >= 0) & (source < seq_count)
        picked = lax.dynamic_index_in_dim(gathered, jnp.clip(source, 0, seq_count - 1), 0, False)
        moved.append(jnp.where(valid, picked, jnp.zeros_like(picked)))
    return moved


def teacher_rows(queries, kv_list, seq_rank):
    local_heads, tok_dev, head_width = queries.shape
    local_groups = kv_list[0].shape[0]
    per_group = local_heads // local_groups
    grouped = queries.reshape(local_groups, per_group, tok_dev, head_width)
    rows = jnp.arange(tok_dev)
    within = rows[:, None] >= rows[None, :]
    block_scores = []
    for distance, block in enumerate(kv_list):
        scores = jnp.einsum(
            "gptd,gkd->gptk", grouped, block[..., :head_width], preferred_element_type=jnp.float32
        )
        scores = scores * head_width ** (-0.5)
        if distance == 0:
            allowed = within
        else:
            allowed = distance <= seq_rank
        block_scores.append(jnp.where(allowed, scores, -jnp.inf))
    highest_score = block_scores[0].max(axis=3, keepdims=True)
    for scores in block_scores[1:]:
        highest_score = jnp.maximum(highest_score, scores.max(axis=3, keepdims=True))
    row_sums = None
    mixed = None
    for scores, block in zip(block_scores, kv_list):
        exponentials = jnp.exp(scores - highest_score)
        part_sum = jnp.sum(exponentials, axis=3, keepdims=True)
        part = jnp.einsum(
            "gptk,gkd->gptd",
            exponentials.astype(jnp.bfloat16),
            block[..., head_width:],
            preferred_element_type=jnp.float32,
        )
        row_sums = part_sum if row_sums is None else row_sums + part_sum
        mixed = part if mixed is None else mixed + part
    mixed = mixed / row_sums
    return mixed.astype(jnp.bfloat16).reshape(local_heads, tok_dev, head_width)


def body(queries, keys_values, student_x, state_maps, decay_logit, skip_gain, init_state):
    local_heads, tok_dev, head_width = student_x.shape
    local_groups = state_maps.shape[0]
    per_group = local_heads // local_groups
    state_size = state_maps.shape[2] // 2
    seq_count = lax.axis_size("seq")
    seq_rank = lax.axis_index("seq")

    kv_earlier = shifted(keys_values, 1)

    log_decay = jax.nn.log_sigmoid(decay_logit)
    cumulative = jnp.cumsum(log_decay, axis=1)
    totals = cumulative[:, -1]
    to_end = jnp.exp(totals[:, None] - cumulative)
    from_start = jnp.exp(cumulative)
    in_maps = state_maps[:, :, :state_size]
    out_maps = state_maps[:, :, state_size:]
    inputs_wide = student_x.astype(jnp.float32)
    in_heads = jnp.repeat(in_maps.astype(jnp.float32), per_group, axis=0)
    out_heads = jnp.repeat(out_maps.astype(jnp.float32), per_group, axis=0)
    weighted_in = in_heads * to_end[..., None]
    end_state = jnp.einsum("hsn,hsp->hnp", weighted_in, inputs_wide, precision=highest)

    state_earlier = shifted(pack_rows(end_state, [totals]), 1)
    ends_earlier = []
    prefix_state = jnp.zeros_like(end_state)
    gap = jnp.zeros_like(totals)
    for distance, received in enumerate(state_earlier, start=1):
        ends, (totals_there,) = unpack_rows(received, end_state.shape, [totals.shape])
        valid = distance <= seq_rank
        totals_there = jnp.where(valid, totals_there, 0.0)
        weight = jnp.where(valid, jnp.exp(gap), 0.0)
        ends_earlier.append(ends)
        prefix_state = prefix_state + weight[:, None, None] * ends.astype(jnp.float32)
        gap = gap + totals_there
    entering = prefix_state + jnp.exp(gap)[:, None, None] * init_state

    intersection = jnp.einsum("gtn,gsn->gts", out_maps, in_maps, preferred_element_type=jnp.float32)
    order_ids = jnp.arange(tok_dev)
    causal = (order_ids[:, None] >= order_ids[None, :])[None]
    gaps = cumulative[:, :, None] - cumulative[:, None, :]
    decayed = jnp.where(causal, jnp.exp(jnp.where(causal, gaps, 0.0)), 0.0)
    mixing = (
        decayed.reshape(local_groups, per_group, tok_dev, tok_dev) * intersection[:, None]
    ).reshape(local_heads, tok_dev, tok_dev)
    local_out = jnp.einsum("hts,hsp->htp", mixing, inputs_wide, precision=highest)

    teacher = teacher_rows(queries, [keys_values] + kv_earlier, seq_rank)
    teacher_wide = teacher.astype(jnp.float32)
    target = teacher_wide * lax.rsqrt(
        jnp.mean(teacher_wide * teacher_wide, axis=2, keepdims=True) + epsilon
    )

    state_out = local_out + from_start[..., None] * jnp.einsum(
        "htn,hnp->htp", out_heads, entering, precision=highest
    )
    outputs = state_out + skip_gain[:, None, None] * inputs_wide
    inverse = lax.rsqrt(jnp.mean(outputs * outputs, axis=2, keepdims=True) + epsilon)
    normed = outputs * inverse
    residual = normed - target
    grad_out = (residual - normed * jnp.mean(residual * normed, axis=2, keepdims=True)) * inverse
    forward_term = jnp.sum(grad_out * state_out, axis=2)
    flow = jnp.einsum(
        "htn,htp->hnp", out_heads * from_start[..., None], grad_out, precision=highest
    )
    closing = jnp.sum(flow * entering, axis=(1, 2))
    if ends_earlier:
        ends_dot_flow = jnp.stack(
            [jnp.sum(ends.astype(jnp.float32) * flow, axis=(1, 2)) for ends in ends_earlier]
        )
    else:
        ends_dot_flow = jnp.zeros((1,) + totals.shape, jnp.float32)

    flow_later = shifted(pack_rows(flow, [totals, closing, ends_dot_flow]), -1)

    local_dx = jnp.einsum("hts,htp->hsp", mixing, grad_out, precision=highest)

    cross = jnp.einsum("htp,hsp->hts", grad_out, inputs_wide, precision=highest)
    paired = decayed * cross
    local_din = lax.optimization_barrier(
        jnp.einsum("hts,htn->hsn", paired, out_heads, precision=highest)
    )
    grad_output_maps = jnp.einsum("hts,hsn->htn", paired, in_heads, precision=highest)
    grad_output_maps = grad_output_maps + from_start[..., None] * jnp.einsum(
        "hnp,htp->htn", entering, grad_out, precision=highest
    )

    incoming = jnp.zeros_like(flow)
    later_sum = jnp.zeros_like(totals)
    gap = jnp.zeros_like(totals)
    through = []
    dots_there = []
    for distance, received in enumerate(flow_later, start=1):
        flows, (totals_there, closing_there, dots) = unpack_rows(
            received, flow.shape, [totals.shape, closing.shape, ends_dot_flow.shape]
        )
        valid = seq_rank + distance < seq_count
        totals_there = jnp.where(valid, totals_there, 0.0)
        weight = jnp.where(valid, jnp.exp(gap), 0.0)
        incoming = incoming + weight[:, None, None] * flows.astype(jnp.float32)
        later_sum = later_sum + jnp.where(valid, closing_there, 0.0)
        for early in range(1, distance):
            pair_gap = gap - through[early - 1]
            later_sum = later_sum - jnp.where(
                valid, jnp.exp(jnp.where(valid, pair_gap, 0.0)) * dots[distance - early - 1], 0.0
            )
        gap = gap + totals_there
        through.append(gap)

    state_dx = local_dx + jnp.einsum("hsn,hnp->hsp", weighted_in, incoming, precision=highest)
    terms = forward_term - jnp.sum(inputs_wide * state_dx, axis=2)
    grad_log_decay = later_sum[:, None] + lax.cumsum(terms, axis=1, reverse=True)
    grad_input_maps = (
        local_din
        + jnp.einsum("hnp,hsp->hsn", incoming, inputs_wide, precision=highest) * to_end[..., None]
    )
    grad_maps = jnp.concatenate([grad_input_maps, grad_output_maps], axis=2)
    grad_maps = grad_maps.reshape(local_groups, per_group, tok_dev, 2 * state_size).sum(axis=1)
    grad_x = state_dx + skip_gain[:, None, None] * grad_out
    return (grad_x.astype(jnp.bfloat16), grad_maps.astype(jnp.bfloat16), grad_log_decay)


def solution(mesh):
    in_specs = (
        P(("head", "sub"), ("groups", "seq"), None),
        P(("head", "sub"), ("groups", "seq"), None),
        P(("head", "sub"), ("groups", "seq"), None),
        P(("head", "sub"), ("groups", "seq"), None),
        P(("head", "sub"), ("groups", "seq")),
        P(("head", "sub")),
        P(("groups", "head", "sub"), None, None),
    )
    out_specs = (
        P(("head", "sub"), ("groups", "seq"), None),
        P(("head", "sub"), ("groups", "seq"), None),
        P(("head", "sub"), ("groups", "seq")),
    )
    return jax.shard_map(body, mesh=mesh, in_specs=in_specs, out_specs=out_specs, check_vma=False)
```

```python
import jax
import jax.numpy as jnp
from jax import lax
from jax.experimental.layout import Layout, with_layout_constraint
from jax.sharding import PartitionSpec as P

epsilon = 1e-05
highest = lax.Precision.HIGHEST


def split_three(values):
    top = lax.reduce_precision(values, exponent_bits=8, mantissa_bits=7)
    rest = values - top
    middle = lax.reduce_precision(rest, exponent_bits=8, mantissa_bits=7)
    low = rest - middle
    return jnp.stack([top, middle, low]).astype(jnp.bfloat16)


def join_three(parts):
    wide = parts.astype(jnp.float32)
    return wide[..., 0, :] + wide[..., 1, :] + wide[..., 2, :]


def pack_rows(big, smalls):
    rows = big.astype(jnp.bfloat16).reshape(-1, 128)
    vector = jnp.concatenate([v.reshape(-1) for v in smalls])
    padded = -(-vector.shape[0] // 128) * 128
    vector = jnp.pad(vector, (0, padded - vector.shape[0]))
    extra = split_three(vector).reshape(3 * padded // 128, 128)
    extra = jnp.pad(extra, ((0, (-extra.shape[0]) % 16), (0, 0)))
    return jnp.concatenate([rows, extra], axis=0)


def unpack_rows(received, big_shape, small_shapes):
    big_rows = 1
    for d in big_shape:
        big_rows *= d
    big_rows //= 128
    big = received[:big_rows].reshape(big_shape)
    sizes = []
    for shape in small_shapes:
        size = 1
        for d in shape:
            size *= d
        sizes.append(size)
    padded = -(-sum(sizes) // 128) * 128
    extra = received[big_rows : big_rows + 3 * padded // 128].reshape(3, padded)
    vector = join_three(extra)
    smalls = []
    offset = 0
    for shape, size in zip(small_shapes, sizes):
        smalls.append(vector[offset : offset + size].reshape(shape))
        offset += size
    return big, smalls


def shifted(x, step):
    seq_count = lax.axis_size("seq")
    seq_rank = lax.axis_index("seq")
    if seq_count <= 8:
        moved = []
        for distance in range(1, seq_count):
            if step > 0:
                pairs = [(j, j + distance) for j in range(seq_count - distance)]
            else:
                pairs = [(j + distance, j) for j in range(seq_count - distance)]
            moved.append(lax.ppermute(x, "seq", pairs))
        return moved
    gathered = lax.all_gather(x, "seq", axis=0)
    moved = []
    for distance in range(1, seq_count):
        source = seq_rank + step * distance
        valid = (source >= 0) & (source < seq_count)
        picked = lax.dynamic_index_in_dim(gathered, jnp.clip(source, 0, seq_count - 1), 0, False)
        moved.append(jnp.where(valid, picked, jnp.zeros_like(picked)))
    return moved


def teacher_rows(queries, kv_list, seq_rank):
    local_heads, tok_dev, head_width = queries.shape
    local_groups = kv_list[0].shape[0]
    per_group = local_heads // local_groups
    grouped = queries.reshape(local_groups, per_group, tok_dev, head_width)
    rows = jnp.arange(tok_dev)
    within = rows[:, None] >= rows[None, :]
    block_scores = []
    for distance, block in enumerate(kv_list):
        scores = jnp.einsum(
            "gptd,gkd->gptk", grouped, block[..., :head_width], preferred_element_type=jnp.float32
        )
        scores = scores * head_width ** (-0.5)
        if distance == 0:
            allowed = within
        else:
            allowed = distance <= seq_rank
        block_scores.append(jnp.where(allowed, scores, -jnp.inf))
    highest_score = block_scores[0].max(axis=3, keepdims=True)
    for scores in block_scores[1:]:
        highest_score = jnp.maximum(highest_score, scores.max(axis=3, keepdims=True))
    row_sums = None
    mixed = None
    for scores, block in zip(block_scores, kv_list):
        exponentials = jnp.exp(scores - highest_score)
        part_sum = jnp.sum(exponentials, axis=3, keepdims=True)
        part = jnp.einsum(
            "gptk,gkd->gptd",
            exponentials.astype(jnp.bfloat16),
            block[..., head_width:],
            preferred_element_type=jnp.float32,
        )
        row_sums = part_sum if row_sums is None else row_sums + part_sum
        mixed = part if mixed is None else mixed + part
    mixed = mixed / row_sums
    return mixed.astype(jnp.bfloat16).reshape(local_heads, tok_dev, head_width)


def body(queries, keys_values, student_x, state_maps, decay_logit, skip_gain, init_state):
    local_heads, tok_dev, head_width = student_x.shape
    local_groups = state_maps.shape[0]
    per_group = local_heads // local_groups
    state_size = state_maps.shape[2] // 2
    seq_count = lax.axis_size("seq")
    seq_rank = lax.axis_index("seq")

    kv_earlier = shifted(keys_values, 1)

    log_decay = jax.nn.log_sigmoid(decay_logit)
    cumulative = jnp.cumsum(log_decay, axis=1)
    totals = cumulative[:, -1]
    to_end = jnp.exp(totals[:, None] - cumulative)
    from_start = jnp.exp(cumulative)
    in_maps = state_maps[:, :, :state_size]
    out_maps = state_maps[:, :, state_size:]
    inputs_wide = student_x.astype(jnp.float32)
    in_heads = jnp.repeat(in_maps.astype(jnp.float32), per_group, axis=0)
    out_heads = jnp.repeat(out_maps.astype(jnp.float32), per_group, axis=0)
    weighted_in = in_heads * to_end[..., None]
    end_state = jnp.einsum("hsn,hsp->hnp", weighted_in, inputs_wide, precision=highest)

    state_earlier = shifted(pack_rows(end_state, [totals]), 1)
    ends_earlier = []
    prefix_state = jnp.zeros_like(end_state)
    gap = jnp.zeros_like(totals)
    for distance, received in enumerate(state_earlier, start=1):
        ends, (totals_there,) = unpack_rows(received, end_state.shape, [totals.shape])
        valid = distance <= seq_rank
        totals_there = jnp.where(valid, totals_there, 0.0)
        weight = jnp.where(valid, jnp.exp(gap), 0.0)
        ends_earlier.append(ends)
        prefix_state = prefix_state + weight[:, None, None] * ends.astype(jnp.float32)
        gap = gap + totals_there
    entering = prefix_state + jnp.exp(gap)[:, None, None] * init_state

    intersection = jnp.einsum("gtn,gsn->gts", out_maps, in_maps, preferred_element_type=jnp.float32)
    order_ids = jnp.arange(tok_dev)
    causal = (order_ids[:, None] >= order_ids[None, :])[None]
    gaps = cumulative[:, :, None] - cumulative[:, None, :]
    decayed = jnp.where(causal, jnp.exp(jnp.where(causal, gaps, 0.0)), 0.0)
    mixing = (
        decayed.reshape(local_groups, per_group, tok_dev, tok_dev) * intersection[:, None]
    ).reshape(local_heads, tok_dev, tok_dev)
    local_out = jnp.einsum("hts,hsp->htp", mixing, inputs_wide, precision=highest)

    teacher = teacher_rows(queries, [keys_values] + kv_earlier, seq_rank)
    teacher_wide = teacher.astype(jnp.float32)
    target = teacher_wide * lax.rsqrt(
        jnp.mean(teacher_wide * teacher_wide, axis=2, keepdims=True) + epsilon
    )

    state_out = local_out + from_start[..., None] * jnp.einsum(
        "htn,hnp->htp", out_heads, entering, precision=highest
    )
    outputs = state_out + skip_gain[:, None, None] * inputs_wide
    inverse = lax.rsqrt(jnp.mean(outputs * outputs, axis=2, keepdims=True) + epsilon)
    normed = outputs * inverse
    residual = normed - target
    grad_out = (residual - normed * jnp.mean(residual * normed, axis=2, keepdims=True)) * inverse
    forward_term = jnp.sum(grad_out * state_out, axis=2)
    flow = jnp.einsum(
        "htn,htp->hnp", out_heads * from_start[..., None], grad_out, precision=highest
    )
    closing = jnp.sum(flow * entering, axis=(1, 2))
    if ends_earlier:
        ends_dot_flow = jnp.stack(
            [jnp.sum(ends.astype(jnp.float32) * flow, axis=(1, 2)) for ends in ends_earlier]
        )
    else:
        ends_dot_flow = jnp.zeros((1,) + totals.shape, jnp.float32)

    flow_later = shifted(pack_rows(flow, [totals, closing, ends_dot_flow]), -1)

    local_dx = jnp.einsum("hts,htp->hsp", mixing, grad_out, precision=highest)

    cross = jnp.einsum("htp,hsp->hts", grad_out, inputs_wide, precision=highest)
    paired = decayed * cross
    local_din = jnp.einsum("hts,htn->hsn", paired, out_heads, precision=highest)
    grad_output_maps = jnp.einsum("hts,hsn->htn", paired, in_heads, precision=highest)
    grad_output_maps = grad_output_maps + from_start[..., None] * jnp.einsum(
        "hnp,htp->htn", entering, grad_out, precision=highest
    )

    incoming = jnp.zeros_like(flow)
    later_sum = jnp.zeros_like(totals)
    gap = jnp.zeros_like(totals)
    through = []
    dots_there = []
    for distance, received in enumerate(flow_later, start=1):
        flows, (totals_there, closing_there, dots) = unpack_rows(
            received, flow.shape, [totals.shape, closing.shape, ends_dot_flow.shape]
        )
        valid = seq_rank + distance < seq_count
        totals_there = jnp.where(valid, totals_there, 0.0)
        weight = jnp.where(valid, jnp.exp(gap), 0.0)
        incoming = incoming + weight[:, None, None] * flows.astype(jnp.float32)
        later_sum = later_sum + jnp.where(valid, closing_there, 0.0)
        for early in range(1, distance):
            pair_gap = gap - through[early - 1]
            later_sum = later_sum - jnp.where(
                valid, jnp.exp(jnp.where(valid, pair_gap, 0.0)) * dots[distance - early - 1], 0.0
            )
        gap = gap + totals_there
        through.append(gap)

    state_dx = local_dx + jnp.einsum("hsn,hnp->hsp", weighted_in, incoming, precision=highest)
    terms = forward_term - jnp.sum(inputs_wide * state_dx, axis=2)
    grad_log_decay = later_sum[:, None] + lax.cumsum(terms, axis=1, reverse=True)
    grad_input_maps = (
        local_din
        + jnp.einsum("hnp,hsp->hsn", incoming, inputs_wide, precision=highest) * to_end[..., None]
    )
    grad_maps = jnp.concatenate([grad_input_maps, grad_output_maps], axis=2)
    grad_maps = grad_maps.reshape(local_groups, per_group, tok_dev, 2 * state_size).sum(axis=1)
    grad_x = state_dx + skip_gain[:, None, None] * grad_out
    grad_x = with_layout_constraint(grad_x.astype(jnp.bfloat16), Layout((0, 1, 2)))
    grad_maps = with_layout_constraint(grad_maps.astype(jnp.bfloat16), Layout((0, 1, 2)))
    return (grad_x, grad_maps, grad_log_decay)


def solution(mesh):
    in_specs = (
        P(("head", "sub"), ("groups", "seq"), None),
        P(("head", "sub"), ("groups", "seq"), None),
        P(("head", "sub"), ("groups", "seq"), None),
        P(("head", "sub"), ("groups", "seq"), None),
        P(("head", "sub"), ("groups", "seq")),
        P(("head", "sub")),
        P(("groups", "head", "sub"), None, None),
    )
    out_specs = (
        P(("head", "sub"), ("groups", "seq"), None),
        P(("head", "sub"), ("groups", "seq"), None),
        P(("head", "sub"), ("groups", "seq")),
    )
    return jax.shard_map(body, mesh=mesh, in_specs=in_specs, out_specs=out_specs, check_vma=False)
```

```python
import jax
import jax.numpy as jnp
from jax import lax
from jax.sharding import PartitionSpec as P

epsilon = 1e-05
highest = lax.Precision.HIGHEST


def split_three(values):
    top = lax.reduce_precision(values, exponent_bits=8, mantissa_bits=7)
    rest = values - top
    middle = lax.reduce_precision(rest, exponent_bits=8, mantissa_bits=7)
    low = rest - middle
    return jnp.stack([top, middle, low]).astype(jnp.bfloat16)


def join_three(parts):
    wide = parts.astype(jnp.float32)
    return wide[..., 0, :] + wide[..., 1, :] + wide[..., 2, :]


def pack_rows(big, smalls):
    rows = big.astype(jnp.bfloat16).reshape(-1, 128)
    vector = jnp.concatenate([v.reshape(-1) for v in smalls])
    padded = -(-vector.shape[0] // 128) * 128
    vector = jnp.pad(vector, (0, padded - vector.shape[0]))
    extra = split_three(vector).reshape(3 * padded // 128, 128)
    extra = jnp.pad(extra, ((0, (-extra.shape[0]) % 16), (0, 0)))
    return jnp.concatenate([rows, extra], axis=0)


def unpack_rows(received, big_shape, small_shapes):
    big_rows = 1
    for d in big_shape:
        big_rows *= d
    big_rows //= 128
    big = received[:big_rows].reshape(big_shape)
    sizes = []
    for shape in small_shapes:
        size = 1
        for d in shape:
            size *= d
        sizes.append(size)
    padded = -(-sum(sizes) // 128) * 128
    extra = received[big_rows : big_rows + 3 * padded // 128].reshape(3, padded)
    vector = join_three(extra)
    smalls = []
    offset = 0
    for shape, size in zip(small_shapes, sizes):
        smalls.append(vector[offset : offset + size].reshape(shape))
        offset += size
    return big, smalls


def shifted(x, step):
    seq_count = lax.axis_size("seq")
    seq_rank = lax.axis_index("seq")
    if seq_count <= 8:
        moved = []
        for distance in range(1, seq_count):
            if step > 0:
                pairs = [(j, j + distance) for j in range(seq_count - distance)]
            else:
                pairs = [(j + distance, j) for j in range(seq_count - distance)]
            moved.append(lax.ppermute(x, "seq", pairs))
        return moved
    gathered = lax.all_gather(x, "seq", axis=0)
    moved = []
    for distance in range(1, seq_count):
        source = seq_rank + step * distance
        valid = (source >= 0) & (source < seq_count)
        picked = lax.dynamic_index_in_dim(gathered, jnp.clip(source, 0, seq_count - 1), 0, False)
        moved.append(jnp.where(valid, picked, jnp.zeros_like(picked)))
    return moved


def teacher_rows(queries, kv_list, seq_rank):
    local_heads, tok_dev, head_width = queries.shape
    local_groups = kv_list[0][0].shape[0]
    per_group = local_heads // local_groups
    grouped = queries.reshape(local_groups, per_group, tok_dev, head_width)
    rows = jnp.arange(tok_dev)
    within = rows[:, None] >= rows[None, :]
    block_scores = []
    for distance, (keys, _) in enumerate(kv_list):
        scores = jnp.einsum("gptd,gkd->gptk", grouped, keys, preferred_element_type=jnp.float32)
        scores = scores * head_width ** (-0.5)
        if distance == 0:
            allowed = within
        else:
            allowed = distance <= seq_rank
        block_scores.append(jnp.where(allowed, scores, -jnp.inf))
    highest_score = block_scores[0].max(axis=3, keepdims=True)
    for scores in block_scores[1:]:
        highest_score = jnp.maximum(highest_score, scores.max(axis=3, keepdims=True))
    row_sums = None
    mixed = None
    for scores, (_, values) in zip(block_scores, kv_list):
        exponentials = jnp.exp(scores - highest_score)
        part_sum = jnp.sum(exponentials, axis=3, keepdims=True)
        part = jnp.einsum(
            "gptk,gkd->gptd",
            exponentials.astype(jnp.bfloat16),
            values,
            preferred_element_type=jnp.float32,
        )
        row_sums = part_sum if row_sums is None else row_sums + part_sum
        mixed = part if mixed is None else mixed + part
    mixed = mixed / row_sums
    return mixed.astype(jnp.bfloat16).reshape(local_heads, tok_dev, head_width)


def body(queries, keys_values, student_x, state_maps, decay_logit, skip_gain, init_state):
    local_heads, tok_dev, head_width = student_x.shape
    local_groups = state_maps.shape[0]
    per_group = local_heads // local_groups
    state_size = state_maps.shape[2] // 2
    seq_count = lax.axis_size("seq")
    seq_rank = lax.axis_index("seq")

    seq_small = seq_count <= 8
    if seq_small:
        kv_earlier = [
            lax.ppermute(keys_values, "seq", [(j, j + distance) for j in range(seq_count - distance)])
            for distance in range(1, seq_count - 1)
        ]
    else:
        kv_earlier = shifted(keys_values, 1)
    kv_earlier = [(block[..., :head_width], block[..., head_width:]) for block in kv_earlier]

    log_decay = jax.nn.log_sigmoid(decay_logit)
    cumulative = jnp.cumsum(log_decay, axis=1)
    totals = cumulative[:, -1]
    to_end = jnp.exp(totals[:, None] - cumulative)
    from_start = jnp.exp(cumulative)
    in_maps = state_maps[:, :, :state_size]
    out_maps = state_maps[:, :, state_size:]
    inputs_wide = student_x.astype(jnp.float32)
    in_heads = jnp.repeat(in_maps.astype(jnp.float32), per_group, axis=0)
    out_heads = jnp.repeat(out_maps.astype(jnp.float32), per_group, axis=0)
    weighted_in = in_heads * to_end[..., None]
    end_state = jnp.einsum("hsn,hsp->hnp", weighted_in, inputs_wide, precision=highest)

    state_payload = pack_rows(end_state, [totals])
    if seq_small and seq_count > 1:
        far = seq_count - 1
        state_earlier = [
            lax.ppermute(state_payload, "seq", [(j, j + distance) for j in range(seq_count - distance)])
            for distance in range(1, far)
        ]
        own_keys = keys_values[..., :head_width]
        own_values = keys_values[..., head_width:]
        key_rows = own_keys.size // 128
        merged = jnp.concatenate(
            [own_keys.reshape(-1, 128), own_values.reshape(-1, 128), state_payload], axis=0
        )
        merged = lax.ppermute(merged, "seq", [(0, far)])
        kv_earlier.append(
            (
                merged[:key_rows].reshape(own_keys.shape),
                merged[key_rows : 2 * key_rows].reshape(own_values.shape),
            )
        )
        state_earlier.append(merged[2 * key_rows :])
    else:
        state_earlier = shifted(state_payload, 1)
    ends_earlier = []
    prefix_state = jnp.zeros_like(end_state)
    gap = jnp.zeros_like(totals)
    for distance, received in enumerate(state_earlier, start=1):
        ends, (totals_there,) = unpack_rows(received, end_state.shape, [totals.shape])
        valid = distance <= seq_rank
        totals_there = jnp.where(valid, totals_there, 0.0)
        weight = jnp.where(valid, jnp.exp(gap), 0.0)
        ends_earlier.append(ends)
        prefix_state = prefix_state + weight[:, None, None] * ends.astype(jnp.float32)
        gap = gap + totals_there
    entering = prefix_state + jnp.exp(gap)[:, None, None] * init_state

    intersection = jnp.einsum("gtn,gsn->gts", out_maps, in_maps, preferred_element_type=jnp.float32)
    order_ids = jnp.arange(tok_dev)
    causal = (order_ids[:, None] >= order_ids[None, :])[None]
    gaps = cumulative[:, :, None] - cumulative[:, None, :]
    decayed = jnp.where(causal, jnp.exp(jnp.where(causal, gaps, 0.0)), 0.0)
    mixing = (
        decayed.reshape(local_groups, per_group, tok_dev, tok_dev) * intersection[:, None]
    ).reshape(local_heads, tok_dev, tok_dev)
    local_out = jnp.einsum("hts,hsp->htp", mixing, inputs_wide, precision=highest)

    teacher = teacher_rows(
        queries, [(keys_values[..., :head_width], keys_values[..., head_width:])] + kv_earlier, seq_rank
    )
    teacher_wide = teacher.astype(jnp.float32)
    target = teacher_wide * lax.rsqrt(
        jnp.mean(teacher_wide * teacher_wide, axis=2, keepdims=True) + epsilon
    )

    state_out = local_out + from_start[..., None] * jnp.einsum(
        "htn,hnp->htp", out_heads, entering, precision=highest
    )
    outputs = state_out + skip_gain[:, None, None] * inputs_wide
    inverse = lax.rsqrt(jnp.mean(outputs * outputs, axis=2, keepdims=True) + epsilon)
    normed = outputs * inverse
    residual = normed - target
    grad_out = (residual - normed * jnp.mean(residual * normed, axis=2, keepdims=True)) * inverse
    forward_term = jnp.sum(grad_out * state_out, axis=2)
    flow = jnp.einsum(
        "htn,htp->hnp", out_heads * from_start[..., None], grad_out, precision=highest
    )
    closing = jnp.sum(flow * entering, axis=(1, 2))
    if ends_earlier:
        ends_dot_flow = jnp.stack(
            [jnp.sum(ends.astype(jnp.float32) * flow, axis=(1, 2)) for ends in ends_earlier]
        )
    else:
        ends_dot_flow = jnp.zeros((1,) + totals.shape, jnp.float32)

    flow_later = shifted(pack_rows(flow, [totals, closing, ends_dot_flow]), -1)

    local_dx = jnp.einsum("hts,htp->hsp", mixing, grad_out, precision=highest)

    cross = jnp.einsum("htp,hsp->hts", grad_out, inputs_wide, precision=highest)
    paired = decayed * cross
    local_din = jnp.einsum("hts,htn->hsn", paired, out_heads, precision=highest)
    grad_output_maps = jnp.einsum("hts,hsn->htn", paired, in_heads, precision=highest)
    grad_output_maps = grad_output_maps + from_start[..., None] * jnp.einsum(
        "hnp,htp->htn", entering, grad_out, precision=highest
    )

    incoming = jnp.zeros_like(flow)
    later_sum = jnp.zeros_like(totals)
    gap = jnp.zeros_like(totals)
    through = []
    dots_there = []
    for distance, received in enumerate(flow_later, start=1):
        flows, (totals_there, closing_there, dots) = unpack_rows(
            received, flow.shape, [totals.shape, closing.shape, ends_dot_flow.shape]
        )
        valid = seq_rank + distance < seq_count
        totals_there = jnp.where(valid, totals_there, 0.0)
        weight = jnp.where(valid, jnp.exp(gap), 0.0)
        incoming = incoming + weight[:, None, None] * flows.astype(jnp.float32)
        later_sum = later_sum + jnp.where(valid, closing_there, 0.0)
        for early in range(1, distance):
            pair_gap = gap - through[early - 1]
            later_sum = later_sum - jnp.where(
                valid, jnp.exp(jnp.where(valid, pair_gap, 0.0)) * dots[distance - early - 1], 0.0
            )
        gap = gap + totals_there
        through.append(gap)

    state_dx = local_dx + jnp.einsum("hsn,hnp->hsp", weighted_in, incoming, precision=highest)
    terms = forward_term - jnp.sum(inputs_wide * state_dx, axis=2)
    grad_log_decay = later_sum[:, None] + lax.cumsum(terms, axis=1, reverse=True)
    grad_input_maps = (
        local_din
        + jnp.einsum("hnp,hsp->hsn", incoming, inputs_wide, precision=highest) * to_end[..., None]
    )
    grad_maps = jnp.concatenate([grad_input_maps, grad_output_maps], axis=2)
    grad_maps = grad_maps.reshape(local_groups, per_group, tok_dev, 2 * state_size).sum(axis=1)
    grad_x = state_dx + skip_gain[:, None, None] * grad_out
    return (grad_x.astype(jnp.bfloat16), grad_maps.astype(jnp.bfloat16), grad_log_decay)


def solution(mesh):
    in_specs = (
        P(("head", "sub"), ("groups", "seq"), None),
        P(("head", "sub"), ("groups", "seq"), None),
        P(("head", "sub"), ("groups", "seq"), None),
        P(("head", "sub"), ("groups", "seq"), None),
        P(("head", "sub"), ("groups", "seq")),
        P(("head", "sub")),
        P(("groups", "head", "sub"), None, None),
    )
    out_specs = (
        P(("head", "sub"), ("groups", "seq"), None),
        P(("head", "sub"), ("groups", "seq"), None),
        P(("head", "sub"), ("groups", "seq")),
    )
    return jax.shard_map(body, mesh=mesh, in_specs=in_specs, out_specs=out_specs, check_vma=False)
```

```python
import jax
import jax.numpy as jnp
from jax import lax
from jax.sharding import PartitionSpec as P

epsilon = 1e-05
highest = lax.Precision.HIGHEST


def split_three(values):
    top = lax.reduce_precision(values, exponent_bits=8, mantissa_bits=7)
    rest = values - top
    middle = lax.reduce_precision(rest, exponent_bits=8, mantissa_bits=7)
    low = rest - middle
    return jnp.stack([top, middle, low]).astype(jnp.bfloat16)


def join_three(parts):
    wide = parts.astype(jnp.float32)
    return wide[..., 0, :] + wide[..., 1, :] + wide[..., 2, :]


def pack_rows(big, smalls):
    rows = big.astype(jnp.bfloat16).reshape(-1, 128)
    vector = jnp.concatenate([v.reshape(-1) for v in smalls])
    padded = -(-vector.shape[0] // 128) * 128
    vector = jnp.pad(vector, (0, padded - vector.shape[0]))
    extra = split_three(vector).reshape(3 * padded // 128, 128)
    extra = jnp.pad(extra, ((0, (-extra.shape[0]) % 16), (0, 0)))
    return jnp.concatenate([rows, extra], axis=0)


def unpack_rows(received, big_shape, small_shapes):
    big_rows = 1
    for d in big_shape:
        big_rows *= d
    big_rows //= 128
    big = received[:big_rows].reshape(big_shape)
    sizes = []
    for shape in small_shapes:
        size = 1
        for d in shape:
            size *= d
        sizes.append(size)
    padded = -(-sum(sizes) // 128) * 128
    extra = received[big_rows : big_rows + 3 * padded // 128].reshape(3, padded)
    vector = join_three(extra)
    smalls = []
    offset = 0
    for shape, size in zip(small_shapes, sizes):
        smalls.append(vector[offset : offset + size].reshape(shape))
        offset += size
    return big, smalls


def shifted(x, step):
    seq_count = lax.axis_size("seq")
    seq_rank = lax.axis_index("seq")
    if seq_count <= 8:
        moved = []
        for distance in range(1, seq_count):
            if step > 0:
                pairs = [(j, j + distance) for j in range(seq_count - distance)]
            else:
                pairs = [(j + distance, j) for j in range(seq_count - distance)]
            moved.append(lax.ppermute(x, "seq", pairs))
        return moved
    gathered = lax.all_gather(x, "seq", axis=0)
    moved = []
    for distance in range(1, seq_count):
        source = seq_rank - step * distance
        valid = (source >= 0) & (source < seq_count)
        picked = lax.dynamic_index_in_dim(gathered, jnp.clip(source, 0, seq_count - 1), 0, False)
        moved.append(jnp.where(valid, picked, jnp.zeros_like(picked)))
    return moved


def teacher_rows(queries, kv_list, seq_rank):
    local_heads, tok_dev, head_width = queries.shape
    local_groups = kv_list[0].shape[0]
    per_group = local_heads // local_groups
    grouped = queries.reshape(local_groups, per_group, tok_dev, head_width)
    rows = jnp.arange(tok_dev)
    within = rows[:, None] >= rows[None, :]
    block_scores = []
    for distance, block in enumerate(kv_list):
        scores = jnp.einsum(
            "gptd,gkd->gptk", grouped, block[..., :head_width], preferred_element_type=jnp.float32
        )
        scores = scores * head_width ** (-0.5)
        if distance == 0:
            allowed = within
        else:
            allowed = distance <= seq_rank
        block_scores.append(jnp.where(allowed, scores, -jnp.inf))
    highest_score = block_scores[0].max(axis=3, keepdims=True)
    for scores in block_scores[1:]:
        highest_score = jnp.maximum(highest_score, scores.max(axis=3, keepdims=True))
    row_sums = None
    mixed = None
    for scores, block in zip(block_scores, kv_list):
        exponentials = jnp.exp(scores - highest_score)
        part_sum = jnp.sum(exponentials, axis=3, keepdims=True)
        part = jnp.einsum(
            "gptk,gkd->gptd",
            exponentials.astype(jnp.bfloat16),
            block[..., head_width:],
            preferred_element_type=jnp.float32,
        )
        row_sums = part_sum if row_sums is None else row_sums + part_sum
        mixed = part if mixed is None else mixed + part
    mixed = mixed / row_sums
    return mixed.astype(jnp.bfloat16).reshape(local_heads, tok_dev, head_width)


def body(queries, keys_values, student_x, state_maps, decay_logit, skip_gain, init_state):
    local_heads, tok_dev, head_width = student_x.shape
    local_groups = state_maps.shape[0]
    per_group = local_heads // local_groups
    state_size = state_maps.shape[2] // 2
    seq_count = lax.axis_size("seq")
    seq_rank = lax.axis_index("seq")

    kv_earlier = shifted(keys_values, 1)

    log_decay = jax.nn.log_sigmoid(decay_logit)
    cumulative = jnp.cumsum(log_decay, axis=1)
    totals = cumulative[:, -1]
    to_end = jnp.exp(totals[:, None] - cumulative)
    from_start = jnp.exp(cumulative)
    in_maps = state_maps[:, :, :state_size]
    out_maps = state_maps[:, :, state_size:]
    inputs_wide = student_x.astype(jnp.float32)
    in_heads = jnp.repeat(in_maps.astype(jnp.float32), per_group, axis=0)
    out_heads = jnp.repeat(out_maps.astype(jnp.float32), per_group, axis=0)
    weighted_in = in_heads * to_end[..., None]
    end_state = jnp.einsum("hsn,hsp->hnp", weighted_in, inputs_wide, precision=highest)

    state_earlier = shifted(pack_rows(end_state, [totals]), 1)
    ends_earlier = []
    prefix_state = jnp.zeros_like(end_state)
    gap = jnp.zeros_like(totals)
    for distance, received in enumerate(state_earlier, start=1):
        ends, (totals_there,) = unpack_rows(received, end_state.shape, [totals.shape])
        valid = distance <= seq_rank
        totals_there = jnp.where(valid, totals_there, 0.0)
        weight = jnp.where(valid, jnp.exp(gap), 0.0)
        ends_earlier.append(ends)
        prefix_state = prefix_state + weight[:, None, None] * ends.astype(jnp.float32)
        gap = gap + totals_there
    entering = prefix_state + jnp.exp(gap)[:, None, None] * init_state

    intersection = jnp.einsum("gtn,gsn->gts", out_maps, in_maps, preferred_element_type=jnp.float32)
    order_ids = jnp.arange(tok_dev)
    causal = (order_ids[:, None] >= order_ids[None, :])[None]
    gaps = cumulative[:, :, None] - cumulative[:, None, :]
    decayed = jnp.where(causal, jnp.exp(jnp.where(causal, gaps, 0.0)), 0.0)
    mixing = (
        decayed.reshape(local_groups, per_group, tok_dev, tok_dev) * intersection[:, None]
    ).reshape(local_heads, tok_dev, tok_dev)
    local_out = jnp.einsum("hts,hsp->htp", mixing, inputs_wide, precision=highest)

    teacher = teacher_rows(queries, [keys_values] + kv_earlier, seq_rank)
    teacher_wide = teacher.astype(jnp.float32)
    target = teacher_wide * lax.rsqrt(
        jnp.mean(teacher_wide * teacher_wide, axis=2, keepdims=True) + epsilon
    )

    state_out = local_out + from_start[..., None] * jnp.einsum(
        "htn,hnp->htp", out_heads, entering, precision=highest
    )
    outputs = state_out + skip_gain[:, None, None] * inputs_wide
    inverse = lax.rsqrt(jnp.mean(outputs * outputs, axis=2, keepdims=True) + epsilon)
    normed = outputs * inverse
    residual = normed - target
    grad_out = (residual - normed * jnp.mean(residual * normed, axis=2, keepdims=True)) * inverse
    forward_term = jnp.sum(grad_out * state_out, axis=2)
    flow = jnp.einsum(
        "htn,htp->hnp", out_heads * from_start[..., None], grad_out, precision=highest
    )
    closing = jnp.sum(flow * entering, axis=(1, 2))
    if ends_earlier:
        ends_dot_flow = jnp.stack(
            [jnp.sum(ends.astype(jnp.float32) * flow, axis=(1, 2)) for ends in ends_earlier]
        )
    else:
        ends_dot_flow = jnp.zeros((1,) + totals.shape, jnp.float32)

    flow_later = shifted(pack_rows(flow, [totals, closing, ends_dot_flow]), -1)

    local_dx = jnp.einsum("hts,htp->hsp", mixing, grad_out, precision=highest)

    cross = jnp.einsum("htp,hsp->hts", grad_out, inputs_wide, precision=highest)
    paired = decayed * cross
    local_din = jnp.einsum("hts,htn->hsn", paired, out_heads, precision=highest)
    grad_output_maps = jnp.einsum("hts,hsn->htn", paired, in_heads, precision=highest)
    grad_output_maps = grad_output_maps + from_start[..., None] * jnp.einsum(
        "hnp,htp->htn", entering, grad_out, precision=highest
    )

    incoming = jnp.zeros_like(flow)
    later_sum = jnp.zeros_like(totals)
    gap = jnp.zeros_like(totals)
    through = []
    dots_there = []
    for distance, received in enumerate(flow_later, start=1):
        flows, (totals_there, closing_there, dots) = unpack_rows(
            received, flow.shape, [totals.shape, closing.shape, ends_dot_flow.shape]
        )
        valid = seq_rank + distance < seq_count
        totals_there = jnp.where(valid, totals_there, 0.0)
        weight = jnp.where(valid, jnp.exp(gap), 0.0)
        incoming = incoming + weight[:, None, None] * flows.astype(jnp.float32)
        later_sum = later_sum + jnp.where(valid, closing_there, 0.0)
        for early in range(1, distance):
            pair_gap = gap - through[early - 1]
            later_sum = later_sum - jnp.where(
                valid, jnp.exp(jnp.where(valid, pair_gap, 0.0)) * dots[distance - early - 1], 0.0
            )
        gap = gap + totals_there
        through.append(gap)

    state_dx = local_dx + jnp.einsum("hsn,hnp->hsp", weighted_in, incoming, precision=highest)
    terms = forward_term - jnp.sum(inputs_wide * state_dx, axis=2)
    grad_log_decay = later_sum[:, None] + lax.cumsum(terms, axis=1, reverse=True)
    grad_input_maps = (
        local_din
        + jnp.einsum("hnp,hsp->hsn", incoming, inputs_wide, precision=highest) * to_end[..., None]
    )
    grad_maps = jnp.concatenate([grad_input_maps, grad_output_maps], axis=2)
    grad_maps = grad_maps.reshape(local_groups, per_group, tok_dev, 2 * state_size).sum(axis=1)
    grad_x = state_dx + skip_gain[:, None, None] * grad_out
    return (grad_x.astype(jnp.bfloat16), grad_maps.astype(jnp.bfloat16), grad_log_decay)


def solution(mesh):
    in_specs = (
        P(("head", "sub"), ("groups", "seq"), None),
        P(("head", "sub"), ("groups", "seq"), None),
        P(("head", "sub"), ("groups", "seq"), None),
        P(("head", "sub"), ("groups", "seq"), None),
        P(("head", "sub"), ("groups", "seq")),
        P(("head", "sub")),
        P(("groups", "head", "sub"), None, None),
    )
    out_specs = (
        P(("head", "sub"), ("groups", "seq"), None),
        P(("head", "sub"), ("groups", "seq"), None),
        P(("head", "sub"), ("groups", "seq")),
    )
    return jax.shard_map(body, mesh=mesh, in_specs=in_specs, out_specs=out_specs, check_vma=False)
```

```python
import jax
import jax.numpy as jnp
from jax import lax
from jax.sharding import PartitionSpec as P

epsilon = 1e-05
highest = lax.Precision.HIGHEST


def split_three(values):
    top = lax.reduce_precision(values, exponent_bits=8, mantissa_bits=7)
    rest = values - top
    middle = lax.reduce_precision(rest, exponent_bits=8, mantissa_bits=7)
    low = rest - middle
    return jnp.stack([top, middle, low]).astype(jnp.bfloat16)


def join_three(parts):
    wide = parts.astype(jnp.float32)
    return wide[..., 0, :] + wide[..., 1, :] + wide[..., 2, :]


def pack_rows(big, smalls):
    rows = big.astype(jnp.bfloat16).reshape(-1, 128)
    vector = jnp.concatenate([v.reshape(-1) for v in smalls])
    padded = -(-vector.shape[0] // 128) * 128
    vector = jnp.pad(vector, (0, padded - vector.shape[0]))
    extra = split_three(vector).reshape(3 * padded // 128, 128)
    extra = jnp.pad(extra, ((0, (-extra.shape[0]) % 16), (0, 0)))
    return jnp.concatenate([rows, extra], axis=0)


def unpack_rows(received, big_shape, small_shapes):
    big_rows = 1
    for d in big_shape:
        big_rows *= d
    big_rows //= 128
    big = received[:big_rows].reshape(big_shape)
    sizes = []
    for shape in small_shapes:
        size = 1
        for d in shape:
            size *= d
        sizes.append(size)
    padded = -(-sum(sizes) // 128) * 128
    extra = received[big_rows : big_rows + 3 * padded // 128].reshape(3, padded)
    vector = join_three(extra)
    smalls = []
    offset = 0
    for shape, size in zip(small_shapes, sizes):
        smalls.append(vector[offset : offset + size].reshape(shape))
        offset += size
    return big, smalls


def shifted(x, step):
    seq_count = lax.axis_size("seq")
    seq_rank = lax.axis_index("seq")
    if seq_count <= 8:
        moved = []
        for distance in range(1, seq_count):
            if step > 0:
                pairs = [(j, j + distance) for j in range(seq_count - distance)]
            else:
                pairs = [(j + distance, j) for j in range(seq_count - distance)]
            moved.append(lax.ppermute(x, "seq", pairs))
        return moved
    gathered = lax.all_gather(x, "seq", axis=0)
    moved = []
    for distance in range(1, seq_count):
        source = seq_rank - step * distance
        valid = (source >= 0) & (source < seq_count)
        picked = lax.dynamic_index_in_dim(gathered, jnp.clip(source, 0, seq_count - 1), 0, False)
        moved.append(jnp.where(valid, picked, jnp.zeros_like(picked)))
    return moved


def teacher_rows(queries, kv_list, seq_rank):
    local_heads, tok_dev, head_width = queries.shape
    local_groups = kv_list[0].shape[0]
    per_group = local_heads // local_groups
    grouped = queries.reshape(local_groups, per_group, tok_dev, head_width)
    rows = jnp.arange(tok_dev)
    within = rows[:, None] >= rows[None, :]
    block_scores = []
    for distance, block in enumerate(kv_list):
        scores = jnp.einsum(
            "gptd,gkd->gptk", grouped, block[..., :head_width], preferred_element_type=jnp.float32
        )
        scores = scores * head_width ** (-0.5)
        if distance == 0:
            allowed = within
        else:
            allowed = distance <= seq_rank
        block_scores.append(jnp.where(allowed, scores, -jnp.inf))
    highest_score = block_scores[0].max(axis=3, keepdims=True)
    for scores in block_scores[1:]:
        highest_score = jnp.maximum(highest_score, scores.max(axis=3, keepdims=True))
    row_sums = None
    mixed = None
    for scores, block in zip(block_scores, kv_list):
        exponentials = jnp.exp(scores - highest_score)
        part_sum = jnp.sum(exponentials, axis=3, keepdims=True)
        part = jnp.einsum(
            "gptk,gkd->gptd",
            exponentials.astype(jnp.bfloat16),
            block[..., head_width:],
            preferred_element_type=jnp.float32,
        )
        row_sums = part_sum if row_sums is None else row_sums + part_sum
        mixed = part if mixed is None else mixed + part
    mixed = mixed / row_sums
    return mixed.astype(jnp.bfloat16).reshape(local_heads, tok_dev, head_width)


def body(queries, keys_values, student_x, state_maps, decay_logit, skip_gain, init_state):
    local_heads, tok_dev, head_width = student_x.shape
    local_groups = state_maps.shape[0]
    per_group = local_heads // local_groups
    state_size = state_maps.shape[2] // 2
    seq_count = lax.axis_size("seq")
    seq_rank = lax.axis_index("seq")

    kv_earlier = shifted(keys_values, 1)

    log_decay = jax.nn.log_sigmoid(decay_logit)
    cumulative = jnp.cumsum(log_decay, axis=1)
    totals = cumulative[:, -1]
    to_end = jnp.exp(totals[:, None] - cumulative)
    from_start = jnp.exp(cumulative)
    in_maps = state_maps[:, :, :state_size]
    out_maps = state_maps[:, :, state_size:]
    inputs_wide = student_x.astype(jnp.float32)
    in_heads = jnp.repeat(in_maps.astype(jnp.float32), per_group, axis=0)
    out_heads = jnp.repeat(out_maps.astype(jnp.float32), per_group, axis=0)
    weighted_in = in_heads * to_end[..., None]
    end_state = jnp.einsum("hsn,hsp->hnp", weighted_in, inputs_wide, precision=highest)

    state_earlier = shifted(pack_rows(end_state, [totals]), 1)
    ends_earlier = []
    prefix_state = jnp.zeros_like(end_state)
    gap = jnp.zeros_like(totals)
    for distance, received in enumerate(state_earlier, start=1):
        ends, (totals_there,) = unpack_rows(received, end_state.shape, [totals.shape])
        valid = distance <= seq_rank
        totals_there = jnp.where(valid, totals_there, 0.0)
        weight = jnp.where(valid, jnp.exp(gap), 0.0)
        ends_earlier.append(ends)
        prefix_state = prefix_state + weight[:, None, None] * ends.astype(jnp.float32)
        gap = gap + totals_there
    entering = prefix_state + jnp.exp(gap)[:, None, None] * init_state

    intersection = jnp.einsum("gtn,gsn->gts", out_maps, in_maps, preferred_element_type=jnp.float32)
    order_ids = jnp.arange(tok_dev)
    causal = (order_ids[:, None] >= order_ids[None, :])[None]
    gaps = cumulative[:, :, None] - cumulative[:, None, :]
    decayed = jnp.where(causal, jnp.exp(jnp.where(causal, gaps, 0.0)), 0.0)
    mixing = (
        decayed.reshape(local_groups, per_group, tok_dev, tok_dev) * intersection[:, None]
    ).reshape(local_heads, tok_dev, tok_dev)
    local_out = jnp.einsum("hts,hsp->htp", mixing, inputs_wide, precision=highest)

    teacher = teacher_rows(queries, [keys_values] + kv_earlier, seq_rank)
    teacher_wide = teacher.astype(jnp.float32)
    target = teacher_wide * lax.rsqrt(
        jnp.mean(teacher_wide * teacher_wide, axis=2, keepdims=True) + epsilon
    )

    state_out = local_out + from_start[..., None] * jnp.einsum(
        "htn,hnp->htp", out_heads, entering, precision=highest
    )
    outputs = state_out + skip_gain[:, None, None] * inputs_wide
    inverse = lax.rsqrt(jnp.mean(outputs * outputs, axis=2, keepdims=True) + epsilon)
    normed = outputs * inverse
    residual = normed - target
    grad_out = (residual - normed * jnp.mean(residual * normed, axis=2, keepdims=True)) * inverse
    forward_term = jnp.sum(grad_out * state_out, axis=2)
    flow = jnp.einsum(
        "htn,htp->hnp", out_heads * from_start[..., None], grad_out, precision=highest
    )
    closing = jnp.sum(flow * entering, axis=(1, 2))
    if ends_earlier:
        ends_dot_flow = jnp.stack(
            [jnp.sum(ends.astype(jnp.float32) * flow, axis=(1, 2)) for ends in ends_earlier]
        )
    else:
        ends_dot_flow = jnp.zeros((1,) + totals.shape, jnp.float32)

    flow_later = shifted(pack_rows(flow, [totals, closing, ends_dot_flow]), -1)

    local_dx = jnp.einsum("hts,htp->hsp", mixing, grad_out, precision=highest)

    cross = jnp.einsum("htp,hsp->hts", grad_out, inputs_wide, precision=highest)
    paired = decayed * cross
    local_din = jnp.einsum("hts,htn->hsn", paired, out_heads, precision=highest)
    grad_output_maps = jnp.einsum("hts,hsn->htn", paired, in_heads, precision=highest)
    grad_output_maps = grad_output_maps + from_start[..., None] * jnp.einsum(
        "hnp,htp->htn", entering, grad_out, precision=highest
    )

    incoming = jnp.zeros_like(flow)
    later_sum = jnp.zeros_like(totals)
    gap = jnp.zeros_like(totals)
    through = []
    dots_there = []
    for distance, received in enumerate(flow_later, start=1):
        flows, (totals_there, closing_there, dots) = unpack_rows(
            received, flow.shape, [totals.shape, closing.shape, ends_dot_flow.shape]
        )
        valid = seq_rank + distance < seq_count
        totals_there = jnp.where(valid, totals_there, 0.0)
        weight = jnp.where(valid, jnp.exp(gap), 0.0)
        incoming = incoming + weight[:, None, None] * flows.astype(jnp.float32)
        later_sum = later_sum + jnp.where(valid, closing_there, 0.0)
        for early in range(1, distance):
            pair_gap = gap - through[early - 1]
            later_sum = later_sum - jnp.where(
                valid, jnp.exp(jnp.where(valid, pair_gap, 0.0)) * dots[distance - early - 1], 0.0
            )
        gap = gap + totals_there
        through.append(gap)

    state_dx = local_dx + jnp.einsum("hsn,hnp->hsp", weighted_in, incoming, precision=highest)
    terms = forward_term - jnp.sum(inputs_wide * state_dx, axis=2)
    upper = (order_ids[:, None] <= order_ids[None, :]).astype(jnp.float32)
    grad_log_decay = later_sum[:, None] + jnp.einsum("hu,su->hs", terms, upper, precision=highest)
    grad_input_maps = (
        local_din
        + jnp.einsum("hnp,hsp->hsn", incoming, inputs_wide, precision=highest) * to_end[..., None]
    )
    grad_maps = jnp.concatenate([grad_input_maps, grad_output_maps], axis=2)
    grad_maps = grad_maps.reshape(local_groups, per_group, tok_dev, 2 * state_size).sum(axis=1)
    grad_x = state_dx + skip_gain[:, None, None] * grad_out
    return (grad_x.astype(jnp.bfloat16), grad_maps.astype(jnp.bfloat16), grad_log_decay)


def solution(mesh):
    in_specs = (
        P(("head", "sub"), ("groups", "seq"), None),
        P(("head", "sub"), ("groups", "seq"), None),
        P(("head", "sub"), ("groups", "seq"), None),
        P(("head", "sub"), ("groups", "seq"), None),
        P(("head", "sub"), ("groups", "seq")),
        P(("head", "sub")),
        P(("groups", "head", "sub"), None, None),
    )
    out_specs = (
        P(("head", "sub"), ("groups", "seq"), None),
        P(("head", "sub"), ("groups", "seq"), None),
        P(("head", "sub"), ("groups", "seq")),
    )
    return jax.shard_map(body, mesh=mesh, in_specs=in_specs, out_specs=out_specs, check_vma=False)
```

```python
import jax
import jax.numpy as jnp
from jax import lax
from jax.sharding import PartitionSpec as P

epsilon = 1e-05
highest = lax.Precision.HIGHEST


def split_three(values):
    top = lax.reduce_precision(values, exponent_bits=8, mantissa_bits=7)
    rest = values - top
    middle = lax.reduce_precision(rest, exponent_bits=8, mantissa_bits=7)
    low = rest - middle
    return jnp.stack([top, middle, low]).astype(jnp.bfloat16)


def join_three(parts):
    wide = parts.astype(jnp.float32)
    return wide[..., 0, :] + wide[..., 1, :] + wide[..., 2, :]


def pack_rows(big, smalls):
    rows = big.astype(jnp.bfloat16).reshape(-1, 128)
    vector = jnp.concatenate([v.reshape(-1) for v in smalls])
    padded = -(-vector.shape[0] // 128) * 128
    vector = jnp.pad(vector, (0, padded - vector.shape[0]))
    extra = split_three(vector).reshape(3 * padded // 128, 128)
    extra = jnp.pad(extra, ((0, (-extra.shape[0]) % 16), (0, 0)))
    return jnp.concatenate([rows, extra], axis=0)


def unpack_rows(received, big_shape, small_shapes):
    big_rows = 1
    for d in big_shape:
        big_rows *= d
    big_rows //= 128
    big = received[:big_rows].reshape(big_shape)
    sizes = []
    for shape in small_shapes:
        size = 1
        for d in shape:
            size *= d
        sizes.append(size)
    padded = -(-sum(sizes) // 128) * 128
    extra = received[big_rows : big_rows + 3 * padded // 128].reshape(3, padded)
    vector = join_three(extra)
    smalls = []
    offset = 0
    for shape, size in zip(small_shapes, sizes):
        smalls.append(vector[offset : offset + size].reshape(shape))
        offset += size
    return big, smalls


def shifted(x, step):
    seq_count = lax.axis_size("seq")
    seq_rank = lax.axis_index("seq")
    if seq_count <= 8:
        moved = []
        for distance in range(1, seq_count):
            if step > 0:
                pairs = [(j, j + distance) for j in range(seq_count - distance)]
            else:
                pairs = [(j + distance, j) for j in range(seq_count - distance)]
            moved.append(lax.ppermute(x, "seq", pairs))
        return moved
    gathered = lax.all_gather(x, "seq", axis=0)
    moved = []
    for distance in range(1, seq_count):
        source = seq_rank - step * distance
        valid = (source >= 0) & (source < seq_count)
        picked = lax.dynamic_index_in_dim(gathered, jnp.clip(source, 0, seq_count - 1), 0, False)
        moved.append(jnp.where(valid, picked, jnp.zeros_like(picked)))
    return moved


def teacher_rows(queries, kv_list, seq_rank):
    local_heads, tok_dev, head_width = queries.shape
    local_groups = kv_list[0].shape[0]
    per_group = local_heads // local_groups
    grouped = queries.reshape(local_groups, per_group, tok_dev, head_width)
    rows = jnp.arange(tok_dev)
    within = rows[:, None] >= rows[None, :]
    block_scores = []
    for distance, block in enumerate(kv_list):
        scores = jnp.einsum(
            "gptd,gkd->gptk", grouped, block[..., :head_width], preferred_element_type=jnp.float32
        )
        scores = scores * head_width ** (-0.5)
        if distance == 0:
            allowed = within
        else:
            allowed = distance <= seq_rank
        block_scores.append(jnp.where(allowed, scores, -jnp.inf))
    highest_score = block_scores[0].max(axis=3, keepdims=True)
    for scores in block_scores[1:]:
        highest_score = jnp.maximum(highest_score, scores.max(axis=3, keepdims=True))
    row_sums = None
    mixed = None
    for scores, block in zip(block_scores, kv_list):
        exponentials = jnp.exp(scores - highest_score)
        part_sum = jnp.sum(exponentials, axis=3, keepdims=True)
        part = jnp.einsum(
            "gptk,gkd->gptd",
            exponentials.astype(jnp.bfloat16),
            block[..., head_width:],
            preferred_element_type=jnp.float32,
        )
        row_sums = part_sum if row_sums is None else row_sums + part_sum
        mixed = part if mixed is None else mixed + part
    mixed = mixed / row_sums
    return mixed.astype(jnp.bfloat16).reshape(local_heads, tok_dev, head_width)


def body(queries, keys_values, student_x, state_maps, decay_logit, skip_gain, init_state):
    local_heads, tok_dev, head_width = student_x.shape
    local_groups = state_maps.shape[0]
    per_group = local_heads // local_groups
    state_size = state_maps.shape[2] // 2
    seq_count = lax.axis_size("seq")
    seq_rank = lax.axis_index("seq")

    kv_earlier = shifted(keys_values, 1)

    log_decay = jax.nn.log_sigmoid(decay_logit)
    token_ids = jnp.arange(tok_dev)
    through = (token_ids[:, None] <= token_ids[None, :]).astype(jnp.float32)
    cumulative = jnp.einsum("hu,ut->ht", log_decay, through, precision=highest)
    totals = cumulative[:, -1]
    to_end = jnp.exp(totals[:, None] - cumulative)
    from_start = jnp.exp(cumulative)
    in_maps = state_maps[:, :, :state_size]
    out_maps = state_maps[:, :, state_size:]
    inputs_wide = student_x.astype(jnp.float32)
    in_heads = jnp.repeat(in_maps.astype(jnp.float32), per_group, axis=0)
    out_heads = jnp.repeat(out_maps.astype(jnp.float32), per_group, axis=0)
    weighted_in = in_heads * to_end[..., None]
    end_state = jnp.einsum("hsn,hsp->hnp", weighted_in, inputs_wide, precision=highest)

    state_earlier = shifted(pack_rows(end_state, [totals]), 1)
    ends_earlier = []
    prefix_state = jnp.zeros_like(end_state)
    gap = jnp.zeros_like(totals)
    for distance, received in enumerate(state_earlier, start=1):
        ends, (totals_there,) = unpack_rows(received, end_state.shape, [totals.shape])
        valid = distance <= seq_rank
        totals_there = jnp.where(valid, totals_there, 0.0)
        weight = jnp.where(valid, jnp.exp(gap), 0.0)
        ends_earlier.append(ends)
        prefix_state = prefix_state + weight[:, None, None] * ends.astype(jnp.float32)
        gap = gap + totals_there
    entering = prefix_state + jnp.exp(gap)[:, None, None] * init_state

    intersection = jnp.einsum("gtn,gsn->gts", out_maps, in_maps, preferred_element_type=jnp.float32)
    order_ids = jnp.arange(tok_dev)
    causal = (order_ids[:, None] >= order_ids[None, :])[None]
    gaps = cumulative[:, :, None] - cumulative[:, None, :]
    decayed = jnp.where(causal, jnp.exp(jnp.where(causal, gaps, 0.0)), 0.0)
    mixing = (
        decayed.reshape(local_groups, per_group, tok_dev, tok_dev) * intersection[:, None]
    ).reshape(local_heads, tok_dev, tok_dev)
    local_out = jnp.einsum("hts,hsp->htp", mixing, inputs_wide, precision=highest)

    teacher = teacher_rows(queries, [keys_values] + kv_earlier, seq_rank)
    teacher_wide = teacher.astype(jnp.float32)
    target = teacher_wide * lax.rsqrt(
        jnp.mean(teacher_wide * teacher_wide, axis=2, keepdims=True) + epsilon
    )

    state_out = local_out + from_start[..., None] * jnp.einsum(
        "htn,hnp->htp", out_heads, entering, precision=highest
    )
    outputs = state_out + skip_gain[:, None, None] * inputs_wide
    inverse = lax.rsqrt(jnp.mean(outputs * outputs, axis=2, keepdims=True) + epsilon)
    normed = outputs * inverse
    residual = normed - target
    grad_out = (residual - normed * jnp.mean(residual * normed, axis=2, keepdims=True)) * inverse
    forward_term = jnp.sum(grad_out * state_out, axis=2)
    flow = jnp.einsum(
        "htn,htp->hnp", out_heads * from_start[..., None], grad_out, precision=highest
    )
    closing = jnp.sum(flow * entering, axis=(1, 2))
    if ends_earlier:
        ends_dot_flow = jnp.stack(
            [jnp.sum(ends.astype(jnp.float32) * flow, axis=(1, 2)) for ends in ends_earlier]
        )
    else:
        ends_dot_flow = jnp.zeros((1,) + totals.shape, jnp.float32)

    flow_later = shifted(pack_rows(flow, [totals, closing, ends_dot_flow]), -1)

    local_dx = jnp.einsum("hts,htp->hsp", mixing, grad_out, precision=highest)

    cross = jnp.einsum("htp,hsp->hts", grad_out, inputs_wide, precision=highest)
    paired = decayed * cross
    local_din = jnp.einsum("hts,htn->hsn", paired, out_heads, precision=highest)
    grad_output_maps = jnp.einsum("hts,hsn->htn", paired, in_heads, precision=highest)
    grad_output_maps = grad_output_maps + from_start[..., None] * jnp.einsum(
        "hnp,htp->htn", entering, grad_out, precision=highest
    )

    incoming = jnp.zeros_like(flow)
    later_sum = jnp.zeros_like(totals)
    gap = jnp.zeros_like(totals)
    through = []
    dots_there = []
    for distance, received in enumerate(flow_later, start=1):
        flows, (totals_there, closing_there, dots) = unpack_rows(
            received, flow.shape, [totals.shape, closing.shape, ends_dot_flow.shape]
        )
        valid = seq_rank + distance < seq_count
        totals_there = jnp.where(valid, totals_there, 0.0)
        weight = jnp.where(valid, jnp.exp(gap), 0.0)
        incoming = incoming + weight[:, None, None] * flows.astype(jnp.float32)
        later_sum = later_sum + jnp.where(valid, closing_there, 0.0)
        for early in range(1, distance):
            pair_gap = gap - through[early - 1]
            later_sum = later_sum - jnp.where(
                valid, jnp.exp(jnp.where(valid, pair_gap, 0.0)) * dots[distance - early - 1], 0.0
            )
        gap = gap + totals_there
        through.append(gap)

    state_dx = local_dx + jnp.einsum("hsn,hnp->hsp", weighted_in, incoming, precision=highest)
    terms = forward_term - jnp.sum(inputs_wide * state_dx, axis=2)
    upper = (order_ids[:, None] <= order_ids[None, :]).astype(jnp.float32)
    grad_log_decay = later_sum[:, None] + jnp.einsum("hu,su->hs", terms, upper, precision=highest)
    grad_input_maps = (
        local_din
        + jnp.einsum("hnp,hsp->hsn", incoming, inputs_wide, precision=highest) * to_end[..., None]
    )
    grad_maps = jnp.concatenate([grad_input_maps, grad_output_maps], axis=2)
    grad_maps = grad_maps.reshape(local_groups, per_group, tok_dev, 2 * state_size).sum(axis=1)
    grad_x = state_dx + skip_gain[:, None, None] * grad_out
    return (grad_x.astype(jnp.bfloat16), grad_maps.astype(jnp.bfloat16), grad_log_decay)


def solution(mesh):
    in_specs = (
        P(("head", "sub"), ("groups", "seq"), None),
        P(("head", "sub"), ("groups", "seq"), None),
        P(("head", "sub"), ("groups", "seq"), None),
        P(("head", "sub"), ("groups", "seq"), None),
        P(("head", "sub"), ("groups", "seq")),
        P(("head", "sub")),
        P(("groups", "head", "sub"), None, None),
    )
    out_specs = (
        P(("head", "sub"), ("groups", "seq"), None),
        P(("head", "sub"), ("groups", "seq"), None),
        P(("head", "sub"), ("groups", "seq")),
    )
    return jax.shard_map(body, mesh=mesh, in_specs=in_specs, out_specs=out_specs, check_vma=False)
```

```python
import jax
import jax.numpy as jnp
from jax import lax
from jax.sharding import PartitionSpec as P

epsilon = 1e-05
highest = lax.Precision.HIGHEST


def split_three(values):
    top = lax.reduce_precision(values, exponent_bits=8, mantissa_bits=7)
    rest = values - top
    middle = lax.reduce_precision(rest, exponent_bits=8, mantissa_bits=7)
    low = rest - middle
    return jnp.stack([top, middle, low]).astype(jnp.bfloat16)


def join_three(parts):
    wide = parts.astype(jnp.float32)
    return wide[..., 0, :] + wide[..., 1, :] + wide[..., 2, :]


def pack_rows(big, smalls):
    rows = big.astype(jnp.bfloat16).reshape(-1, 128)
    vector = jnp.concatenate([v.reshape(-1) for v in smalls])
    padded = -(-vector.shape[0] // 128) * 128
    vector = jnp.pad(vector, (0, padded - vector.shape[0]))
    extra = split_three(vector).reshape(3 * padded // 128, 128)
    extra = jnp.pad(extra, ((0, (-extra.shape[0]) % 16), (0, 0)))
    return jnp.concatenate([rows, extra], axis=0)


def unpack_rows(received, big_shape, small_shapes):
    big_rows = 1
    for d in big_shape:
        big_rows *= d
    big_rows //= 128
    big = received[:big_rows].reshape(big_shape)
    sizes = []
    for shape in small_shapes:
        size = 1
        for d in shape:
            size *= d
        sizes.append(size)
    padded = -(-sum(sizes) // 128) * 128
    extra = received[big_rows : big_rows + 3 * padded // 128].reshape(3, padded)
    vector = join_three(extra)
    smalls = []
    offset = 0
    for shape, size in zip(small_shapes, sizes):
        smalls.append(vector[offset : offset + size].reshape(shape))
        offset += size
    return big, smalls


def shifted(x, step):
    seq_count = lax.axis_size("seq")
    seq_rank = lax.axis_index("seq")
    if seq_count <= 8:
        moved = []
        for distance in range(1, seq_count):
            if step > 0:
                pairs = [(j, j + distance) for j in range(seq_count - distance)]
            else:
                pairs = [(j + distance, j) for j in range(seq_count - distance)]
            moved.append(lax.ppermute(x, "seq", pairs))
        return moved
    gathered = lax.all_gather(x, "seq", axis=0)
    moved = []
    for distance in range(1, seq_count):
        source = seq_rank - step * distance
        valid = (source >= 0) & (source < seq_count)
        picked = lax.dynamic_index_in_dim(gathered, jnp.clip(source, 0, seq_count - 1), 0, False)
        moved.append(jnp.where(valid, picked, jnp.zeros_like(picked)))
    return moved


def teacher_rows(queries, kv_list, seq_rank):
    local_heads, tok_dev, head_width = queries.shape
    local_groups = kv_list[0].shape[0]
    per_group = local_heads // local_groups
    grouped = queries.reshape(local_groups, per_group, tok_dev, head_width)
    rows = jnp.arange(tok_dev)
    within = rows[:, None] >= rows[None, :]
    block_scores = []
    for distance, block in enumerate(kv_list):
        scores = jnp.einsum(
            "gptd,gkd->gptk", grouped, block[..., :head_width], preferred_element_type=jnp.float32
        )
        scores = scores * head_width ** (-0.5)
        if distance == 0:
            allowed = within
        else:
            allowed = distance <= seq_rank
        block_scores.append(jnp.where(allowed, scores, -jnp.inf))
    highest_score = block_scores[0].max(axis=3, keepdims=True)
    for scores in block_scores[1:]:
        highest_score = jnp.maximum(highest_score, scores.max(axis=3, keepdims=True))
    row_sums = None
    mixed = None
    for scores, block in zip(block_scores, kv_list):
        exponentials = jnp.exp(scores - highest_score)
        part_sum = jnp.sum(exponentials, axis=3, keepdims=True)
        part = jnp.einsum(
            "gptk,gkd->gptd",
            exponentials.astype(jnp.bfloat16),
            block[..., head_width:],
            preferred_element_type=jnp.float32,
        )
        row_sums = part_sum if row_sums is None else row_sums + part_sum
        mixed = part if mixed is None else mixed + part
    mixed = mixed / row_sums
    return mixed.astype(jnp.bfloat16).reshape(local_heads, tok_dev, head_width)


def body(queries, keys_values, student_x, state_maps, decay_logit, skip_gain, init_state):
    local_heads, tok_dev, head_width = student_x.shape
    local_groups = state_maps.shape[0]
    per_group = local_heads // local_groups
    state_size = state_maps.shape[2] // 2
    seq_count = lax.axis_size("seq")
    seq_rank = lax.axis_index("seq")

    kv_earlier = shifted(keys_values, 1)

    log_decay = jax.nn.log_sigmoid(decay_logit)
    cumulative = jnp.cumsum(log_decay, axis=1)
    totals = cumulative[:, -1]
    to_end = jnp.exp(totals[:, None] - cumulative)
    from_start = jnp.exp(cumulative)
    in_maps = state_maps[:, :, :state_size]
    out_maps = state_maps[:, :, state_size:]
    inputs_wide = student_x.astype(jnp.float32)
    in_heads = jnp.repeat(in_maps.astype(jnp.float32), per_group, axis=0)
    out_heads = jnp.repeat(out_maps.astype(jnp.float32), per_group, axis=0)
    weighted_in = in_heads * to_end[..., None]
    end_state = jnp.einsum("hsn,hsp->hnp", weighted_in, inputs_wide, precision=highest)

    state_earlier = shifted(pack_rows(end_state, [totals]), 1)
    ends_earlier = []
    prefix_state = jnp.zeros_like(end_state)
    gap = jnp.zeros_like(totals)
    for distance, received in enumerate(state_earlier, start=1):
        ends, (totals_there,) = unpack_rows(received, end_state.shape, [totals.shape])
        valid = distance <= seq_rank
        totals_there = jnp.where(valid, totals_there, 0.0)
        weight = jnp.where(valid, jnp.exp(gap), 0.0)
        ends_earlier.append(ends)
        prefix_state = prefix_state + weight[:, None, None] * ends.astype(jnp.float32)
        gap = gap + totals_there
    entering = prefix_state + jnp.exp(gap)[:, None, None] * init_state

    intersection = jnp.einsum("gtn,gsn->gts", out_maps, in_maps, preferred_element_type=jnp.float32)
    order_ids = jnp.arange(tok_dev)
    causal = (order_ids[:, None] >= order_ids[None, :])[None]
    gaps = cumulative[:, :, None] - cumulative[:, None, :]
    decayed = jnp.where(causal, jnp.exp(jnp.where(causal, gaps, 0.0)), 0.0)
    mixing = (
        decayed.reshape(local_groups, per_group, tok_dev, tok_dev) * intersection[:, None]
    ).reshape(local_heads, tok_dev, tok_dev)
    local_out = jnp.einsum("hts,hsp->htp", mixing, inputs_wide, precision=highest)

    teacher = teacher_rows(queries, [keys_values] + kv_earlier, seq_rank)
    teacher_wide = teacher.astype(jnp.float32)
    target = teacher_wide * lax.rsqrt(
        jnp.mean(teacher_wide * teacher_wide, axis=2, keepdims=True) + epsilon
    )

    state_out = local_out + from_start[..., None] * jnp.einsum(
        "htn,hnp->htp", out_heads, entering, precision=highest
    )
    outputs = state_out + skip_gain[:, None, None] * inputs_wide
    lane_mean = jnp.full((head_width, 1), 1.0 / head_width, jnp.float32)
    inverse = lax.rsqrt(
        jnp.einsum("htp,pk->htk", outputs * outputs, lane_mean, precision=highest) + epsilon
    )
    normed = outputs * inverse
    residual = normed - target
    projection = jnp.einsum("htp,pk->htk", residual * normed, lane_mean, precision=highest)
    grad_out = (residual - normed * projection) * inverse
    forward_term = jnp.sum(grad_out * state_out, axis=2)
    flow = jnp.einsum(
        "htn,htp->hnp", out_heads * from_start[..., None], grad_out, precision=highest
    )
    closing = jnp.sum(flow * entering, axis=(1, 2))
    if ends_earlier:
        ends_dot_flow = jnp.stack(
            [jnp.sum(ends.astype(jnp.float32) * flow, axis=(1, 2)) for ends in ends_earlier]
        )
    else:
        ends_dot_flow = jnp.zeros((1,) + totals.shape, jnp.float32)

    flow_later = shifted(pack_rows(flow, [totals, closing, ends_dot_flow]), -1)

    local_dx = jnp.einsum("hts,htp->hsp", mixing, grad_out, precision=highest)

    cross = jnp.einsum("htp,hsp->hts", grad_out, inputs_wide, precision=highest)
    paired = decayed * cross
    local_din = jnp.einsum("hts,htn->hsn", paired, out_heads, precision=highest)
    grad_output_maps = jnp.einsum("hts,hsn->htn", paired, in_heads, precision=highest)
    grad_output_maps = grad_output_maps + from_start[..., None] * jnp.einsum(
        "hnp,htp->htn", entering, grad_out, precision=highest
    )

    incoming = jnp.zeros_like(flow)
    later_sum = jnp.zeros_like(totals)
    gap = jnp.zeros_like(totals)
    through = []
    dots_there = []
    for distance, received in enumerate(flow_later, start=1):
        flows, (totals_there, closing_there, dots) = unpack_rows(
            received, flow.shape, [totals.shape, closing.shape, ends_dot_flow.shape]
        )
        valid = seq_rank + distance < seq_count
        totals_there = jnp.where(valid, totals_there, 0.0)
        weight = jnp.where(valid, jnp.exp(gap), 0.0)
        incoming = incoming + weight[:, None, None] * flows.astype(jnp.float32)
        later_sum = later_sum + jnp.where(valid, closing_there, 0.0)
        for early in range(1, distance):
            pair_gap = gap - through[early - 1]
            later_sum = later_sum - jnp.where(
                valid, jnp.exp(jnp.where(valid, pair_gap, 0.0)) * dots[distance - early - 1], 0.0
            )
        gap = gap + totals_there
        through.append(gap)

    state_dx = local_dx + jnp.einsum("hsn,hnp->hsp", weighted_in, incoming, precision=highest)
    terms = forward_term - jnp.sum(inputs_wide * state_dx, axis=2)
    upper = (order_ids[:, None] <= order_ids[None, :]).astype(jnp.float32)
    grad_log_decay = later_sum[:, None] + jnp.einsum("hu,su->hs", terms, upper, precision=highest)
    grad_input_maps = (
        local_din
        + jnp.einsum("hnp,hsp->hsn", incoming, inputs_wide, precision=highest) * to_end[..., None]
    )
    grad_maps = jnp.concatenate([grad_input_maps, grad_output_maps], axis=2)
    grad_maps = grad_maps.reshape(local_groups, per_group, tok_dev, 2 * state_size).sum(axis=1)
    grad_x = state_dx + skip_gain[:, None, None] * grad_out
    return (grad_x.astype(jnp.bfloat16), grad_maps.astype(jnp.bfloat16), grad_log_decay)


def solution(mesh):
    in_specs = (
        P(("head", "sub"), ("groups", "seq"), None),
        P(("head", "sub"), ("groups", "seq"), None),
        P(("head", "sub"), ("groups", "seq"), None),
        P(("head", "sub"), ("groups", "seq"), None),
        P(("head", "sub"), ("groups", "seq")),
        P(("head", "sub")),
        P(("groups", "head", "sub"), None, None),
    )
    out_specs = (
        P(("head", "sub"), ("groups", "seq"), None),
        P(("head", "sub"), ("groups", "seq"), None),
        P(("head", "sub"), ("groups", "seq")),
    )
    return jax.shard_map(body, mesh=mesh, in_specs=in_specs, out_specs=out_specs, check_vma=False)
```
